32 devices in a mesh: grp: 2 (over y), dp: 4 (over x, core), sub: 4 (over z).
Axes of the slice: x: 2, y: 2, z: 4, core: 2. Of those that a mesh axis runs over, the one named last changes fastest.
Arguments:
- hidden_in: bfloat16 [128, 5120], P(('grp', 'dp'), 'sub'), parts along dimension 0, may hold values from -76 to 76
- queries: bfloat16 [128, 128, 576], P(('grp', 'dp', 'sub')), parts along dimension 0, may hold values from -260 to 260
- cache_pool: bfloat16 [2048, 128, 576], P(('grp', 'dp', 'sub')), parts along dimension 0, may hold values from -6 to 6
- page_table: int32 [128, 16], P(('grp', 'dp', 'sub')), parts along dimension 0, may hold values from 0 to 63, as said below
- lengths: int32 [128], P(('grp', 'dp', 'sub')), parts along dimension 0, may hold values from 128 to 2048, as said below
- value_up: bfloat16 [128, 512, 128], P(('dp', 'sub')), may hold values from -0.25 to 0.25
- out_proj: bfloat16 [16384, 5120], P('dp', 'sub'), may hold values from -0.125 to 0.125
- norm_gain: bfloat16 [5120], P('sub'), may hold values from 0.099609375 to 1.8984375
- gate_proj: bfloat16 [5120, 12288], P('sub', 'dp'), may hold values from -0.078125 to 0.078125
- up_proj: bfloat16 [5120, 12288], P('sub', 'dp'), may hold values from -0.078125 to 0.078125
- down_proj: bfloat16 [12288, 5120], P('dp', 'sub'), may hold values from -0.21875 to 0.21875
Outputs:
- attn_out: bfloat16 [128, 5120], P(('grp', 'dp'), 'sub'), parts along dimension 0
- next_hidden: bfloat16 [128, 5120], P(('grp', 'dp'), 'sub'), parts along dimension 0
The draws below stay inside these ranges and needn't reach their ends.
There are 2 independent parts, one for each index of `grp`. The reference program is written for one: setup_inputs(seed, part) draws one part's arguments, and reference() takes and returns one part's arrays. A program takes and returns all parts, laid end to end along the dimension named above; an argument that names none is the same for every part. Nothing has to cross between parts.
Inputs may be any that keep to these rules, and one draw needn't show every extreme that they name: `page_table`: row r lists 16 pages of the pool of request r's device; the 4 rows of one device use each of its 64 pages exactly once. `lengths`: some request has exactly 2048 positions and some exactly 128.
All inputs are finite; a program needn't handle non-finite values.
Results may differ from the reference program's by a relative error of at most 0.02.
Values may be sent and summed in bfloat16 or wider, within the bound.
No kernel may reach another device: no remote copies, remote signals or barrier semaphores. Data moves between devices by JAX's collectives and lax.ppermute only.
A program may use at most 192 MiB of HBM per device.

```python
import math
import jax
import jax.numpy as jnp
from jax import lax

D = 5120
HEADS = 128
LATENT = 512
ROPE = 64
VDIM = 128
FF = 12288
PAGE = 128
PAGES_REQ = 16
R_DEV = 4
REQUESTS = 64
CTX = 2048


def page_helper(key):
    device_count = REQUESTS // R_DEV
    device_keys = jax.random.split(jax.random.fold_in(key, 11), device_count)

    def device_order(device_key):
        return jax.random.permutation(device_key, R_DEV * PAGES_REQ)
    orders = jax.vmap(device_order)(device_keys)
    return orders.reshape(REQUESTS, PAGES_REQ).astype(jnp.int32)


def rope_helper(key):
    first_rope = jax.random.normal(jax.random.fold_in(key, 23), (REQUESTS * PAGES_REQ, ROPE), jnp.float32)
    return jnp.clip(first_rope, -4.0, 4.0)


def draw_page_table(key, part):
    return page_helper(key)


def draw_lengths(key, part):
    key_a, key_b, key_c = jax.random.split(jax.random.fold_in(key, 13), 3)
    spans = jax.random.randint(key_a, (REQUESTS,), PAGE, CTX + 1)
    longest = jax.random.randint(key_b, (), 0, REQUESTS)
    shortest = (longest + jax.random.randint(key_c, (), 1, REQUESTS)) % REQUESTS
    spans = spans.at[longest].set(CTX).at[shortest].set(PAGE)
    return spans.astype(jnp.int32)


def draw_cache_pool(key, part):
    key_a = jax.random.fold_in(jax.random.fold_in(key, 17), 0)
    pool_shape = (REQUESTS * PAGES_REQ, PAGE, LATENT + ROPE)
    pool = jnp.clip(jax.random.normal(key_a, pool_shape, jnp.float32), -6.0, 6.0)
    rope_first = rope_helper(key)
    pool = pool.at[:, 0, LATENT:].set(rope_first)
    return pool.astype(jnp.bfloat16)


def draw_queries(key, part):
    key_a = jax.random.fold_in(jax.random.fold_in(key, 19), 0)
    query_shape = (REQUESTS, HEADS, LATENT + ROPE)
    query_rows = 1.3 * jnp.clip(jax.random.normal(key_a, query_shape, jnp.float32), -8.0, 8.0)
    return query_rows.astype(jnp.bfloat16)


def draw_hidden_in(key, part):
    key_a, key_b, key_c = jax.random.split(jax.random.fold_in(key, 29), 3)
    row_scale = jnp.exp(jax.random.uniform(key_b, (REQUESTS, 1), jnp.float32, math.log(0.3), math.log(3.0)))
    rough = jnp.exp(jax.random.uniform(key_c, (1, D), jnp.float32, math.log(0.5), math.log(2.0)))
    place = jnp.arange(D, dtype=jnp.float32)[None, :] / float(D)
    ramp = jnp.exp(place * math.log(math.sqrt(3.0)))
    base_rows = jnp.clip(jax.random.normal(key_a, (REQUESTS, D), jnp.float32), -6.0, 6.0)
    column_scale = 0.7 * ramp * rough
    values_out = jnp.clip(base_rows * row_scale * column_scale, -75.0, 75.0)
    return values_out.astype(jnp.bfloat16)


def shard_levels(stream_key, shape, cuts, smallest, top_value):
    factor_of, own = 1.0, jax.random.fold_in(stream_key, 6)
    for axis_at, shards_of in cuts:
        heights = jnp.exp(jax.random.uniform(jax.random.fold_in(own, axis_at), (shards_of,), jnp.float32, smallest / len(cuts), top_value / len(cuts)))
        factor_of = factor_of * jnp.repeat(heights, shape[axis_at] // shards_of).reshape([-1 if axis == axis_at else 1 for axis in range(len(shape))])
    return factor_of


def scatter_about(rng, extent, deviation, reach, cuts=(), kind=jnp.bfloat16):
    factor_of = shard_levels(rng, extent, cuts, -0.22, 0.18) if cuts else 1.0
    entries = jax.random.normal(rng, extent, jnp.float32) * deviation * factor_of
    return jnp.minimum(jnp.maximum(entries, -reach), reach).astype(kind)


def setup_inputs(seed: int = 0, part: int = 0) -> dict:
    key_list = jax.random.split(jax.random.key(seed), 12)
    part_splits = jax.random.split(jax.random.fold_in(key_list[11], part), 12)
    return {
        "hidden_in": draw_hidden_in(jax.random.fold_in(jax.random.fold_in(key_list[11], part), 71), part),
        "queries": draw_queries(jax.random.fold_in(jax.random.fold_in(key_list[11], part), 71), part),
        "cache_pool": draw_cache_pool(jax.random.fold_in(jax.random.fold_in(key_list[11], part), 71), part),
        "page_table": draw_page_table(jax.random.fold_in(jax.random.fold_in(key_list[11], part), 71), part),
        "lengths": draw_lengths(jax.random.fold_in(jax.random.fold_in(key_list[11], part), 71), part),
        "value_up": scatter_about(key_list[5], (HEADS, LATENT, VDIM), LATENT ** -0.5, 0.25, ((0, 16),)),
        "out_proj": scatter_about(key_list[6], (HEADS * VDIM, D), (HEADS * VDIM // 8) ** -0.5, 0.125, ((0, 4), (1, 4))),
        "norm_gain": jnp.clip(1.0 + 0.18 * jax.random.normal(key_list[7], (D,), jnp.float32), 0.099609375, 1.8984375).astype(jnp.bfloat16),
        "gate_proj": scatter_about(key_list[8], (D, FF), D ** -0.5, 0.078125, ((0, 4), (1, 4))),
        "up_proj": scatter_about(key_list[9], (D, FF), D ** -0.5, 0.078125, ((0, 4), (1, 4))),
        "down_proj": scatter_about(key_list[10], (FF, D), (FF // 16) ** -0.5, 0.21875, ((0, 4), (1, 4))),
    }


masked_score = -1e+30

def rms_norm(rows_in, norm_gain):
    spread = lax.optimization_barrier(jnp.mean(rows_in * rows_in, axis=1, keepdims=True))
    return (rows_in * lax.rsqrt(spread + 1e-06) * norm_gain.astype(jnp.float32)).astype(jnp.bfloat16)

def reference(hidden_in, queries, cache_pool, page_table, lengths, value_up, out_proj, norm_gain, gate_proj, up_proj, down_proj):
    score_scale = float(VDIM + ROPE) ** (-0.5)
    owner_base = jnp.arange(REQUESTS, dtype=jnp.int32) // R_DEV * (R_DEV * PAGES_REQ)
    page_index = (page_table + owner_base[:, None]).astype(jnp.int32)
    positions = jnp.arange(PAGES_REQ * PAGE, dtype=jnp.int32)

    def per_request(operands):
        query_rows, page_row, length = operands
        key_rows = cache_pool[page_row].reshape(PAGES_REQ * PAGE, LATENT + ROPE).astype(jnp.float32)
        scores = jnp.einsum('hc,tc->ht', query_rows.astype(jnp.float32), key_rows) * score_scale
        scores = jnp.where(positions[None, :] < length, scores, masked_score)
        row_max = lax.optimization_barrier(jnp.max(scores, axis=1, keepdims=True))
        exponent = jnp.where(positions[None, :] < length, jnp.exp(scores - row_max), 0.0)
        denominator = lax.optimization_barrier(jnp.sum(exponent, axis=1))
        weights_bf = exponent.astype(jnp.bfloat16)
        weighted = jnp.einsum('ht,tc->hc', weights_bf.astype(jnp.float32), key_rows[:, :LATENT])
        return (weighted / denominator[:, None]).astype(jnp.bfloat16)
    contexts = lax.map(per_request, (queries, page_index, lengths))
    values = jnp.einsum('rhc,hcv->rhv', contexts.astype(jnp.float32), value_up.astype(jnp.float32))
    values = values.astype(jnp.bfloat16).reshape(REQUESTS, HEADS * VDIM)
    attention = jnp.dot(values, out_proj, preferred_element_type=jnp.float32)
    residual = hidden_in.astype(jnp.float32) + attention
    normed = rms_norm(residual, norm_gain)
    gate_out = jnp.dot(normed, gate_proj, preferred_element_type=jnp.float32)
    up_out = jnp.dot(normed, up_proj, preferred_element_type=jnp.float32)
    hidden_units = (jax.nn.silu(gate_out) * up_out).astype(jnp.bfloat16)
    result = residual + jnp.dot(hidden_units, down_proj, preferred_element_type=jnp.float32)
    return (attention.astype(jnp.bfloat16), result.astype(jnp.bfloat16))
```

```python
import functools

import jax
import jax.numpy as jnp
from jax import lax
from jax.experimental import pallas as pl
from jax.experimental.pallas import tpu as pltpu
from jax.sharding import PartitionSpec as P

D = 5120
ROPE = 64
VDIM = 128


masked_score = -1e30


def attend_kernel(page_table, lengths, queries, cache_pool, contexts, keys, scores, weighted, copy_sems,
                  *, latent, score_scale):
    req_dev, pages_req = page_table.shape
    page_size = cache_pool.shape[1]
    head_count = queries.shape[1]

    def page_copy(slot, page):
        return pltpu.make_async_copy(
            cache_pool.at[page_table[slot, page]],
            keys.at[slot * pages_req + page],
            copy_sems.at[slot * pages_req + page],
        )

    def pages_of(slot):
        return (lengths[slot] + page_size - 1) // page_size

    for slot in range(req_dev):
        def start(page, carry, slot=slot):
            page_copy(slot, page).start()
            return carry

        lax.fori_loop(0, pages_of(slot), start, 0)

    positions = lax.broadcasted_iota(jnp.int32, (head_count, page_size), 1)
    for slot in range(req_dev):
        length = lengths[slot]
        query_rows = queries[slot]

        def score_step(page, running_max, slot=slot, length=length, query_rows=query_rows):
            page_copy(slot, page).wait()
            key_rows = keys[slot * pages_req + page]
            block = lax.dot_general(
                query_rows, key_rows, (((1,), (1,)), ((), ())), preferred_element_type=jnp.float32
            ) * score_scale
            block = jnp.where(positions + page * page_size < length, block, masked_score)
            scores[page] = block
            return jnp.maximum(running_max, jnp.max(block, axis=1, keepdims=True))

        row_max = lax.fori_loop(
            0, pages_of(slot), score_step, jnp.full((head_count, 1), masked_score, jnp.float32)
        )
        weighted[...] = jnp.zeros_like(weighted)

        def weight_step(page, denominator, slot=slot, length=length, row_max=row_max):
            live = positions + page * page_size < length
            exponent = jnp.where(live, jnp.exp(scores[page] - row_max), 0.0)
            value_rows = keys[slot * pages_req + page, :, :latent]
            weighted[...] += jnp.dot(
                exponent.astype(jnp.bfloat16), value_rows, preferred_element_type=jnp.float32
            )
            return denominator + jnp.sum(exponent, axis=1, keepdims=True)

        denominator = lax.fori_loop(
            0, pages_of(slot), weight_step, jnp.zeros((head_count, 1), jnp.float32)
        )
        contexts[slot] = (weighted[...] / denominator).astype(contexts.dtype)


def attend_all(queries, page_table, lengths, cache_pool, latent, score_scale):
    req_dev, head_count, width = queries.shape
    pages_req = page_table.shape[1]
    page_size = cache_pool.shape[1]
    kernel = functools.partial(attend_kernel, latent=latent, score_scale=score_scale)
    return pl.pallas_call(
        kernel,
        out_shape=jax.ShapeDtypeStruct((req_dev, head_count, latent), jnp.bfloat16),
        in_specs=[
            pl.BlockSpec(memory_space=pltpu.SMEM),
            pl.BlockSpec(memory_space=pltpu.SMEM),
            pl.BlockSpec(memory_space=pltpu.VMEM),
            pl.BlockSpec(memory_space=pl.ANY),
        ],
        out_specs=pl.BlockSpec(memory_space=pltpu.VMEM),
        scratch_shapes=[
            pltpu.VMEM((req_dev * pages_req, page_size, width), jnp.bfloat16),
            pltpu.VMEM((pages_req, head_count, page_size), jnp.float32),
            pltpu.VMEM((head_count, latent), jnp.float32),
            pltpu.SemaphoreType.DMA((req_dev * pages_req,)),
        ],
        compiler_params=pltpu.CompilerParams(vmem_limit_bytes=48 * 1024 * 1024),
    )(page_table, lengths, queries, cache_pool)


def shards(
    hidden_in,
    queries,
    cache_pool,
    page_table,
    lengths,
    value_up,
    out_proj,
    norm_gain,
    gate_proj,
    up_proj,
    down_proj,
):
    req_dev = queries.shape[0]
    latent = value_up.shape[1]
    value_dim = value_up.shape[2]
    heads_here = value_up.shape[0]
    pages_req = page_table.shape[1]
    score_scale = float(VDIM + ROPE) ** (-0.5)
    units_here = gate_proj.shape[1]
    contexts = attend_all(queries, page_table, lengths, cache_pool, latent, score_scale)
    received = lax.all_to_all(
        contexts[None], ("dp", "sub"), split_axis=2, concat_axis=0, tiled=True
    )
    received = received.reshape(-1, heads_here, latent)
    row_count = received.shape[0]
    values = jnp.einsum("rhc,hcv->rhv", received, value_up, preferred_element_type=jnp.float32)
    values = values.astype(jnp.bfloat16).reshape(row_count, heads_here * value_dim)
    group_values = lax.all_gather(values, "sub", axis=1, tiled=True)
    attention = lax.psum_scatter(
        jnp.dot(group_values, out_proj, preferred_element_type=jnp.float32).astype(jnp.bfloat16),
        "dp",
        scatter_dimension=0,
        tiled=True,
    ).astype(jnp.float32)
    residual = hidden_in.astype(jnp.float32) + attention
    squares = lax.psum(jnp.sum(residual * residual, axis=1), "sub")
    scale_rows = lax.rsqrt(squares / float(D) + 1e-06)
    normed = (residual * scale_rows[:, None] * norm_gain.astype(jnp.float32)).astype(jnp.bfloat16)
    piece = lax.all_gather(normed, "dp", axis=0, tiled=True)
    gate_part = jnp.dot(piece, gate_proj, preferred_element_type=jnp.float32)
    up_part = jnp.dot(piece, up_proj, preferred_element_type=jnp.float32)
    partials = jnp.concatenate([gate_part, up_part], axis=1)
    summed = lax.psum(partials.astype(jnp.bfloat16), "sub").astype(jnp.float32)
    hidden_units = (jax.nn.silu(summed[:, :units_here]) * summed[:, units_here:]).astype(
        jnp.bfloat16
    )
    feed_forward = lax.psum_scatter(
        jnp.dot(hidden_units, down_proj, preferred_element_type=jnp.float32).astype(jnp.bfloat16),
        "dp",
        scatter_dimension=0,
        tiled=True,
    ).astype(jnp.float32)
    return (attention.astype(jnp.bfloat16), (residual + feed_forward).astype(jnp.bfloat16))


def solution(mesh):
    placed = (
        P(("grp", "dp"), "sub"),
        P(("grp", "dp", "sub"), None, None),
        P(("grp", "dp", "sub"), None, None),
        P(("grp", "dp", "sub"), None),
        P(("grp", "dp", "sub")),
        P(("dp", "sub"), None, None),
        P("dp", "sub"),
        P("sub"),
        P("sub", "dp"),
        P("sub", "dp"),
        P("dp", "sub"),
    )
    return jax.shard_map(
        shards,
        mesh=mesh,
        in_specs=placed,
        out_specs=(P(("grp", "dp"), "sub"), P(("grp", "dp"), "sub")),
        check_vma=False,
    )
```

```python
import functools

import jax
import jax.numpy as jnp
from jax import lax
from jax.experimental import pallas as pl
from jax.experimental.pallas import tpu as pltpu
from jax.sharding import PartitionSpec as P

D = 5120
ROPE = 64
VDIM = 128


masked_score = -1e30


def attend_kernel(page_table, lengths, queries, cache_pool, contexts, keys, scores, weighted, copy_sems,
                  *, latent, score_scale):
    req_dev, pages_req = page_table.shape
    page_size = cache_pool.shape[2]
    head_count = queries.shape[1]

    def page_copy(slot, page):
        return pltpu.make_async_copy(
            cache_pool.at[page_table[slot, page]],
            keys.at[slot * pages_req + page],
            copy_sems.at[slot * pages_req + page],
        )

    def pages_of(slot):
        return (lengths[slot] + page_size - 1) // page_size

    for slot in range(req_dev):
        def start(page, carry, slot=slot):
            page_copy(slot, page).start()
            return carry

        lax.fori_loop(0, pages_of(slot), start, 0)

    positions = lax.broadcasted_iota(jnp.int32, (head_count, page_size), 1)
    for slot in range(req_dev):
        length = lengths[slot]
        query_rows = queries[slot]

        def score_step(page, running_max, slot=slot, length=length, query_rows=query_rows):
            page_copy(slot, page).wait()
            key_columns = keys[slot * pages_req + page]
            block = jnp.dot(query_rows, key_columns, preferred_element_type=jnp.float32) * score_scale
            block = jnp.where(positions + page * page_size < length, block, masked_score)
            scores[page] = block
            return jnp.maximum(running_max, jnp.max(block, axis=1, keepdims=True))

        row_max = lax.fori_loop(
            0, pages_of(slot), score_step, jnp.full((head_count, 1), masked_score, jnp.float32)
        )
        weighted[...] = jnp.zeros_like(weighted)

        def weight_step(page, denominator, slot=slot, length=length, row_max=row_max):
            live = positions + page * page_size < length
            exponent = jnp.where(live, jnp.exp(scores[page] - row_max), 0.0)
            value_columns = keys[slot * pages_req + page, :latent, :]
            weighted[...] += lax.dot_general(
                exponent.astype(jnp.bfloat16),
                value_columns,
                (((1,), (1,)), ((), ())),
                preferred_element_type=jnp.float32,
            )
            return denominator + jnp.sum(exponent, axis=1, keepdims=True)

        denominator = lax.fori_loop(
            0, pages_of(slot), weight_step, jnp.zeros((head_count, 1), jnp.float32)
        )
        contexts[slot] = (weighted[...] / denominator).astype(contexts.dtype)


def attend_all(queries, page_table, lengths, cache_pool, latent, score_scale):
    req_dev, head_count, width = queries.shape
    pages_req = page_table.shape[1]
    page_size = cache_pool.shape[1]
    cache_columns = jnp.swapaxes(cache_pool, 1, 2)
    kernel = functools.partial(attend_kernel, latent=latent, score_scale=score_scale)
    return pl.pallas_call(
        kernel,
        out_shape=jax.ShapeDtypeStruct((req_dev, head_count, latent), jnp.bfloat16),
        in_specs=[
            pl.BlockSpec(memory_space=pltpu.SMEM),
            pl.BlockSpec(memory_space=pltpu.SMEM),
            pl.BlockSpec(memory_space=pltpu.VMEM),
            pl.BlockSpec(memory_space=pl.ANY),
        ],
        out_specs=pl.BlockSpec(memory_space=pltpu.VMEM),
        scratch_shapes=[
            pltpu.VMEM((req_dev * pages_req, width, page_size), jnp.bfloat16),
            pltpu.VMEM((pages_req, head_count, page_size), jnp.float32),
            pltpu.VMEM((head_count, latent), jnp.float32),
            pltpu.SemaphoreType.DMA((req_dev * pages_req,)),
        ],
        compiler_params=pltpu.CompilerParams(vmem_limit_bytes=48 * 1024 * 1024),
    )(page_table, lengths, queries, cache_columns)


def shards(
    hidden_in,
    queries,
    cache_pool,
    page_table,
    lengths,
    value_up,
    out_proj,
    norm_gain,
    gate_proj,
    up_proj,
    down_proj,
):
    req_dev = queries.shape[0]
    latent = value_up.shape[1]
    value_dim = value_up.shape[2]
    heads_here = value_up.shape[0]
    pages_req = page_table.shape[1]
    score_scale = float(VDIM + ROPE) ** (-0.5)
    units_here = gate_proj.shape[1]
    contexts = attend_all(queries, page_table, lengths, cache_pool, latent, score_scale)
    received = lax.all_to_all(
        contexts[None], ("dp", "sub"), split_axis=2, concat_axis=0, tiled=True
    )
    received = received.reshape(-1, heads_here, latent)
    row_count = received.shape[0]
    values = jnp.einsum("rhc,hcv->rhv", received, value_up, preferred_element_type=jnp.float32)
    values = values.astype(jnp.bfloat16).reshape(row_count, heads_here * value_dim)
    group_values = lax.all_gather(values, "sub", axis=1, tiled=True)
    attention = lax.psum_scatter(
        jnp.dot(group_values, out_proj, preferred_element_type=jnp.float32).astype(jnp.bfloat16),
        "dp",
        scatter_dimension=0,
        tiled=True,
    ).astype(jnp.float32)
    residual = hidden_in.astype(jnp.float32) + attention
    squares = lax.psum(jnp.sum(residual * residual, axis=1), "sub")
    scale_rows = lax.rsqrt(squares / float(D) + 1e-06)
    normed = (residual * scale_rows[:, None] * norm_gain.astype(jnp.float32)).astype(jnp.bfloat16)
    piece = lax.all_gather(normed, "dp", axis=0, tiled=True)
    gate_part = jnp.dot(piece, gate_proj, preferred_element_type=jnp.float32)
    up_part = jnp.dot(piece, up_proj, preferred_element_type=jnp.float32)
    partials = jnp.concatenate([gate_part, up_part], axis=1)
    summed = lax.psum(partials.astype(jnp.bfloat16), "sub").astype(jnp.float32)
    hidden_units = (jax.nn.silu(summed[:, :units_here]) * summed[:, units_here:]).astype(
        jnp.bfloat16
    )
    feed_forward = lax.psum_scatter(
        jnp.dot(hidden_units, down_proj, preferred_element_type=jnp.float32).astype(jnp.bfloat16),
        "dp",
        scatter_dimension=0,
        tiled=True,
    ).astype(jnp.float32)
    return (attention.astype(jnp.bfloat16), (residual + feed_forward).astype(jnp.bfloat16))


def solution(mesh):
    placed = (
        P(("grp", "dp"), "sub"),
        P(("grp", "dp", "sub"), None, None),
        P(("grp", "dp", "sub"), None, None),
        P(("grp", "dp", "sub"), None),
        P(("grp", "dp", "sub")),
        P(("dp", "sub"), None, None),
        P("dp", "sub"),
        P("sub"),
        P("sub", "dp"),
        P("sub", "dp"),
        P("dp", "sub"),
    )
    return jax.shard_map(
        shards,
        mesh=mesh,
        in_specs=placed,
        out_specs=(P(("grp", "dp"), "sub"), P(("grp", "dp"), "sub")),
        check_vma=False,
    )
```

```python
import functools

import jax
import jax.numpy as jnp
from jax import lax
from jax.experimental import pallas as pl
from jax.experimental.pallas import tpu as pltpu
from jax.sharding import PartitionSpec as P

D = 5120
ROPE = 64
VDIM = 128


masked_score = -1e30


def attend_kernel(page_table, lengths, queries, cache_pool, contexts, keys, scores, weighted, copy_sems,
                  *, latent, score_scale):
    req_dev, pages_req = page_table.shape
    page_size = cache_pool.shape[2]
    head_count = queries.shape[1]

    def page_copy(slot, page):
        return pltpu.make_async_copy(
            cache_pool.at[page_table[slot, page]],
            keys.at[slot * pages_req + page],
            copy_sems.at[slot * pages_req + page],
        )

    def pages_of(slot):
        return (lengths[slot] + page_size - 1) // page_size

    for slot in range(req_dev):
        def start(page, carry, slot=slot):
            page_copy(slot, page).start()
            return carry

        lax.fori_loop(0, pages_of(slot), start, 0)

    positions = lax.broadcasted_iota(jnp.int32, (head_count, page_size), 1)
    for slot in range(req_dev):
        length = lengths[slot]
        query_rows = queries[slot]

        def score_step(page, running_max, slot=slot, length=length, query_rows=query_rows):
            page_copy(slot, page).wait()
            key_columns = keys[slot * pages_req + page]
            block = jnp.dot(query_rows, key_columns, preferred_element_type=jnp.float32) * score_scale
            block = jnp.where(positions + page * page_size < length, block, masked_score)
            scores[page] = block
            return jnp.maximum(running_max, jnp.max(block, axis=1, keepdims=True))

        row_max = lax.fori_loop(
            0, pages_of(slot), score_step, jnp.full((head_count, 1), masked_score, jnp.float32)
        )
        weighted[...] = jnp.zeros_like(weighted)

        def weight_step(page, denominator, slot=slot, length=length, row_max=row_max):
            live = positions + page * page_size < length
            exponent = jnp.where(live, jnp.exp(scores[page] - row_max), 0.0)
            value_columns = keys[slot * pages_req + page, :latent, :]
            weighted[...] += lax.dot_general(
                exponent.astype(jnp.bfloat16),
                value_columns,
                (((1,), (1,)), ((), ())),
                preferred_element_type=jnp.float32,
            )
            return denominator + jnp.sum(exponent, axis=1, keepdims=True)

        denominator = lax.fori_loop(
            0, pages_of(slot), weight_step, jnp.zeros((head_count, 1), jnp.float32)
        )
        contexts[slot] = (weighted[...] / denominator).astype(contexts.dtype)


def attend_all(queries, page_table, lengths, cache_pool, latent, score_scale):
    req_dev, head_count, width = queries.shape
    pages_req = page_table.shape[1]
    page_size = cache_pool.shape[1]
    cache_columns = jnp.swapaxes(cache_pool, 1, 2)
    kernel = functools.partial(attend_kernel, latent=latent, score_scale=score_scale)
    return pl.pallas_call(
        kernel,
        out_shape=jax.ShapeDtypeStruct((req_dev, head_count, latent), jnp.bfloat16),
        in_specs=[
            pl.BlockSpec(memory_space=pltpu.SMEM),
            pl.BlockSpec(memory_space=pltpu.SMEM),
            pl.BlockSpec(memory_space=pltpu.VMEM),
            pl.BlockSpec(memory_space=pl.ANY),
        ],
        out_specs=pl.BlockSpec(memory_space=pltpu.VMEM),
        scratch_shapes=[
            pltpu.VMEM((req_dev * pages_req, width, page_size), jnp.bfloat16),
            pltpu.VMEM((pages_req, head_count, page_size), jnp.float32),
            pltpu.VMEM((head_count, latent), jnp.float32),
            pltpu.SemaphoreType.DMA((req_dev * pages_req,)),
        ],
        compiler_params=pltpu.CompilerParams(vmem_limit_bytes=48 * 1024 * 1024),
    )(page_table, lengths, queries, cache_columns)


def swap_with(x, axis, distance, size):
    return lax.ppermute(x, axis, [(i, i ^ distance) for i in range(size)])


def halving_scatter(x, axis, size, dim=0):
    index = lax.axis_index(axis)
    x = x.astype(jnp.float32)
    distance = size // 2
    while distance >= 1:
        half = x.shape[dim] // 2
        low = lax.slice_in_dim(x, 0, half, axis=dim)
        high = lax.slice_in_dim(x, half, 2 * half, axis=dim)
        upper = (index & distance) != 0
        keep = jnp.where(upper, high, low)
        send = jnp.where(upper, low, high)
        x = keep + swap_with(send.astype(jnp.bfloat16), axis, distance, size).astype(jnp.float32)
        distance //= 2
    return x


def shards(
    axis_sizes,
    hidden_in,
    queries,
    cache_pool,
    page_table,
    lengths,
    value_up,
    out_proj,
    norm_gain,
    gate_proj,
    up_proj,
    down_proj,
):
    req_dev = queries.shape[0]
    latent = value_up.shape[1]
    value_dim = value_up.shape[2]
    heads_here = value_up.shape[0]
    pages_req = page_table.shape[1]
    score_scale = float(VDIM + ROPE) ** (-0.5)
    units_here = gate_proj.shape[1]
    contexts = attend_all(queries, page_table, lengths, cache_pool, latent, score_scale)
    received = lax.all_to_all(
        contexts[None], ("dp", "sub"), split_axis=2, concat_axis=0, tiled=True
    )
    received = received.reshape(-1, heads_here, latent)
    row_count = received.shape[0]
    values = jnp.einsum("rhc,hcv->rhv", received, value_up, preferred_element_type=jnp.float32)
    values = values.astype(jnp.bfloat16).reshape(row_count, heads_here * value_dim)
    group_values = lax.all_gather(values, "sub", axis=1, tiled=True)
    attention = halving_scatter(
        jnp.dot(group_values, out_proj, preferred_element_type=jnp.float32), "dp", axis_sizes["dp"]
    )
    residual = hidden_in.astype(jnp.float32) + attention
    squares = lax.psum(jnp.sum(residual * residual, axis=1), "sub")
    scale_rows = lax.rsqrt(squares / float(D) + 1e-06)
    normed = (residual * scale_rows[:, None] * norm_gain.astype(jnp.float32)).astype(jnp.bfloat16)
    piece = lax.all_gather(normed, "dp", axis=0, tiled=True)
    gate_part = jnp.dot(piece, gate_proj, preferred_element_type=jnp.float32)
    up_part = jnp.dot(piece, up_proj, preferred_element_type=jnp.float32)
    partials = jnp.concatenate([gate_part, up_part], axis=1)
    summed = lax.psum(partials.astype(jnp.bfloat16), "sub").astype(jnp.float32)
    hidden_units = (jax.nn.silu(summed[:, :units_here]) * summed[:, units_here:]).astype(
        jnp.bfloat16
    )
    feed_forward = halving_scatter(
        jnp.dot(hidden_units, down_proj, preferred_element_type=jnp.float32), "dp", axis_sizes["dp"]
    )
    return (attention.astype(jnp.bfloat16), (residual + feed_forward).astype(jnp.bfloat16))


def solution(mesh):
    placed = (
        P(("grp", "dp"), "sub"),
        P(("grp", "dp", "sub"), None, None),
        P(("grp", "dp", "sub"), None, None),
        P(("grp", "dp", "sub"), None),
        P(("grp", "dp", "sub")),
        P(("dp", "sub"), None, None),
        P("dp", "sub"),
        P("sub"),
        P("sub", "dp"),
        P("sub", "dp"),
        P("dp", "sub"),
    )
    return jax.shard_map(
        functools.partial(shards, dict(mesh.shape)),
        mesh=mesh,
        in_specs=placed,
        out_specs=(P(("grp", "dp"), "sub"), P(("grp", "dp"), "sub")),
        check_vma=False,
    )
```

```python
import functools

import jax
import jax.numpy as jnp
from jax import lax
from jax.experimental import pallas as pl
from jax.experimental.pallas import tpu as pltpu
from jax.sharding import PartitionSpec as P

D = 5120
ROPE = 64
VDIM = 128


masked_score = -1e30


def attend_kernel(page_table, lengths, queries, cache_pool, contexts, keys, scores, weighted, copy_sems,
                  *, latent, score_scale):
    req_dev, pages_req = page_table.shape
    page_size = cache_pool.shape[2]
    head_count = queries.shape[1]

    def page_copy(slot, page):
        return pltpu.make_async_copy(
            cache_pool.at[page_table[slot, page]],
            keys.at[slot * pages_req + page],
            copy_sems.at[slot * pages_req + page],
        )

    def pages_of(slot):
        return (lengths[slot] + page_size - 1) // page_size

    for slot in range(req_dev):
        def start(page, carry, slot=slot):
            page_copy(slot, page).start()
            return carry

        lax.fori_loop(0, pages_of(slot), start, 0)

    positions = lax.broadcasted_iota(jnp.int32, (head_count, page_size), 1)
    for slot in range(req_dev):
        length = lengths[slot]
        query_rows = queries[slot]

        def score_step(page, running_max, slot=slot, length=length, query_rows=query_rows):
            page_copy(slot, page).wait()
            key_columns = keys[slot * pages_req + page]
            block = jnp.dot(query_rows, key_columns, preferred_element_type=jnp.float32) * score_scale
            block = jnp.where(positions + page * page_size < length, block, masked_score)
            scores[page] = block
            return jnp.maximum(running_max, jnp.max(block, axis=1, keepdims=True))

        row_max = lax.fori_loop(
            0, pages_of(slot), score_step, jnp.full((head_count, 1), masked_score, jnp.float32)
        )
        weighted[...] = jnp.zeros_like(weighted)

        def weight_step(page, denominator, slot=slot, length=length, row_max=row_max):
            live = positions + page * page_size < length
            exponent = jnp.where(live, jnp.exp(scores[page] - row_max), 0.0)
            value_columns = keys[slot * pages_req + page, :latent, :]
            weighted[...] += lax.dot_general(
                exponent.astype(jnp.bfloat16),
                value_columns,
                (((1,), (1,)), ((), ())),
                preferred_element_type=jnp.float32,
            )
            return denominator + jnp.sum(exponent, axis=1, keepdims=True)

        denominator = lax.fori_loop(
            0, pages_of(slot), weight_step, jnp.zeros((head_count, 1), jnp.float32)
        )
        contexts[slot] = (weighted[...] / denominator).astype(contexts.dtype)


def attend_all(queries, page_table, lengths, cache_pool, latent, score_scale):
    req_dev, head_count, width = queries.shape
    pages_req = page_table.shape[1]
    page_size = cache_pool.shape[1]
    cache_columns = jnp.swapaxes(cache_pool, 1, 2)
    kernel = functools.partial(attend_kernel, latent=latent, score_scale=score_scale)
    return pl.pallas_call(
        kernel,
        out_shape=jax.ShapeDtypeStruct((req_dev, head_count, latent), jnp.bfloat16),
        in_specs=[
            pl.BlockSpec(memory_space=pltpu.SMEM),
            pl.BlockSpec(memory_space=pltpu.SMEM),
            pl.BlockSpec(memory_space=pltpu.VMEM),
            pl.BlockSpec(memory_space=pl.ANY),
        ],
        out_specs=pl.BlockSpec(memory_space=pltpu.VMEM),
        scratch_shapes=[
            pltpu.VMEM((req_dev * pages_req, width, page_size), jnp.bfloat16),
            pltpu.VMEM((pages_req, head_count, page_size), jnp.float32),
            pltpu.VMEM((head_count, latent), jnp.float32),
            pltpu.SemaphoreType.DMA((req_dev * pages_req,)),
        ],
        compiler_params=pltpu.CompilerParams(vmem_limit_bytes=48 * 1024 * 1024),
    )(page_table, lengths, queries, cache_columns)


def swap_with(x, axis, distance, size):
    return lax.ppermute(x, axis, [(i, i ^ distance) for i in range(size)])


def halving_scatter(x, axis, size, dim=0):
    index = lax.axis_index(axis)
    x = x.astype(jnp.float32)
    distance = size // 2
    while distance >= 1:
        half = x.shape[dim] // 2
        low = lax.slice_in_dim(x, 0, half, axis=dim)
        high = lax.slice_in_dim(x, half, 2 * half, axis=dim)
        upper = (index & distance) != 0
        keep = jnp.where(upper, high, low)
        send = jnp.where(upper, low, high)
        x = keep + swap_with(send.astype(jnp.bfloat16), axis, distance, size).astype(jnp.float32)
        distance //= 2
    return x


def nearest_first_scatter(x, axis, size):
    index = lax.axis_index(axis)
    x = x.astype(jnp.float32)
    distance = 1
    while distance < size:
        pairs = x.reshape(x.shape[:1] + (x.shape[1] // 2, 2) + x.shape[2:])
        even = pairs[:, :, 0]
        odd = pairs[:, :, 1]
        upper = (index & distance) != 0
        keep = jnp.where(upper, odd, even)
        send = jnp.where(upper, even, odd)
        x = keep + swap_with(send.astype(jnp.bfloat16), axis, distance, size).astype(jnp.float32)
        distance *= 2
    return x[:, 0]


def doubling_gather(x, axis, size, dim):
    index = lax.axis_index(axis)
    distance = 1
    while distance < size:
        got = swap_with(x, axis, distance, size)
        upper = (index & distance) != 0
        x = jnp.where(
            upper, jnp.concatenate([got, x], axis=dim), jnp.concatenate([x, got], axis=dim)
        )
        distance *= 2
    return x


def shards(
    axis_sizes,
    hidden_in,
    queries,
    cache_pool,
    page_table,
    lengths,
    value_up,
    out_proj,
    norm_gain,
    gate_proj,
    up_proj,
    down_proj,
):
    req_dev = queries.shape[0]
    latent = value_up.shape[1]
    value_dim = value_up.shape[2]
    heads_here = value_up.shape[0]
    pages_req = page_table.shape[1]
    score_scale = float(VDIM + ROPE) ** (-0.5)
    units_here = gate_proj.shape[1]
    contexts = attend_all(queries, page_table, lengths, cache_pool, latent, score_scale)
    received = lax.all_to_all(
        contexts[None], ("dp", "sub"), split_axis=2, concat_axis=0, tiled=True
    )
    received = received.reshape(-1, heads_here, latent)
    row_count = received.shape[0]
    values = jnp.einsum("rhc,hcv->rhv", received, value_up, preferred_element_type=jnp.float32)
    values = values.astype(jnp.bfloat16).reshape(row_count, heads_here * value_dim)
    group_values = lax.all_gather(values, "sub", axis=1, tiled=True)
    attention = halving_scatter(
        jnp.dot(group_values, out_proj, preferred_element_type=jnp.float32), "dp", axis_sizes["dp"]
    )
    residual = hidden_in.astype(jnp.float32) + attention
    squares = lax.psum(jnp.sum(residual * residual, axis=1), "sub")
    scale_rows = lax.rsqrt(squares / float(D) + 1e-06)
    normed = (residual * scale_rows[:, None] * norm_gain.astype(jnp.float32)).astype(jnp.bfloat16)
    piece = lax.all_gather(normed, "dp", axis=0, tiled=True)
    gate_part = jnp.dot(piece, gate_proj, preferred_element_type=jnp.float32)
    up_part = jnp.dot(piece, up_proj, preferred_element_type=jnp.float32)
    sub_size = axis_sizes["sub"]
    row_count = piece.shape[0]
    unit_chunk = units_here // sub_size
    partials = jnp.stack(
        [
            gate_part.reshape(row_count, sub_size, unit_chunk),
            up_part.reshape(row_count, sub_size, unit_chunk),
        ],
        axis=2,
    )
    summed = nearest_first_scatter(partials, "sub", sub_size)
    hidden_chunk = (jax.nn.silu(summed[:, 0]) * summed[:, 1]).astype(jnp.bfloat16)
    hidden_units = doubling_gather(hidden_chunk, "sub", sub_size, 1)
    feed_forward = halving_scatter(
        jnp.dot(hidden_units, down_proj, preferred_element_type=jnp.float32), "dp", axis_sizes["dp"]
    )
    return (attention.astype(jnp.bfloat16), (residual + feed_forward).astype(jnp.bfloat16))


def solution(mesh):
    placed = (
        P(("grp", "dp"), "sub"),
        P(("grp", "dp", "sub"), None, None),
        P(("grp", "dp", "sub"), None, None),
        P(("grp", "dp", "sub"), None),
        P(("grp", "dp", "sub")),
        P(("dp", "sub"), None, None),
        P("dp", "sub"),
        P("sub"),
        P("sub", "dp"),
        P("sub", "dp"),
        P("dp", "sub"),
    )
    return jax.shard_map(
        functools.partial(shards, dict(mesh.shape)),
        mesh=mesh,
        in_specs=placed,
        out_specs=(P(("grp", "dp"), "sub"), P(("grp", "dp"), "sub")),
        check_vma=False,
    )
```

```python
import functools

import jax
import jax.numpy as jnp
from jax import lax
from jax.experimental import pallas as pl
from jax.experimental.pallas import tpu as pltpu
from jax.sharding import PartitionSpec as P

D = 5120
ROPE = 64
VDIM = 128


masked_score = -1e30


def attend_kernel(page_table, lengths, queries, cache_pool, contexts, keys, scores, weighted, copy_sems,
                  *, latent, score_scale):
    req_dev, pages_req = page_table.shape
    page_size = cache_pool.shape[2]
    head_count = queries.shape[1]

    def page_copy(slot, page):
        return pltpu.make_async_copy(
            cache_pool.at[page_table[slot, page]],
            keys.at[slot * pages_req + page],
            copy_sems.at[slot * pages_req + page],
        )

    def pages_of(slot):
        return (lengths[slot] + page_size - 1) // page_size

    for slot in range(req_dev):
        def start(page, carry, slot=slot):
            page_copy(slot, page).start()
            return carry

        lax.fori_loop(0, pages_of(slot), start, 0)

    positions = lax.broadcasted_iota(jnp.int32, (head_count, page_size), 1)
    for slot in range(req_dev):
        length = lengths[slot]
        query_rows = queries[slot]

        def score_step(page, running_max, slot=slot, length=length, query_rows=query_rows):
            page_copy(slot, page).wait()
            key_columns = keys[slot * pages_req + page]
            block = jnp.dot(query_rows, key_columns, preferred_element_type=jnp.float32) * score_scale
            block = jnp.where(positions + page * page_size < length, block, masked_score)
            scores[page] = block
            return jnp.maximum(running_max, jnp.max(block, axis=1, keepdims=True))

        row_max = lax.fori_loop(
            0, pages_of(slot), score_step, jnp.full((head_count, 1), masked_score, jnp.float32)
        )
        weighted[...] = jnp.zeros_like(weighted)

        def weight_step(page, denominator, slot=slot, length=length, row_max=row_max):
            live = positions + page * page_size < length
            exponent = jnp.where(live, jnp.exp(scores[page] - row_max), 0.0)
            value_columns = keys[slot * pages_req + page, :latent, :]
            weighted[...] += lax.dot_general(
                exponent.astype(jnp.bfloat16),
                value_columns,
                (((1,), (1,)), ((), ())),
                preferred_element_type=jnp.float32,
            )
            return denominator + jnp.sum(exponent, axis=1, keepdims=True)

        denominator = lax.fori_loop(
            0, pages_of(slot), weight_step, jnp.zeros((head_count, 1), jnp.float32)
        )
        contexts[slot] = (weighted[...] / denominator).astype(contexts.dtype)


def attend_all(queries, page_table, lengths, cache_pool, latent, score_scale):
    req_dev, head_count, width = queries.shape
    pages_req = page_table.shape[1]
    page_size = cache_pool.shape[1]
    cache_columns = jnp.swapaxes(cache_pool, 1, 2)
    kernel = functools.partial(attend_kernel, latent=latent, score_scale=score_scale)
    return pl.pallas_call(
        kernel,
        out_shape=jax.ShapeDtypeStruct((req_dev, head_count, latent), jnp.bfloat16),
        in_specs=[
            pl.BlockSpec(memory_space=pltpu.SMEM),
            pl.BlockSpec(memory_space=pltpu.SMEM),
            pl.BlockSpec(memory_space=pltpu.VMEM),
            pl.BlockSpec(memory_space=pl.ANY),
        ],
        out_specs=pl.BlockSpec(memory_space=pltpu.VMEM),
        scratch_shapes=[
            pltpu.VMEM((req_dev * pages_req, width, page_size), jnp.bfloat16),
            pltpu.VMEM((pages_req, head_count, page_size), jnp.float32),
            pltpu.VMEM((head_count, latent), jnp.float32),
            pltpu.SemaphoreType.DMA((req_dev * pages_req,)),
        ],
        compiler_params=pltpu.CompilerParams(vmem_limit_bytes=48 * 1024 * 1024),
    )(page_table, lengths, queries, cache_columns)


def swap_with(x, axis, distance, size):
    return lax.ppermute(x, axis, [(i, i ^ distance) for i in range(size)])


def halving_scatter(x, axis, size, dim=0):
    index = lax.axis_index(axis)
    x = x.astype(jnp.float32)
    distance = size // 2
    while distance >= 1:
        half = x.shape[dim] // 2
        low = lax.slice_in_dim(x, 0, half, axis=dim)
        high = lax.slice_in_dim(x, half, 2 * half, axis=dim)
        upper = (index & distance) != 0
        keep = jnp.where(upper, high, low)
        send = jnp.where(upper, low, high)
        x = keep + swap_with(send.astype(jnp.bfloat16), axis, distance, size).astype(jnp.float32)
        distance //= 2
    return x


def nearest_first_scatter(parts, axis, size):
    index = lax.axis_index(axis)
    parts = tuple(part.astype(jnp.float32) for part in parts)
    distance = 1
    while distance < size:
        half = parts[0].shape[1] // 2
        upper = (index & distance) != 0
        keeps = tuple(jnp.where(upper, part[:, half:], part[:, :half]) for part in parts)
        sends = tuple(
            jnp.where(upper, part[:, :half], part[:, half:]).astype(jnp.bfloat16) for part in parts
        )
        got = swap_with(sends, axis, distance, size)
        parts = tuple(keep + more.astype(jnp.float32) for keep, more in zip(keeps, got))
        distance *= 2
    return parts


def farthest_first_gather(x, axis, size, dim):
    index = lax.axis_index(axis)
    distance = size // 2
    while distance >= 1:
        got = swap_with(x, axis, distance, size)
        upper = (index & distance) != 0
        x = jnp.where(
            upper, jnp.concatenate([got, x], axis=dim), jnp.concatenate([x, got], axis=dim)
        )
        distance //= 2
    return x


def doubling_gather(x, axis, size, dim):
    index = lax.axis_index(axis)
    distance = 1
    while distance < size:
        got = swap_with(x, axis, distance, size)
        upper = (index & distance) != 0
        x = jnp.where(
            upper, jnp.concatenate([got, x], axis=dim), jnp.concatenate([x, got], axis=dim)
        )
        distance *= 2
    return x


def doubling_sum(x, axis, size):
    distance = 1
    while distance < size:
        x = x + swap_with(x, axis, distance, size)
        distance *= 2
    return x


def shards(
    axis_sizes,
    hidden_in,
    queries,
    cache_pool,
    page_table,
    lengths,
    value_up,
    out_proj,
    norm_gain,
    gate_proj,
    up_proj,
    down_proj,
):
    req_dev = queries.shape[0]
    latent = value_up.shape[1]
    value_dim = value_up.shape[2]
    heads_here = value_up.shape[0]
    pages_req = page_table.shape[1]
    score_scale = float(VDIM + ROPE) ** (-0.5)
    units_here = gate_proj.shape[1]
    contexts = attend_all(queries, page_table, lengths, cache_pool, latent, score_scale)
    received = lax.all_to_all(
        contexts[None], ("dp", "sub"), split_axis=2, concat_axis=0, tiled=True
    )
    received = received.reshape(-1, heads_here, latent)
    row_count = received.shape[0]
    values = jnp.einsum("rhc,hcv->rhv", received, value_up, preferred_element_type=jnp.float32)
    values = values.astype(jnp.bfloat16).reshape(row_count, heads_here * value_dim)
    group_values = lax.all_gather(values, "sub", axis=1, tiled=True)
    attention = halving_scatter(
        jnp.dot(group_values, out_proj, preferred_element_type=jnp.float32), "dp", axis_sizes["dp"]
    )
    residual = hidden_in.astype(jnp.float32) + attention
    sub_size = axis_sizes["sub"]
    all_residual = doubling_gather(residual, "dp", axis_sizes["dp"], 0)
    squares = doubling_sum(jnp.sum(all_residual * all_residual, axis=1), "sub", sub_size)
    gained = (all_residual * norm_gain.astype(jnp.float32)).astype(jnp.bfloat16)
    gate_part = jnp.dot(gained, gate_proj, preferred_element_type=jnp.float32)
    up_part = jnp.dot(gained, up_proj, preferred_element_type=jnp.float32)
    gate_sum, up_sum = nearest_first_scatter((gate_part, up_part), "sub", sub_size)
    scale_rows = lax.rsqrt(squares / float(D) + 1e-06)[:, None]
    hidden_chunk = (jax.nn.silu(gate_sum * scale_rows) * (up_sum * scale_rows)).astype(jnp.bfloat16)
    hidden_units = farthest_first_gather(hidden_chunk, "sub", sub_size, 1)
    feed_forward = halving_scatter(
        jnp.dot(hidden_units, down_proj, preferred_element_type=jnp.float32), "dp", axis_sizes["dp"]
    )
    return (attention.astype(jnp.bfloat16), (residual + feed_forward).astype(jnp.bfloat16))


def solution(mesh):
    placed = (
        P(("grp", "dp"), "sub"),
        P(("grp", "dp", "sub"), None, None),
        P(("grp", "dp", "sub"), None, None),
        P(("grp", "dp", "sub"), None),
        P(("grp", "dp", "sub")),
        P(("dp", "sub"), None, None),
        P("dp", "sub"),
        P("sub"),
        P("sub", "dp"),
        P("sub", "dp"),
        P("dp", "sub"),
    )
    return jax.shard_map(
        functools.partial(shards, dict(mesh.shape)),
        mesh=mesh,
        in_specs=placed,
        out_specs=(P(("grp", "dp"), "sub"), P(("grp", "dp"), "sub")),
        check_vma=False,
    )
```

```python
import functools

import jax
import jax.numpy as jnp
from jax import lax
from jax.experimental import pallas as pl
from jax.experimental.pallas import tpu as pltpu
from jax.sharding import PartitionSpec as P

D = 5120
ROPE = 64
VDIM = 128


masked_score = -1e30


def attend_kernel(page_table, lengths, queries, cache_pool, contexts, keys, copy_sems,
                  *, latent, score_scale):
    req_dev, pages_req = page_table.shape
    page_size = cache_pool.shape[2]
    head_count = queries.shape[1]

    def page_copy(slot, page):
        return pltpu.make_async_copy(
            cache_pool.at[page_table[slot, page]],
            keys.at[slot, :, pl.ds(pl.multiple_of(page * page_size, page_size), page_size)],
            copy_sems.at[slot * pages_req + page],
        )

    for slot in range(req_dev):
        def start(page, carry, slot=slot):
            page_copy(slot, page).start()
            return carry

        lax.fori_loop(0, pages_req, start, 0)

    span = pages_req * page_size
    positions = lax.broadcasted_iota(jnp.int32, (head_count, span), 1)
    for slot in range(req_dev):
        def finish(page, carry, slot=slot):
            page_copy(slot, page).wait()
            return carry

        lax.fori_loop(0, pages_req, finish, 0)
        live = positions < lengths[slot]
        scores = jnp.dot(queries[slot], keys[slot], preferred_element_type=jnp.float32) * score_scale
        scores = jnp.where(live, scores, masked_score)
        row_max = jnp.max(scores, axis=1, keepdims=True)
        exponent = jnp.where(live, jnp.exp(scores - row_max), 0.0)
        denominator = jnp.sum(exponent, axis=1, keepdims=True)
        weighted = lax.dot_general(
            exponent.astype(jnp.bfloat16),
            keys[slot, :latent, :],
            (((1,), (1,)), ((), ())),
            preferred_element_type=jnp.float32,
        )
        contexts[slot] = (weighted / denominator).astype(contexts.dtype)


def attend_all(queries, page_table, lengths, cache_pool, latent, score_scale):
    req_dev, head_count, width = queries.shape
    pages_req = page_table.shape[1]
    page_size = cache_pool.shape[1]
    cache_columns = jnp.swapaxes(cache_pool, 1, 2)
    kernel = functools.partial(attend_kernel, latent=latent, score_scale=score_scale)
    return pl.pallas_call(
        kernel,
        out_shape=jax.ShapeDtypeStruct((req_dev, head_count, latent), jnp.bfloat16),
        in_specs=[
            pl.BlockSpec(memory_space=pltpu.SMEM),
            pl.BlockSpec(memory_space=pltpu.SMEM),
            pl.BlockSpec(memory_space=pltpu.VMEM),
            pl.BlockSpec(memory_space=pl.ANY),
        ],
        out_specs=pl.BlockSpec(memory_space=pltpu.VMEM),
        scratch_shapes=[
            pltpu.VMEM((req_dev, width, pages_req * page_size), jnp.bfloat16),
            pltpu.SemaphoreType.DMA((req_dev * pages_req,)),
        ],
        compiler_params=pltpu.CompilerParams(vmem_limit_bytes=48 * 1024 * 1024),
    )(page_table, lengths, queries, cache_columns)


def swap_with(x, axis, distance, size):
    return lax.ppermute(x, axis, [(i, i ^ distance) for i in range(size)])


def halving_scatter(x, axis, size, dim=0):
    index = lax.axis_index(axis)
    x = x.astype(jnp.float32)
    distance = size // 2
    while distance >= 1:
        half = x.shape[dim] // 2
        low = lax.slice_in_dim(x, 0, half, axis=dim)
        high = lax.slice_in_dim(x, half, 2 * half, axis=dim)
        upper = (index & distance) != 0
        keep = jnp.where(upper, high, low)
        send = jnp.where(upper, low, high)
        x = keep + swap_with(send.astype(jnp.bfloat16), axis, distance, size).astype(jnp.float32)
        distance //= 2
    return x


def nearest_first_scatter(parts, axis, size):
    index = lax.axis_index(axis)
    parts = tuple(part.astype(jnp.float32) for part in parts)
    distance = 1
    while distance < size:
        half = parts[0].shape[1] // 2
        upper = (index & distance) != 0
        keeps = tuple(jnp.where(upper, part[:, half:], part[:, :half]) for part in parts)
        sends = tuple(
            jnp.where(upper, part[:, :half], part[:, half:]).astype(jnp.bfloat16) for part in parts
        )
        got = swap_with(sends, axis, distance, size)
        parts = tuple(keep + more.astype(jnp.float32) for keep, more in zip(keeps, got))
        distance *= 2
    return parts


def farthest_first_gather(x, axis, size, dim):
    index = lax.axis_index(axis)
    distance = size // 2
    while distance >= 1:
        got = swap_with(x, axis, distance, size)
        upper = (index & distance) != 0
        x = jnp.where(
            upper, jnp.concatenate([got, x], axis=dim), jnp.concatenate([x, got], axis=dim)
        )
        distance //= 2
    return x


def doubling_gather(x, axis, size, dim):
    index = lax.axis_index(axis)
    distance = 1
    while distance < size:
        got = swap_with(x, axis, distance, size)
        upper = (index & distance) != 0
        x = jnp.where(
            upper, jnp.concatenate([got, x], axis=dim), jnp.concatenate([x, got], axis=dim)
        )
        distance *= 2
    return x


def doubling_sum(x, axis, size):
    distance = 1
    while distance < size:
        x = x + swap_with(x, axis, distance, size)
        distance *= 2
    return x


def shards(
    axis_sizes,
    hidden_in,
    queries,
    cache_pool,
    page_table,
    lengths,
    value_up,
    out_proj,
    norm_gain,
    gate_proj,
    up_proj,
    down_proj,
):
    req_dev = queries.shape[0]
    latent = value_up.shape[1]
    value_dim = value_up.shape[2]
    heads_here = value_up.shape[0]
    pages_req = page_table.shape[1]
    score_scale = float(VDIM + ROPE) ** (-0.5)
    units_here = gate_proj.shape[1]
    contexts = attend_all(queries, page_table, lengths, cache_pool, latent, score_scale)
    received = lax.all_to_all(
        contexts[None], ("dp", "sub"), split_axis=2, concat_axis=0, tiled=True
    )
    received = received.reshape(-1, heads_here, latent)
    row_count = received.shape[0]
    values = jnp.einsum("rhc,hcv->rhv", received, value_up, preferred_element_type=jnp.float32)
    values = values.astype(jnp.bfloat16).reshape(row_count, heads_here * value_dim)
    group_values = lax.all_gather(values, "sub", axis=1, tiled=True)
    attention = halving_scatter(
        jnp.dot(group_values, out_proj, preferred_element_type=jnp.float32), "dp", axis_sizes["dp"]
    )
    residual = hidden_in.astype(jnp.float32) + attention
    sub_size = axis_sizes["sub"]
    all_residual = doubling_gather(residual, "dp", axis_sizes["dp"], 0)
    squares = doubling_sum(jnp.sum(all_residual * all_residual, axis=1), "sub", sub_size)
    gained = (all_residual * norm_gain.astype(jnp.float32)).astype(jnp.bfloat16)
    gate_part = jnp.dot(gained, gate_proj, preferred_element_type=jnp.float32)
    up_part = jnp.dot(gained, up_proj, preferred_element_type=jnp.float32)
    gate_sum, up_sum = nearest_first_scatter((gate_part, up_part), "sub", sub_size)
    scale_rows = lax.rsqrt(squares / float(D) + 1e-06)[:, None]
    hidden_chunk = (jax.nn.silu(gate_sum * scale_rows) * (up_sum * scale_rows)).astype(jnp.bfloat16)
    hidden_units = farthest_first_gather(hidden_chunk, "sub", sub_size, 1)
    feed_forward = halving_scatter(
        jnp.dot(hidden_units, down_proj, preferred_element_type=jnp.float32), "dp", axis_sizes["dp"]
    )
    return (attention.astype(jnp.bfloat16), (residual + feed_forward).astype(jnp.bfloat16))


def solution(mesh):
    placed = (
        P(("grp", "dp"), "sub"),
        P(("grp", "dp", "sub"), None, None),
        P(("grp", "dp", "sub"), None, None),
        P(("grp", "dp", "sub"), None),
        P(("grp", "dp", "sub")),
        P(("dp", "sub"), None, None),
        P("dp", "sub"),
        P("sub"),
        P("sub", "dp"),
        P("sub", "dp"),
        P("dp", "sub"),
    )
    return jax.shard_map(
        functools.partial(shards, dict(mesh.shape)),
        mesh=mesh,
        in_specs=placed,
        out_specs=(P(("grp", "dp"), "sub"), P(("grp", "dp"), "sub")),
        check_vma=False,
    )
```

```python
import functools

import jax
import jax.numpy as jnp
from jax import lax
from jax.experimental import pallas as pl
from jax.experimental.pallas import tpu as pltpu
from jax.sharding import PartitionSpec as P

D = 5120
ROPE = 64
VDIM = 128


masked_score = -1e30


def attend_kernel(page_table, lengths, queries, cache_pool, contexts, keys, copy_sems,
                  *, latent, score_scale):
    req_dev, pages_req = page_table.shape
    page_size = cache_pool.shape[2]
    head_count = queries.shape[1]

    def page_copy(slot, page):
        return pltpu.make_async_copy(
            cache_pool.at[page_table[slot, page]],
            keys.at[slot, :, pl.ds(pl.multiple_of(page * page_size, page_size), page_size)],
            copy_sems.at[slot * pages_req + page],
        )

    for slot in range(req_dev):
        def start(page, carry, slot=slot):
            page_copy(slot, page).start()
            return carry

        lax.fori_loop(0, pages_req, start, 0)

    span = pages_req * page_size
    positions = lax.broadcasted_iota(jnp.int32, (head_count, span), 1)
    for slot in range(req_dev):
        def finish(page, carry, slot=slot):
            page_copy(slot, page).wait()
            return carry

        lax.fori_loop(0, pages_req, finish, 0)
        live = positions < lengths[slot]
        scores = jnp.dot(queries[slot], keys[slot], preferred_element_type=jnp.float32) * score_scale
        scores = jnp.where(live, scores, masked_score)
        row_max = jnp.max(scores, axis=1, keepdims=True)
        exponent = jnp.where(live, jnp.exp(scores - row_max), 0.0)
        denominator = jnp.sum(exponent, axis=1, keepdims=True)
        weighted = lax.dot_general(
            exponent.astype(jnp.bfloat16),
            keys[slot, :latent, :],
            (((1,), (1,)), ((), ())),
            preferred_element_type=jnp.float32,
        )
        contexts[slot] = (weighted / denominator).astype(contexts.dtype)


def attend_all(queries, page_table, lengths, cache_pool, latent, score_scale):
    req_dev, head_count, width = queries.shape
    pages_req = page_table.shape[1]
    page_size = cache_pool.shape[1]
    cache_columns = jnp.swapaxes(cache_pool, 1, 2)
    kernel = functools.partial(attend_kernel, latent=latent, score_scale=score_scale)
    return pl.pallas_call(
        kernel,
        out_shape=jax.ShapeDtypeStruct((req_dev, head_count, latent), jnp.bfloat16),
        in_specs=[
            pl.BlockSpec(memory_space=pltpu.SMEM),
            pl.BlockSpec(memory_space=pltpu.SMEM),
            pl.BlockSpec(memory_space=pltpu.VMEM),
            pl.BlockSpec(memory_space=pl.ANY),
        ],
        out_specs=pl.BlockSpec(memory_space=pltpu.VMEM),
        scratch_shapes=[
            pltpu.VMEM((req_dev, width, pages_req * page_size), jnp.bfloat16),
            pltpu.SemaphoreType.DMA((req_dev * pages_req,)),
        ],
        compiler_params=pltpu.CompilerParams(vmem_limit_bytes=48 * 1024 * 1024),
    )(page_table, lengths, queries, cache_columns)


def swap_with(x, axis, distance, size):
    return lax.ppermute(x, axis, [(i, i ^ distance) for i in range(size)])


def halving_scatter(x, axis, size, dim=0):
    index = lax.axis_index(axis)
    x = x.astype(jnp.float32)
    distance = size // 2
    while distance >= 1:
        half = x.shape[dim] // 2
        low = lax.slice_in_dim(x, 0, half, axis=dim)
        high = lax.slice_in_dim(x, half, 2 * half, axis=dim)
        upper = (index & distance) != 0
        keep = jnp.where(upper, high, low)
        send = jnp.where(upper, low, high)
        x = keep + swap_with(send.astype(jnp.bfloat16), axis, distance, size).astype(jnp.float32)
        distance //= 2
    return x


def nearest_first_scatter(parts, axis, size):
    index = lax.axis_index(axis)
    parts = tuple(part.astype(jnp.float32) for part in parts)
    distance = 1
    while distance < size:
        half = parts[0].shape[1] // 2
        upper = (index & distance) != 0
        keeps = tuple(jnp.where(upper, part[:, half:], part[:, :half]) for part in parts)
        sends = tuple(
            jnp.where(upper, part[:, :half], part[:, half:]).astype(jnp.bfloat16) for part in parts
        )
        got = swap_with(sends, axis, distance, size)
        parts = tuple(keep + more.astype(jnp.float32) for keep, more in zip(keeps, got))
        distance *= 2
    return parts


def farthest_first_gather(x, axis, size, dim):
    index = lax.axis_index(axis)
    distance = size // 2
    while distance >= 1:
        got = swap_with(x, axis, distance, size)
        upper = (index & distance) != 0
        x = jnp.where(
            upper, jnp.concatenate([got, x], axis=dim), jnp.concatenate([x, got], axis=dim)
        )
        distance //= 2
    return x


def doubling_gather(x, axis, size, dim):
    index = lax.axis_index(axis)
    distance = 1
    while distance < size:
        got = swap_with(x, axis, distance, size)
        upper = (index & distance) != 0
        x = jnp.where(
            upper, jnp.concatenate([got, x], axis=dim), jnp.concatenate([x, got], axis=dim)
        )
        distance *= 2
    return x


def doubling_sum(x, axis, size):
    distance = 1
    while distance < size:
        x = x + swap_with(x, axis, distance, size)
        distance *= 2
    return x


def nearest_first_rows_scatter(x, axis, size):
    index = lax.axis_index(axis)
    x = x.astype(jnp.float32)
    x = x.reshape((size, x.shape[0] // size) + x.shape[1:])
    distance = 1
    while distance < size:
        pairs = x.reshape((x.shape[0] // 2, 2) + x.shape[1:])
        upper = (index & distance) != 0
        keep = jnp.where(upper, pairs[:, 1], pairs[:, 0])
        send = jnp.where(upper, pairs[:, 0], pairs[:, 1])
        x = keep + swap_with(send.astype(jnp.bfloat16), axis, distance, size).astype(jnp.float32)
        distance *= 2
    return x[0]


def farthest_first_rows_gather(x, axis, size):
    index = lax.axis_index(axis)
    x = x[None]
    distance = size // 2
    while distance >= 1:
        got = swap_with(x, axis, distance, size)
        upper = (index & distance) != 0
        x = jnp.where(upper, jnp.stack([got, x], axis=1), jnp.stack([x, got], axis=1))
        x = x.reshape((-1,) + x.shape[2:])
        distance //= 2
    return x.reshape((-1,) + x.shape[2:])


def shards(
    axis_sizes,
    hidden_in,
    queries,
    cache_pool,
    page_table,
    lengths,
    value_up,
    out_proj,
    norm_gain,
    gate_proj,
    up_proj,
    down_proj,
):
    req_dev = queries.shape[0]
    latent = value_up.shape[1]
    value_dim = value_up.shape[2]
    heads_here = value_up.shape[0]
    pages_req = page_table.shape[1]
    score_scale = float(VDIM + ROPE) ** (-0.5)
    units_here = gate_proj.shape[1]
    contexts = attend_all(queries, page_table, lengths, cache_pool, latent, score_scale)
    received = lax.all_to_all(
        contexts[None], ("dp", "sub"), split_axis=2, concat_axis=0, tiled=True
    )
    received = received.reshape(-1, heads_here, latent)
    row_count = received.shape[0]
    values = jnp.einsum("rhc,hcv->rhv", received, value_up, preferred_element_type=jnp.float32)
    values = values.astype(jnp.bfloat16).reshape(row_count, heads_here * value_dim)
    group_values = lax.all_gather(values, "sub", axis=1, tiled=True)
    attention = nearest_first_rows_scatter(
        jnp.dot(group_values, out_proj, preferred_element_type=jnp.float32), "dp", axis_sizes["dp"]
    )
    residual = hidden_in.astype(jnp.float32) + attention
    sub_size = axis_sizes["sub"]
    all_residual = farthest_first_rows_gather(residual, "dp", axis_sizes["dp"])
    squares = doubling_sum(jnp.sum(all_residual * all_residual, axis=1), "sub", sub_size)
    gained = (all_residual * norm_gain.astype(jnp.float32)).astype(jnp.bfloat16)
    gate_part = jnp.dot(gained, gate_proj, preferred_element_type=jnp.float32)
    up_part = jnp.dot(gained, up_proj, preferred_element_type=jnp.float32)
    gate_sum, up_sum = nearest_first_scatter((gate_part, up_part), "sub", sub_size)
    scale_rows = lax.rsqrt(squares / float(D) + 1e-06)[:, None]
    hidden_chunk = (jax.nn.silu(gate_sum * scale_rows) * (up_sum * scale_rows)).astype(jnp.bfloat16)
    hidden_units = farthest_first_gather(hidden_chunk, "sub", sub_size, 1)
    feed_forward = nearest_first_rows_scatter(
        jnp.dot(hidden_units, down_proj, preferred_element_type=jnp.float32), "dp", axis_sizes["dp"]
    )
    return (attention.astype(jnp.bfloat16), (residual + feed_forward).astype(jnp.bfloat16))


def solution(mesh):
    placed = (
        P(("grp", "dp"), "sub"),
        P(("grp", "dp", "sub"), None, None),
        P(("grp", "dp", "sub"), None, None),
        P(("grp", "dp", "sub"), None),
        P(("grp", "dp", "sub")),
        P(("dp", "sub"), None, None),
        P("dp", "sub"),
        P("sub"),
        P("sub", "dp"),
        P("sub", "dp"),
        P("dp", "sub"),
    )
    return jax.shard_map(
        functools.partial(shards, dict(mesh.shape)),
        mesh=mesh,
        in_specs=placed,
        out_specs=(P(("grp", "dp"), "sub"), P(("grp", "dp"), "sub")),
        check_vma=False,
    )
```

```python
import functools

import jax
import jax.numpy as jnp
from jax import lax
from jax.experimental import pallas as pl
from jax.experimental.pallas import tpu as pltpu
from jax.sharding import PartitionSpec as P

D = 5120
ROPE = 64
VDIM = 128


masked_score = -1e30


def attend_kernel(page_table, lengths, queries, cache_pool, contexts, keys, copy_sems,
                  *, latent, score_scale):
    req_dev, pages_req = page_table.shape
    page_size = cache_pool.shape[2]
    head_count = queries.shape[1]

    def page_copy(slot, page):
        return pltpu.make_async_copy(
            cache_pool.at[page_table[slot, page]],
            keys.at[slot, :, pl.ds(pl.multiple_of(page * page_size, page_size), page_size)],
            copy_sems.at[slot * pages_req + page],
        )

    for slot in range(req_dev):
        def start(page, carry, slot=slot):
            page_copy(slot, page).start()
            return carry

        lax.fori_loop(0, pages_req, start, 0)

    span = pages_req * page_size
    positions = lax.broadcasted_iota(jnp.int32, (head_count, span), 1)
    for slot in range(req_dev):
        def finish(page, carry, slot=slot):
            page_copy(slot, page).wait()
            return carry

        lax.fori_loop(0, pages_req, finish, 0)
        live = positions < lengths[slot]
        scores = jnp.dot(queries[slot], keys[slot], preferred_element_type=jnp.float32) * score_scale
        scores = jnp.where(live, scores, masked_score)
        row_max = jnp.max(scores, axis=1, keepdims=True)
        exponent = jnp.exp(scores - row_max)
        denominator = jnp.sum(exponent, axis=1, keepdims=True)
        weighted = lax.dot_general(
            exponent.astype(jnp.bfloat16),
            keys[slot, :latent, :],
            (((1,), (1,)), ((), ())),
            preferred_element_type=jnp.float32,
        )
        contexts[slot] = (weighted / denominator).astype(contexts.dtype)


def attend_all(queries, page_table, lengths, cache_pool, latent, score_scale):
    req_dev, head_count, width = queries.shape
    pages_req = page_table.shape[1]
    page_size = cache_pool.shape[1]
    cache_columns = jnp.swapaxes(cache_pool, 1, 2)
    kernel = functools.partial(attend_kernel, latent=latent, score_scale=score_scale)
    return pl.pallas_call(
        kernel,
        out_shape=jax.ShapeDtypeStruct((req_dev, head_count, latent), jnp.bfloat16),
        in_specs=[
            pl.BlockSpec(memory_space=pltpu.SMEM),
            pl.BlockSpec(memory_space=pltpu.SMEM),
            pl.BlockSpec(memory_space=pltpu.VMEM),
            pl.BlockSpec(memory_space=pl.ANY),
        ],
        out_specs=pl.BlockSpec(memory_space=pltpu.VMEM),
        scratch_shapes=[
            pltpu.VMEM((req_dev, width, pages_req * page_size), jnp.bfloat16),
            pltpu.SemaphoreType.DMA((req_dev * pages_req,)),
        ],
        compiler_params=pltpu.CompilerParams(vmem_limit_bytes=48 * 1024 * 1024),
    )(page_table, lengths, queries, cache_columns)


def swap_with(x, axis, distance, size):
    return lax.ppermute(x, axis, [(i, i ^ distance) for i in range(size)])


def halving_scatter(x, axis, size, dim=0):
    index = lax.axis_index(axis)
    x = x.astype(jnp.float32)
    distance = size // 2
    while distance >= 1:
        half = x.shape[dim] // 2
        low = lax.slice_in_dim(x, 0, half, axis=dim)
        high = lax.slice_in_dim(x, half, 2 * half, axis=dim)
        upper = (index & distance) != 0
        keep = jnp.where(upper, high, low)
        send = jnp.where(upper, low, high)
        x = keep + swap_with(send.astype(jnp.bfloat16), axis, distance, size).astype(jnp.float32)
        distance //= 2
    return x


def nearest_first_scatter(parts, axis, size):
    index = lax.axis_index(axis)
    parts = tuple(part.astype(jnp.float32) for part in parts)
    distance = 1
    while distance < size:
        half = parts[0].shape[1] // 2
        upper = (index & distance) != 0
        keeps = tuple(jnp.where(upper, part[:, half:], part[:, :half]) for part in parts)
        sends = tuple(
            jnp.where(upper, part[:, :half], part[:, half:]).astype(jnp.bfloat16) for part in parts
        )
        got = swap_with(sends, axis, distance, size)
        parts = tuple(keep + more.astype(jnp.float32) for keep, more in zip(keeps, got))
        distance *= 2
    return parts


def farthest_first_gather(x, axis, size, dim):
    index = lax.axis_index(axis)
    distance = size // 2
    while distance >= 1:
        got = swap_with(x, axis, distance, size)
        upper = (index & distance) != 0
        x = jnp.where(
            upper, jnp.concatenate([got, x], axis=dim), jnp.concatenate([x, got], axis=dim)
        )
        distance //= 2
    return x


def doubling_gather(x, axis, size, dim):
    index = lax.axis_index(axis)
    distance = 1
    while distance < size:
        got = swap_with(x, axis, distance, size)
        upper = (index & distance) != 0
        x = jnp.where(
            upper, jnp.concatenate([got, x], axis=dim), jnp.concatenate([x, got], axis=dim)
        )
        distance *= 2
    return x


def doubling_sum(x, axis, size):
    distance = 1
    while distance < size:
        x = x + swap_with(x, axis, distance, size)
        distance *= 2
    return x


def nearest_first_rows_scatter(x, axis, size):
    index = lax.axis_index(axis)
    x = x.astype(jnp.float32)
    x = x.reshape((size, x.shape[0] // size) + x.shape[1:])
    distance = 1
    while distance < size:
        pairs = x.reshape((x.shape[0] // 2, 2) + x.shape[1:])
        upper = (index & distance) != 0
        keep = jnp.where(upper, pairs[:, 1], pairs[:, 0])
        send = jnp.where(upper, pairs[:, 0], pairs[:, 1])
        x = keep + swap_with(send.astype(jnp.bfloat16), axis, distance, size).astype(jnp.float32)
        distance *= 2
    return x[0]


def farthest_first_rows_gather(x, axis, size):
    index = lax.axis_index(axis)
    x = x[None]
    distance = size // 2
    while distance >= 1:
        got = swap_with(x, axis, distance, size)
        upper = (index & distance) != 0
        x = jnp.where(upper, jnp.stack([got, x], axis=1), jnp.stack([x, got], axis=1))
        x = x.reshape((-1,) + x.shape[2:])
        distance //= 2
    return x.reshape((-1,) + x.shape[2:])


def matched_sum(x, axis, size):
    x = x.astype(jnp.float32)
    distance = 1
    while distance < size:
        mine = x.astype(jnp.bfloat16)
        x = mine.astype(jnp.float32) + swap_with(mine, axis, distance, size).astype(jnp.float32)
        distance *= 2
    return x


def shards(
    axis_sizes,
    hidden_in,
    queries,
    cache_pool,
    page_table,
    lengths,
    value_up,
    out_proj,
    norm_gain,
    gate_proj,
    up_proj,
    down_proj,
):
    req_dev = queries.shape[0]
    latent = value_up.shape[1]
    value_dim = value_up.shape[2]
    heads_here = value_up.shape[0]
    pages_req = page_table.shape[1]
    score_scale = float(VDIM + ROPE) ** (-0.5)
    units_here = gate_proj.shape[1]
    contexts = attend_all(queries, page_table, lengths, cache_pool, latent, score_scale)
    received = lax.all_to_all(
        contexts[None], ("dp", "sub"), split_axis=2, concat_axis=0, tiled=True
    )
    received = received.reshape(-1, heads_here, latent)
    row_count = received.shape[0]
    values = jnp.einsum("rhc,hcv->rhv", received, value_up, preferred_element_type=jnp.float32)
    values = values.astype(jnp.bfloat16).reshape(row_count, heads_here * value_dim)
    group_values = lax.all_gather(values, "sub", axis=1, tiled=True)
    dp_size = axis_sizes["dp"]
    sub_size = axis_sizes["sub"]
    attention_all = matched_sum(
        jnp.dot(group_values, out_proj, preferred_element_type=jnp.float32), "dp", dp_size
    )
    hidden_all = farthest_first_rows_gather(hidden_in, "dp", dp_size)
    all_residual = hidden_all.astype(jnp.float32) + attention_all
    squares = doubling_sum(jnp.sum(all_residual * all_residual, axis=1), "sub", sub_size)
    gained = (all_residual * norm_gain.astype(jnp.float32)).astype(jnp.bfloat16)
    gate_part = jnp.dot(gained, gate_proj, preferred_element_type=jnp.float32)
    up_part = jnp.dot(gained, up_proj, preferred_element_type=jnp.float32)
    gate_sum, up_sum = nearest_first_scatter((gate_part, up_part), "sub", sub_size)
    scale_rows = lax.rsqrt(squares / float(D) + 1e-06)[:, None]
    hidden_chunk = (jax.nn.silu(gate_sum * scale_rows) * (up_sum * scale_rows)).astype(jnp.bfloat16)
    hidden_units = farthest_first_gather(hidden_chunk, "sub", sub_size, 1)
    feed_forward = nearest_first_rows_scatter(
        jnp.dot(hidden_units, down_proj, preferred_element_type=jnp.float32), "dp", axis_sizes["dp"]
    )
    own_rows = hidden_in.shape[0]
    first_row = lax.axis_index("dp") * own_rows
    attention = lax.dynamic_slice_in_dim(attention_all, first_row, own_rows, 0)
    residual = lax.dynamic_slice_in_dim(all_residual, first_row, own_rows, 0)
    return (attention.astype(jnp.bfloat16), (residual + feed_forward).astype(jnp.bfloat16))


def solution(mesh):
    placed = (
        P(("grp", "dp"), "sub"),
        P(("grp", "dp", "sub"), None, None),
        P(("grp", "dp", "sub"), None, None),
        P(("grp", "dp", "sub"), None),
        P(("grp", "dp", "sub")),
        P(("dp", "sub"), None, None),
        P("dp", "sub"),
        P("sub"),
        P("sub", "dp"),
        P("sub", "dp"),
        P("dp", "sub"),
    )
    return jax.shard_map(
        functools.partial(shards, dict(mesh.shape)),
        mesh=mesh,
        in_specs=placed,
        out_specs=(P(("grp", "dp"), "sub"), P(("grp", "dp"), "sub")),
        check_vma=False,
    )
```

```python
import functools

import jax
import jax.numpy as jnp
from jax import lax
from jax.experimental import pallas as pl
from jax.experimental.pallas import tpu as pltpu
from jax.sharding import PartitionSpec as P

D = 5120
ROPE = 64
VDIM = 128


masked_score = -1e30


def attend_kernel(page_table, lengths, queries, cache_pool, contexts, keys, copy_sems,
                  *, latent, score_scale):
    req_dev, pages_req = page_table.shape
    page_size = cache_pool.shape[2]
    head_count = queries.shape[2]

    def page_copy(slot, page):
        return pltpu.make_async_copy(
            cache_pool.at[page_table[slot, page]],
            keys.at[slot, :, pl.ds(pl.multiple_of(page * page_size, page_size), page_size)],
            copy_sems.at[slot * pages_req + page],
        )

    for slot in range(req_dev):
        def start(page, carry, slot=slot):
            page_copy(slot, page).start()
            return carry

        lax.fori_loop(0, pages_req, start, 0)

    span = pages_req * page_size
    positions = lax.broadcasted_iota(jnp.int32, (head_count, span), 1)
    for slot in range(req_dev):
        def finish(page, carry, slot=slot):
            page_copy(slot, page).wait()
            return carry

        lax.fori_loop(0, pages_req, finish, 0)
        live = positions < lengths[slot]
        query_rows = jnp.transpose(queries[slot])
        scores = jnp.dot(query_rows, keys[slot], preferred_element_type=jnp.float32) * score_scale
        scores = jnp.where(live, scores, masked_score)
        row_max = jnp.max(scores, axis=1, keepdims=True)
        exponent = jnp.exp(scores - row_max)
        denominator = jnp.sum(exponent, axis=1, keepdims=True)
        weighted = lax.dot_general(
            exponent.astype(jnp.bfloat16),
            keys[slot, :latent, :],
            (((1,), (1,)), ((), ())),
            preferred_element_type=jnp.float32,
        )
        contexts[slot] = (weighted / denominator).astype(contexts.dtype)


def attend_all(queries, page_table, lengths, cache_pool, latent, score_scale):
    req_dev, head_count, width = queries.shape
    pages_req = page_table.shape[1]
    query_columns = jnp.swapaxes(queries, 1, 2)
    page_size = cache_pool.shape[1]
    cache_columns = jnp.swapaxes(cache_pool, 1, 2)
    kernel = functools.partial(attend_kernel, latent=latent, score_scale=score_scale)
    return pl.pallas_call(
        kernel,
        out_shape=jax.ShapeDtypeStruct((req_dev, head_count, latent), jnp.bfloat16),
        in_specs=[
            pl.BlockSpec(memory_space=pltpu.SMEM),
            pl.BlockSpec(memory_space=pltpu.SMEM),
            pl.BlockSpec(memory_space=pltpu.VMEM),
            pl.BlockSpec(memory_space=pl.ANY),
        ],
        out_specs=pl.BlockSpec(memory_space=pltpu.VMEM),
        scratch_shapes=[
            pltpu.VMEM((req_dev, width, pages_req * page_size), jnp.bfloat16),
            pltpu.SemaphoreType.DMA((req_dev * pages_req,)),
        ],
        compiler_params=pltpu.CompilerParams(vmem_limit_bytes=48 * 1024 * 1024),
    )(page_table, lengths, query_columns, cache_columns)


def swap_with(x, axis, distance, size):
    return lax.ppermute(x, axis, [(i, i ^ distance) for i in range(size)])


def halving_scatter(x, axis, size, dim=0):
    index = lax.axis_index(axis)
    x = x.astype(jnp.float32)
    distance = size // 2
    while distance >= 1:
        half = x.shape[dim] // 2
        low = lax.slice_in_dim(x, 0, half, axis=dim)
        high = lax.slice_in_dim(x, half, 2 * half, axis=dim)
        upper = (index & distance) != 0
        keep = jnp.where(upper, high, low)
        send = jnp.where(upper, low, high)
        x = keep + swap_with(send.astype(jnp.bfloat16), axis, distance, size).astype(jnp.float32)
        distance //= 2
    return x


def nearest_first_scatter(parts, axis, size):
    index = lax.axis_index(axis)
    parts = tuple(part.astype(jnp.float32) for part in parts)
    distance = 1
    while distance < size:
        half = parts[0].shape[1] // 2
        upper = (index & distance) != 0
        keeps = tuple(jnp.where(upper, part[:, half:], part[:, :half]) for part in parts)
        sends = tuple(
            jnp.where(upper, part[:, :half], part[:, half:]).astype(jnp.bfloat16) for part in parts
        )
        got = swap_with(sends, axis, distance, size)
        parts = tuple(keep + more.astype(jnp.float32) for keep, more in zip(keeps, got))
        distance *= 2
    return parts


def farthest_first_gather(x, axis, size, dim):
    index = lax.axis_index(axis)
    distance = size // 2
    while distance >= 1:
        got = swap_with(x, axis, distance, size)
        upper = (index & distance) != 0
        x = jnp.where(
            upper, jnp.concatenate([got, x], axis=dim), jnp.concatenate([x, got], axis=dim)
        )
        distance //= 2
    return x


def doubling_gather(x, axis, size, dim):
    index = lax.axis_index(axis)
    distance = 1
    while distance < size:
        got = swap_with(x, axis, distance, size)
        upper = (index & distance) != 0
        x = jnp.where(
            upper, jnp.concatenate([got, x], axis=dim), jnp.concatenate([x, got], axis=dim)
        )
        distance *= 2
    return x


def doubling_sum(x, axis, size):
    distance = 1
    while distance < size:
        x = x + swap_with(x, axis, distance, size)
        distance *= 2
    return x


def nearest_first_rows_scatter(x, axis, size):
    index = lax.axis_index(axis)
    x = x.astype(jnp.float32)
    x = x.reshape((size, x.shape[0] // size) + x.shape[1:])
    distance = 1
    while distance < size:
        pairs = x.reshape((x.shape[0] // 2, 2) + x.shape[1:])
        upper = (index & distance) != 0
        keep = jnp.where(upper, pairs[:, 1], pairs[:, 0])
        send = jnp.where(upper, pairs[:, 0], pairs[:, 1])
        x = keep + swap_with(send.astype(jnp.bfloat16), axis, distance, size).astype(jnp.float32)
        distance *= 2
    return x[0]


def farthest_first_rows_gather(x, axis, size):
    index = lax.axis_index(axis)
    x = x[None]
    distance = size // 2
    while distance >= 1:
        got = swap_with(x, axis, distance, size)
        upper = (index & distance) != 0
        x = jnp.where(upper, jnp.stack([got, x], axis=1), jnp.stack([x, got], axis=1))
        x = x.reshape((-1,) + x.shape[2:])
        distance //= 2
    return x.reshape((-1,) + x.shape[2:])


def matched_sum(x, axis, size):
    x = x.astype(jnp.float32)
    distance = 1
    while distance < size:
        mine = x.astype(jnp.bfloat16)
        x = mine.astype(jnp.float32) + swap_with(mine, axis, distance, size).astype(jnp.float32)
        distance *= 2
    return x


def shards(
    axis_sizes,
    hidden_in,
    queries,
    cache_pool,
    page_table,
    lengths,
    value_up,
    out_proj,
    norm_gain,
    gate_proj,
    up_proj,
    down_proj,
):
    req_dev = queries.shape[0]
    latent = value_up.shape[1]
    value_dim = value_up.shape[2]
    heads_here = value_up.shape[0]
    pages_req = page_table.shape[1]
    score_scale = float(VDIM + ROPE) ** (-0.5)
    units_here = gate_proj.shape[1]
    contexts = attend_all(queries, page_table, lengths, cache_pool, latent, score_scale)
    received = lax.all_to_all(
        contexts[None], ("dp", "sub"), split_axis=2, concat_axis=0, tiled=True
    )
    received = received.reshape(-1, heads_here, latent)
    row_count = received.shape[0]
    values = jnp.einsum("rhc,hcv->rhv", received, value_up, preferred_element_type=jnp.float32)
    values = values.astype(jnp.bfloat16).reshape(row_count, heads_here * value_dim)
    group_values = lax.all_gather(values, "sub", axis=1, tiled=True)
    dp_size = axis_sizes["dp"]
    sub_size = axis_sizes["sub"]
    attention_all = matched_sum(
        jnp.dot(group_values, out_proj, preferred_element_type=jnp.float32), "dp", dp_size
    )
    hidden_all = farthest_first_rows_gather(hidden_in, "dp", dp_size)
    all_residual = hidden_all.astype(jnp.float32) + attention_all
    squares = doubling_sum(jnp.sum(all_residual * all_residual, axis=1), "sub", sub_size)
    gained = (all_residual * norm_gain.astype(jnp.float32)).astype(jnp.bfloat16)
    gate_part = jnp.dot(gained, gate_proj, preferred_element_type=jnp.float32)
    up_part = jnp.dot(gained, up_proj, preferred_element_type=jnp.float32)
    gate_sum, up_sum = nearest_first_scatter((gate_part, up_part), "sub", sub_size)
    scale_rows = lax.rsqrt(squares / float(D) + 1e-06)[:, None]
    hidden_chunk = (jax.nn.silu(gate_sum * scale_rows) * (up_sum * scale_rows)).astype(jnp.bfloat16)
    hidden_units = farthest_first_gather(hidden_chunk, "sub", sub_size, 1)
    feed_forward = nearest_first_rows_scatter(
        jnp.dot(hidden_units, down_proj, preferred_element_type=jnp.float32), "dp", axis_sizes["dp"]
    )
    own_rows = hidden_in.shape[0]
    first_row = lax.axis_index("dp") * own_rows
    attention = lax.dynamic_slice_in_dim(attention_all, first_row, own_rows, 0)
    residual = lax.dynamic_slice_in_dim(all_residual, first_row, own_rows, 0)
    return (attention.astype(jnp.bfloat16), (residual + feed_forward).astype(jnp.bfloat16))


def solution(mesh):
    placed = (
        P(("grp", "dp"), "sub"),
        P(("grp", "dp", "sub"), None, None),
        P(("grp", "dp", "sub"), None, None),
        P(("grp", "dp", "sub"), None),
        P(("grp", "dp", "sub")),
        P(("dp", "sub"), None, None),
        P("dp", "sub"),
        P("sub"),
        P("sub", "dp"),
        P("sub", "dp"),
        P("dp", "sub"),
    )
    return jax.shard_map(
        functools.partial(shards, dict(mesh.shape)),
        mesh=mesh,
        in_specs=placed,
        out_specs=(P(("grp", "dp"), "sub"), P(("grp", "dp"), "sub")),
        check_vma=False,
    )
```

```python
import functools

import jax
import jax.numpy as jnp
from jax import lax
from jax.experimental import pallas as pl
from jax.experimental.pallas import tpu as pltpu
from jax.sharding import PartitionSpec as P

D = 5120
ROPE = 64
VDIM = 128


masked_score = -1e30


def attend_kernel(page_table, lengths, queries, cache_pool, contexts, keys, copy_sems,
                  *, latent, score_scale):
    req_dev, pages_req = page_table.shape
    page_size = cache_pool.shape[2]
    head_count = queries.shape[2]

    def page_copy(slot, page):
        return pltpu.make_async_copy(
            cache_pool.at[page_table[slot, page]],
            keys.at[slot, :, pl.ds(pl.multiple_of(page * page_size, page_size), page_size)],
            copy_sems.at[slot * pages_req + page],
        )

    for slot in range(req_dev):
        def start(page, carry, slot=slot):
            page_copy(slot, page).start()
            return carry

        lax.fori_loop(0, pages_req, start, 0)

    span = pages_req * page_size
    positions = lax.broadcasted_iota(jnp.int32, (head_count, span), 1)
    for slot in range(req_dev):
        def finish(page, carry, slot=slot):
            page_copy(slot, page).wait()
            return carry

        lax.fori_loop(0, pages_req, finish, 0)
        live = positions < lengths[slot]
        query_rows = jnp.transpose(queries[slot])
        scores = jnp.dot(query_rows, keys[slot], preferred_element_type=jnp.float32) * score_scale
        scores = jnp.where(live, scores, masked_score)
        row_max = jnp.max(scores, axis=1, keepdims=True)
        exponent = jnp.exp(scores - row_max)
        denominator = jnp.sum(exponent, axis=1, keepdims=True)
        weighted = lax.dot_general(
            exponent.astype(jnp.bfloat16),
            keys[slot, :latent, :],
            (((1,), (1,)), ((), ())),
            preferred_element_type=jnp.float32,
        )
        contexts[slot] = (weighted / denominator).astype(contexts.dtype)


def attend_all(queries, page_table, lengths, cache_pool, latent, score_scale):
    req_dev, head_count, width = queries.shape
    pages_req = page_table.shape[1]
    query_columns = jnp.swapaxes(queries, 1, 2)
    page_size = cache_pool.shape[1]
    cache_columns = jnp.swapaxes(cache_pool, 1, 2)
    kernel = functools.partial(attend_kernel, latent=latent, score_scale=score_scale)
    return pl.pallas_call(
        kernel,
        out_shape=jax.ShapeDtypeStruct((req_dev, head_count, latent), jnp.bfloat16),
        in_specs=[
            pl.BlockSpec(memory_space=pltpu.SMEM),
            pl.BlockSpec(memory_space=pltpu.SMEM),
            pl.BlockSpec(memory_space=pltpu.VMEM),
            pl.BlockSpec(memory_space=pl.ANY),
        ],
        out_specs=pl.BlockSpec(memory_space=pltpu.VMEM),
        scratch_shapes=[
            pltpu.VMEM((req_dev, width, pages_req * page_size), jnp.bfloat16),
            pltpu.SemaphoreType.DMA((req_dev * pages_req,)),
        ],
        compiler_params=pltpu.CompilerParams(vmem_limit_bytes=48 * 1024 * 1024),
    )(page_table, lengths, query_columns, cache_columns)


def resident_matmul(rows, weights):
    def kernel(rows_ref, weights_ref, out_ref):
        out_ref[...] = jnp.dot(rows_ref[...], weights_ref[...], preferred_element_type=jnp.float32)

    return pl.pallas_call(
        kernel,
        out_shape=jax.ShapeDtypeStruct((rows.shape[0], weights.shape[1]), jnp.float32),
        in_specs=[pl.BlockSpec(memory_space=pltpu.VMEM)] * 2,
        out_specs=pl.BlockSpec(memory_space=pltpu.VMEM),
        compiler_params=pltpu.CompilerParams(vmem_limit_bytes=40 * 1024 * 1024),
    )(rows, weights)


def swap_with(x, axis, distance, size):
    return lax.ppermute(x, axis, [(i, i ^ distance) for i in range(size)])


def halving_scatter(x, axis, size, dim=0):
    index = lax.axis_index(axis)
    x = x.astype(jnp.float32)
    distance = size // 2
    while distance >= 1:
        half = x.shape[dim] // 2
        low = lax.slice_in_dim(x, 0, half, axis=dim)
        high = lax.slice_in_dim(x, half, 2 * half, axis=dim)
        upper = (index & distance) != 0
        keep = jnp.where(upper, high, low)
        send = jnp.where(upper, low, high)
        x = keep + swap_with(send.astype(jnp.bfloat16), axis, distance, size).astype(jnp.float32)
        distance //= 2
    return x


def nearest_first_scatter(parts, axis, size):
    index = lax.axis_index(axis)
    parts = tuple(part.astype(jnp.float32) for part in parts)
    distance = 1
    while distance < size:
        half = parts[0].shape[1] // 2
        upper = (index & distance) != 0
        keeps = tuple(jnp.where(upper, part[:, half:], part[:, :half]) for part in parts)
        sends = tuple(
            jnp.where(upper, part[:, :half], part[:, half:]).astype(jnp.bfloat16) for part in parts
        )
        got = swap_with(sends, axis, distance, size)
        parts = tuple(keep + more.astype(jnp.float32) for keep, more in zip(keeps, got))
        distance *= 2
    return parts


def farthest_first_gather(x, axis, size, dim):
    index = lax.axis_index(axis)
    distance = size // 2
    while distance >= 1:
        got = swap_with(x, axis, distance, size)
        upper = (index & distance) != 0
        x = jnp.where(
            upper, jnp.concatenate([got, x], axis=dim), jnp.concatenate([x, got], axis=dim)
        )
        distance //= 2
    return x


def doubling_gather(x, axis, size, dim):
    index = lax.axis_index(axis)
    distance = 1
    while distance < size:
        got = swap_with(x, axis, distance, size)
        upper = (index & distance) != 0
        x = jnp.where(
            upper, jnp.concatenate([got, x], axis=dim), jnp.concatenate([x, got], axis=dim)
        )
        distance *= 2
    return x


def doubling_sum(x, axis, size):
    distance = 1
    while distance < size:
        x = x + swap_with(x, axis, distance, size)
        distance *= 2
    return x


def nearest_first_rows_scatter(x, axis, size):
    index = lax.axis_index(axis)
    x = x.astype(jnp.float32)
    x = x.reshape((size, x.shape[0] // size) + x.shape[1:])
    distance = 1
    while distance < size:
        pairs = x.reshape((x.shape[0] // 2, 2) + x.shape[1:])
        upper = (index & distance) != 0
        keep = jnp.where(upper, pairs[:, 1], pairs[:, 0])
        send = jnp.where(upper, pairs[:, 0], pairs[:, 1])
        x = keep + swap_with(send.astype(jnp.bfloat16), axis, distance, size).astype(jnp.float32)
        distance *= 2
    return x[0]


def farthest_first_rows_gather(x, axis, size):
    index = lax.axis_index(axis)
    x = x[None]
    distance = size // 2
    while distance >= 1:
        got = swap_with(x, axis, distance, size)
        upper = (index & distance) != 0
        x = jnp.where(upper, jnp.stack([got, x], axis=1), jnp.stack([x, got], axis=1))
        x = x.reshape((-1,) + x.shape[2:])
        distance //= 2
    return x.reshape((-1,) + x.shape[2:])


def matched_sum(x, axis, size):
    x = x.astype(jnp.float32)
    distance = 1
    while distance < size:
        mine = x.astype(jnp.bfloat16)
        x = mine.astype(jnp.float32) + swap_with(mine, axis, distance, size).astype(jnp.float32)
        distance *= 2
    return x


def shards(
    axis_sizes,
    hidden_in,
    queries,
    cache_pool,
    page_table,
    lengths,
    value_up,
    out_proj,
    norm_gain,
    gate_proj,
    up_proj,
    down_proj,
):
    req_dev = queries.shape[0]
    latent = value_up.shape[1]
    value_dim = value_up.shape[2]
    heads_here = value_up.shape[0]
    pages_req = page_table.shape[1]
    score_scale = float(VDIM + ROPE) ** (-0.5)
    units_here = gate_proj.shape[1]
    contexts = attend_all(queries, page_table, lengths, cache_pool, latent, score_scale)
    received = lax.all_to_all(
        contexts[None], ("dp", "sub"), split_axis=2, concat_axis=0, tiled=True
    )
    received = received.reshape(-1, heads_here, latent)
    row_count = received.shape[0]
    values = jnp.einsum("rhc,hcv->rhv", received, value_up, preferred_element_type=jnp.float32)
    values = values.astype(jnp.bfloat16).reshape(row_count, heads_here * value_dim)
    group_values = lax.all_gather(values, "sub", axis=1, tiled=True)
    dp_size = axis_sizes["dp"]
    sub_size = axis_sizes["sub"]
    attention_all = matched_sum(resident_matmul(group_values, out_proj), "dp", dp_size)
    hidden_all = farthest_first_rows_gather(hidden_in, "dp", dp_size)
    all_residual = hidden_all.astype(jnp.float32) + attention_all
    squares = doubling_sum(jnp.sum(all_residual * all_residual, axis=1), "sub", sub_size)
    gained = (all_residual * norm_gain.astype(jnp.float32)).astype(jnp.bfloat16)
    gate_part = jnp.dot(gained, gate_proj, preferred_element_type=jnp.float32)
    up_part = jnp.dot(gained, up_proj, preferred_element_type=jnp.float32)
    gate_sum, up_sum = nearest_first_scatter((gate_part, up_part), "sub", sub_size)
    scale_rows = lax.rsqrt(squares / float(D) + 1e-06)[:, None]
    hidden_chunk = (jax.nn.silu(gate_sum * scale_rows) * (up_sum * scale_rows)).astype(jnp.bfloat16)
    hidden_units = farthest_first_gather(hidden_chunk, "sub", sub_size, 1)
    feed_forward = nearest_first_rows_scatter(
        jnp.dot(hidden_units, down_proj, preferred_element_type=jnp.float32), "dp", axis_sizes["dp"]
    )
    own_rows = hidden_in.shape[0]
    first_row = lax.axis_index("dp") * own_rows
    attention = lax.dynamic_slice_in_dim(attention_all, first_row, own_rows, 0)
    residual = lax.dynamic_slice_in_dim(all_residual, first_row, own_rows, 0)
    return (attention.astype(jnp.bfloat16), (residual + feed_forward).astype(jnp.bfloat16))


def solution(mesh):
    placed = (
        P(("grp", "dp"), "sub"),
        P(("grp", "dp", "sub"), None, None),
        P(("grp", "dp", "sub"), None, None),
        P(("grp", "dp", "sub"), None),
        P(("grp", "dp", "sub")),
        P(("dp", "sub"), None, None),
        P("dp", "sub"),
        P("sub"),
        P("sub", "dp"),
        P("sub", "dp"),
        P("dp", "sub"),
    )
    return jax.shard_map(
        functools.partial(shards, dict(mesh.shape)),
        mesh=mesh,
        in_specs=placed,
        out_specs=(P(("grp", "dp"), "sub"), P(("grp", "dp"), "sub")),
        check_vma=False,
    )
```

```python
import functools

import jax
import jax.numpy as jnp
from jax import lax
from jax.experimental import pallas as pl
from jax.experimental.pallas import tpu as pltpu
from jax.sharding import PartitionSpec as P

D = 5120
ROPE = 64
VDIM = 128


masked_score = -1e30


def attend_kernel(page_table, lengths, queries, cache_pool, contexts, keys, copy_sems,
                  *, latent, score_scale):
    req_dev, pages_req = page_table.shape
    page_size = cache_pool.shape[2]
    head_count = queries.shape[2]

    def page_copy(slot, page):
        return pltpu.make_async_copy(
            cache_pool.at[page_table[slot, page]],
            keys.at[slot, :, pl.ds(pl.multiple_of(page * page_size, page_size), page_size)],
            copy_sems.at[slot * pages_req + page],
        )

    for slot in range(req_dev):
        def start(page, carry, slot=slot):
            page_copy(slot, page).start()
            return carry

        lax.fori_loop(0, pages_req, start, 0)

    span = pages_req * page_size
    positions = lax.broadcasted_iota(jnp.int32, (head_count, span), 1)
    for slot in range(req_dev):
        def finish(page, carry, slot=slot):
            page_copy(slot, page).wait()
            return carry

        lax.fori_loop(0, pages_req, finish, 0)
        live = positions < lengths[slot]
        query_rows = jnp.transpose(queries[slot])
        scores = jnp.dot(query_rows, keys[slot], preferred_element_type=jnp.float32) * score_scale
        scores = jnp.where(live, scores, masked_score)
        row_max = jnp.max(scores, axis=1, keepdims=True)
        exponent = jnp.exp(scores - row_max)
        denominator = jnp.sum(exponent, axis=1, keepdims=True)
        weighted = lax.dot_general(
            exponent.astype(jnp.bfloat16),
            keys[slot, :latent, :],
            (((1,), (1,)), ((), ())),
            preferred_element_type=jnp.float32,
        )
        contexts[slot] = (weighted / denominator).astype(contexts.dtype)


def attend_all(queries, page_table, lengths, cache_pool, latent, score_scale):
    req_dev, head_count, width = queries.shape
    pages_req = page_table.shape[1]
    query_columns = jnp.swapaxes(queries, 1, 2)
    page_size = cache_pool.shape[1]
    cache_columns = jnp.swapaxes(cache_pool, 1, 2)
    kernel = functools.partial(attend_kernel, latent=latent, score_scale=score_scale)
    return pl.pallas_call(
        kernel,
        out_shape=jax.ShapeDtypeStruct((req_dev, head_count, latent), jnp.bfloat16),
        in_specs=[
            pl.BlockSpec(memory_space=pltpu.SMEM),
            pl.BlockSpec(memory_space=pltpu.SMEM),
            pl.BlockSpec(memory_space=pltpu.VMEM),
            pl.BlockSpec(memory_space=pltpu.HBM),
        ],
        out_specs=pl.BlockSpec(memory_space=pltpu.VMEM),
        scratch_shapes=[
            pltpu.VMEM((req_dev, width, pages_req * page_size), jnp.bfloat16),
            pltpu.SemaphoreType.DMA((req_dev * pages_req,)),
        ],
        compiler_params=pltpu.CompilerParams(vmem_limit_bytes=20 * 1024 * 1024),
    )(page_table, lengths, query_columns, cache_columns)


def swap_with(x, axis, distance, size):
    return lax.ppermute(x, axis, [(i, i ^ distance) for i in range(size)])


def halving_scatter(x, axis, size, dim=0):
    index = lax.axis_index(axis)
    x = x.astype(jnp.float32)
    distance = size // 2
    while distance >= 1:
        half = x.shape[dim] // 2
        low = lax.slice_in_dim(x, 0, half, axis=dim)
        high = lax.slice_in_dim(x, half, 2 * half, axis=dim)
        upper = (index & distance) != 0
        keep = jnp.where(upper, high, low)
        send = jnp.where(upper, low, high)
        x = keep + swap_with(send.astype(jnp.bfloat16), axis, distance, size).astype(jnp.float32)
        distance //= 2
    return x


def nearest_first_scatter(parts, axis, size):
    index = lax.axis_index(axis)
    parts = tuple(part.astype(jnp.float32) for part in parts)
    distance = 1
    while distance < size:
        half = parts[0].shape[1] // 2
        upper = (index & distance) != 0
        keeps = tuple(jnp.where(upper, part[:, half:], part[:, :half]) for part in parts)
        sends = tuple(
            jnp.where(upper, part[:, :half], part[:, half:]).astype(jnp.bfloat16) for part in parts
        )
        got = swap_with(sends, axis, distance, size)
        parts = tuple(keep + more.astype(jnp.float32) for keep, more in zip(keeps, got))
        distance *= 2
    return parts


def farthest_first_gather(x, axis, size, dim):
    index = lax.axis_index(axis)
    distance = size // 2
    while distance >= 1:
        got = swap_with(x, axis, distance, size)
        upper = (index & distance) != 0
        x = jnp.where(
            upper, jnp.concatenate([got, x], axis=dim), jnp.concatenate([x, got], axis=dim)
        )
        distance //= 2
    return x


def doubling_gather(x, axis, size, dim):
    index = lax.axis_index(axis)
    distance = 1
    while distance < size:
        got = swap_with(x, axis, distance, size)
        upper = (index & distance) != 0
        x = jnp.where(
            upper, jnp.concatenate([got, x], axis=dim), jnp.concatenate([x, got], axis=dim)
        )
        distance *= 2
    return x


def doubling_sum(x, axis, size):
    distance = 1
    while distance < size:
        x = x + swap_with(x, axis, distance, size)
        distance *= 2
    return x


def nearest_first_rows_scatter(x, axis, size):
    index = lax.axis_index(axis)
    x = x.astype(jnp.float32)
    x = x.reshape((size, x.shape[0] // size) + x.shape[1:])
    distance = 1
    while distance < size:
        pairs = x.reshape((x.shape[0] // 2, 2) + x.shape[1:])
        upper = (index & distance) != 0
        keep = jnp.where(upper, pairs[:, 1], pairs[:, 0])
        send = jnp.where(upper, pairs[:, 0], pairs[:, 1])
        x = keep + swap_with(send.astype(jnp.bfloat16), axis, distance, size).astype(jnp.float32)
        distance *= 2
    return x[0]


def farthest_first_rows_gather(x, axis, size):
    index = lax.axis_index(axis)
    x = x[None]
    distance = size // 2
    while distance >= 1:
        got = swap_with(x, axis, distance, size)
        upper = (index & distance) != 0
        x = jnp.where(upper, jnp.stack([got, x], axis=1), jnp.stack([x, got], axis=1))
        x = x.reshape((-1,) + x.shape[2:])
        distance //= 2
    return x.reshape((-1,) + x.shape[2:])


def matched_sum(x, axis, size):
    x = x.astype(jnp.float32)
    distance = 1
    while distance < size:
        mine = x.astype(jnp.bfloat16)
        x = mine.astype(jnp.float32) + swap_with(mine, axis, distance, size).astype(jnp.float32)
        distance *= 2
    return x


def shards(
    axis_sizes,
    hidden_in,
    queries,
    cache_pool,
    page_table,
    lengths,
    value_up,
    out_proj,
    norm_gain,
    gate_proj,
    up_proj,
    down_proj,
):
    req_dev = queries.shape[0]
    latent = value_up.shape[1]
    value_dim = value_up.shape[2]
    heads_here = value_up.shape[0]
    pages_req = page_table.shape[1]
    score_scale = float(VDIM + ROPE) ** (-0.5)
    units_here = gate_proj.shape[1]
    contexts = attend_all(queries, page_table, lengths, cache_pool, latent, score_scale)
    received = lax.all_to_all(
        contexts[None], ("dp", "sub"), split_axis=2, concat_axis=0, tiled=True
    )
    received = received.reshape(-1, heads_here, latent)
    row_count = received.shape[0]
    values = jnp.einsum("rhc,hcv->rhv", received, value_up, preferred_element_type=jnp.float32)
    values = values.astype(jnp.bfloat16).reshape(row_count, heads_here * value_dim)
    group_values = lax.all_gather(values, "sub", axis=1, tiled=True)
    dp_size = axis_sizes["dp"]
    sub_size = axis_sizes["sub"]
    attention_all = matched_sum(
        jnp.dot(group_values, out_proj, preferred_element_type=jnp.float32), "dp", dp_size
    )
    hidden_all = farthest_first_rows_gather(hidden_in, "dp", dp_size)
    all_residual = hidden_all.astype(jnp.float32) + attention_all
    squares = doubling_sum(jnp.sum(all_residual * all_residual, axis=1), "sub", sub_size)
    gained = (all_residual * norm_gain.astype(jnp.float32)).astype(jnp.bfloat16)
    gate_part = jnp.dot(gained, gate_proj, preferred_element_type=jnp.float32)
    up_part = jnp.dot(gained, up_proj, preferred_element_type=jnp.float32)
    gate_sum, up_sum = nearest_first_scatter((gate_part, up_part), "sub", sub_size)
    scale_rows = lax.rsqrt(squares / float(D) + 1e-06)[:, None]
    hidden_chunk = (jax.nn.silu(gate_sum * scale_rows) * (up_sum * scale_rows)).astype(jnp.bfloat16)
    hidden_units = farthest_first_gather(hidden_chunk, "sub", sub_size, 1)
    feed_forward = nearest_first_rows_scatter(
        jnp.dot(hidden_units, down_proj, preferred_element_type=jnp.float32), "dp", axis_sizes["dp"]
    )
    own_rows = hidden_in.shape[0]
    first_row = lax.axis_index("dp") * own_rows
    attention = lax.dynamic_slice_in_dim(attention_all, first_row, own_rows, 0)
    residual = lax.dynamic_slice_in_dim(all_residual, first_row, own_rows, 0)
    return (attention.astype(jnp.bfloat16), (residual + feed_forward).astype(jnp.bfloat16))


def solution(mesh):
    placed = (
        P(("grp", "dp"), "sub"),
        P(("grp", "dp", "sub"), None, None),
        P(("grp", "dp", "sub"), None, None),
        P(("grp", "dp", "sub"), None),
        P(("grp", "dp", "sub")),
        P(("dp", "sub"), None, None),
        P("dp", "sub"),
        P("sub"),
        P("sub", "dp"),
        P("sub", "dp"),
        P("dp", "sub"),
    )
    return jax.shard_map(
        functools.partial(shards, dict(mesh.shape)),
        mesh=mesh,
        in_specs=placed,
        out_specs=(P(("grp", "dp"), "sub"), P(("grp", "dp"), "sub")),
        check_vma=False,
    )
```

```python
import functools

import jax
import jax.numpy as jnp
from jax import lax
from jax.experimental import pallas as pl
from jax.experimental.pallas import tpu as pltpu
from jax.sharding import PartitionSpec as P

D = 5120
ROPE = 64
VDIM = 128


masked_score = -1e30


def attend_kernel(page_table, lengths, queries, cache_pool, contexts, keys, copy_sems,
                  *, latent, score_scale):
    req_dev, pages_req = page_table.shape
    page_size = cache_pool.shape[2]
    head_count = queries.shape[2]

    def page_copy(slot, page):
        return pltpu.make_async_copy(
            cache_pool.at[page_table[slot, page]],
            keys.at[slot, :, pl.ds(pl.multiple_of(page * page_size, page_size), page_size)],
            copy_sems.at[slot * pages_req + page],
        )

    for slot in range(req_dev):
        def start(page, carry, slot=slot):
            page_copy(slot, page).start()
            return carry

        lax.fori_loop(0, pages_req, start, 0)

    span = pages_req * page_size
    positions = lax.broadcasted_iota(jnp.int32, (head_count, span), 1)
    for slot in range(req_dev):
        def finish(page, carry, slot=slot):
            page_copy(slot, page).wait()
            return carry

        lax.fori_loop(0, pages_req, finish, 0)
        live = positions < lengths[slot]
        query_rows = jnp.transpose(queries[slot])
        scores = jnp.dot(query_rows, keys[slot], preferred_element_type=jnp.float32) * score_scale
        scores = jnp.where(live, scores, masked_score)
        row_max = jnp.max(scores, axis=1, keepdims=True)
        exponent = jnp.exp(scores - row_max)
        denominator = jnp.sum(exponent, axis=1, keepdims=True)
        weighted = lax.dot_general(
            exponent.astype(jnp.bfloat16),
            keys[slot, :latent, :],
            (((1,), (1,)), ((), ())),
            preferred_element_type=jnp.float32,
        )
        blocks, block_heads = contexts.shape[0], head_count // contexts.shape[0]
        context = (weighted / denominator).reshape(blocks, block_heads, latent)
        contexts[:, slot * block_heads:(slot + 1) * block_heads, :] = context.astype(contexts.dtype)


def attend_all(queries, page_table, lengths, cache_pool, latent, score_scale, blocks):
    req_dev, head_count, width = queries.shape
    pages_req = page_table.shape[1]
    query_columns = jnp.swapaxes(queries, 1, 2)
    page_size = cache_pool.shape[1]
    cache_columns = jnp.swapaxes(cache_pool, 1, 2)
    kernel = functools.partial(attend_kernel, latent=latent, score_scale=score_scale)
    return pl.pallas_call(
        kernel,
        out_shape=jax.ShapeDtypeStruct((blocks, req_dev * (head_count // blocks), latent), jnp.bfloat16),
        in_specs=[
            pl.BlockSpec(memory_space=pltpu.SMEM),
            pl.BlockSpec(memory_space=pltpu.SMEM),
            pl.BlockSpec(memory_space=pltpu.VMEM),
            pl.BlockSpec(memory_space=pl.ANY),
        ],
        out_specs=pl.BlockSpec(memory_space=pltpu.VMEM),
        scratch_shapes=[
            pltpu.VMEM((req_dev, width, pages_req * page_size), jnp.bfloat16),
            pltpu.SemaphoreType.DMA((req_dev * pages_req,)),
        ],
        compiler_params=pltpu.CompilerParams(vmem_limit_bytes=48 * 1024 * 1024),
    )(page_table, lengths, query_columns, cache_columns)


def swap_with(x, axis, distance, size):
    return lax.ppermute(x, axis, [(i, i ^ distance) for i in range(size)])


def halving_scatter(x, axis, size, dim=0):
    index = lax.axis_index(axis)
    x = x.astype(jnp.float32)
    distance = size // 2
    while distance >= 1:
        half = x.shape[dim] // 2
        low = lax.slice_in_dim(x, 0, half, axis=dim)
        high = lax.slice_in_dim(x, half, 2 * half, axis=dim)
        upper = (index & distance) != 0
        keep = jnp.where(upper, high, low)
        send = jnp.where(upper, low, high)
        x = keep + swap_with(send.astype(jnp.bfloat16), axis, distance, size).astype(jnp.float32)
        distance //= 2
    return x


def nearest_first_scatter(parts, axis, size):
    index = lax.axis_index(axis)
    parts = tuple(part.astype(jnp.float32) for part in parts)
    distance = 1
    while distance < size:
        half = parts[0].shape[1] // 2
        upper = (index & distance) != 0
        keeps = tuple(jnp.where(upper, part[:, half:], part[:, :half]) for part in parts)
        sends = tuple(
            jnp.where(upper, part[:, :half], part[:, half:]).astype(jnp.bfloat16) for part in parts
        )
        got = swap_with(sends, axis, distance, size)
        parts = tuple(keep + more.astype(jnp.float32) for keep, more in zip(keeps, got))
        distance *= 2
    return parts


def farthest_first_gather(x, axis, size, dim):
    index = lax.axis_index(axis)
    distance = size // 2
    while distance >= 1:
        got = swap_with(x, axis, distance, size)
        upper = (index & distance) != 0
        x = jnp.where(
            upper, jnp.concatenate([got, x], axis=dim), jnp.concatenate([x, got], axis=dim)
        )
        distance //= 2
    return x


def doubling_gather(x, axis, size, dim):
    index = lax.axis_index(axis)
    distance = 1
    while distance < size:
        got = swap_with(x, axis, distance, size)
        upper = (index & distance) != 0
        x = jnp.where(
            upper, jnp.concatenate([got, x], axis=dim), jnp.concatenate([x, got], axis=dim)
        )
        distance *= 2
    return x


def doubling_sum(x, axis, size):
    distance = 1
    while distance < size:
        x = x + swap_with(x, axis, distance, size)
        distance *= 2
    return x


def nearest_first_rows_scatter(x, axis, size):
    index = lax.axis_index(axis)
    x = x.astype(jnp.float32)
    x = x.reshape((size, x.shape[0] // size) + x.shape[1:])
    distance = 1
    while distance < size:
        pairs = x.reshape((x.shape[0] // 2, 2) + x.shape[1:])
        upper = (index & distance) != 0
        keep = jnp.where(upper, pairs[:, 1], pairs[:, 0])
        send = jnp.where(upper, pairs[:, 0], pairs[:, 1])
        x = keep + swap_with(send.astype(jnp.bfloat16), axis, distance, size).astype(jnp.float32)
        distance *= 2
    return x[0]


def farthest_first_rows_gather(x, axis, size):
    index = lax.axis_index(axis)
    x = x[None]
    distance = size // 2
    while distance >= 1:
        got = swap_with(x, axis, distance, size)
        upper = (index & distance) != 0
        x = jnp.where(upper, jnp.stack([got, x], axis=1), jnp.stack([x, got], axis=1))
        x = x.reshape((-1,) + x.shape[2:])
        distance //= 2
    return x.reshape((-1,) + x.shape[2:])


def matched_sum(x, axis, size):
    x = x.astype(jnp.float32)
    distance = 1
    while distance < size:
        mine = x.astype(jnp.bfloat16)
        x = mine.astype(jnp.float32) + swap_with(mine, axis, distance, size).astype(jnp.float32)
        distance *= 2
    return x


def shards(
    axis_sizes,
    hidden_in,
    queries,
    cache_pool,
    page_table,
    lengths,
    value_up,
    out_proj,
    norm_gain,
    gate_proj,
    up_proj,
    down_proj,
):
    req_dev = queries.shape[0]
    latent = value_up.shape[1]
    value_dim = value_up.shape[2]
    heads_here = value_up.shape[0]
    pages_req = page_table.shape[1]
    score_scale = float(VDIM + ROPE) ** (-0.5)
    units_here = gate_proj.shape[1]
    blocks = axis_sizes["dp"] * axis_sizes["sub"]
    contexts = attend_all(queries, page_table, lengths, cache_pool, latent, score_scale, blocks)
    received = lax.all_to_all(contexts, ("dp", "sub"), split_axis=0, concat_axis=0, tiled=True)
    received = received.reshape(-1, heads_here, latent)
    row_count = received.shape[0]
    values = jnp.einsum("rhc,hcv->rhv", received, value_up, preferred_element_type=jnp.float32)
    values = values.astype(jnp.bfloat16).reshape(row_count, heads_here * value_dim)
    group_values = lax.all_gather(values, "sub", axis=1, tiled=True)
    dp_size = axis_sizes["dp"]
    sub_size = axis_sizes["sub"]
    attention_all = matched_sum(
        jnp.dot(group_values, out_proj, preferred_element_type=jnp.float32), "dp", dp_size
    )
    hidden_all = farthest_first_rows_gather(hidden_in, "dp", dp_size)
    all_residual = hidden_all.astype(jnp.float32) + attention_all
    squares = doubling_sum(jnp.sum(all_residual * all_residual, axis=1), "sub", sub_size)
    gained = (all_residual * norm_gain.astype(jnp.float32)).astype(jnp.bfloat16)
    gate_part = jnp.dot(gained, gate_proj, preferred_element_type=jnp.float32)
    up_part = jnp.dot(gained, up_proj, preferred_element_type=jnp.float32)
    gate_sum, up_sum = nearest_first_scatter((gate_part, up_part), "sub", sub_size)
    scale_rows = lax.rsqrt(squares / float(D) + 1e-06)[:, None]
    hidden_chunk = (jax.nn.silu(gate_sum * scale_rows) * (up_sum * scale_rows)).astype(jnp.bfloat16)
    hidden_units = farthest_first_gather(hidden_chunk, "sub", sub_size, 1)
    feed_forward = nearest_first_rows_scatter(
        jnp.dot(hidden_units, down_proj, preferred_element_type=jnp.float32), "dp", axis_sizes["dp"]
    )
    own_rows = hidden_in.shape[0]
    first_row = lax.axis_index("dp") * own_rows
    attention = lax.dynamic_slice_in_dim(attention_all, first_row, own_rows, 0)
    residual = lax.dynamic_slice_in_dim(all_residual, first_row, own_rows, 0)
    return (attention.astype(jnp.bfloat16), (residual + feed_forward).astype(jnp.bfloat16))


def solution(mesh):
    placed = (
        P(("grp", "dp"), "sub"),
        P(("grp", "dp", "sub"), None, None),
        P(("grp", "dp", "sub"), None, None),
        P(("grp", "dp", "sub"), None),
        P(("grp", "dp", "sub")),
        P(("dp", "sub"), None, None),
        P("dp", "sub"),
        P("sub"),
        P("sub", "dp"),
        P("sub", "dp"),
        P("dp", "sub"),
    )
    return jax.shard_map(
        functools.partial(shards, dict(mesh.shape)),
        mesh=mesh,
        in_specs=placed,
        out_specs=(P(("grp", "dp"), "sub"), P(("grp", "dp"), "sub")),
        check_vma=False,
    )
```

```python
import functools

import jax
import jax.numpy as jnp
from jax import lax
from jax.experimental import pallas as pl
from jax.experimental.pallas import tpu as pltpu
from jax.sharding import PartitionSpec as P

D = 5120
ROPE = 64
VDIM = 128


masked_score = -1e30


def attend_kernel(page_table, lengths, queries, cache_pool, contexts, keys, copy_sems,
                  *, latent, score_scale):
    req_dev, pages_req = page_table.shape
    page_size = cache_pool.shape[2]
    head_count = queries.shape[2]

    def page_copy(slot, page):
        return pltpu.make_async_copy(
            cache_pool.at[page_table[slot, page]],
            keys.at[slot, :, pl.ds(pl.multiple_of(page * page_size, page_size), page_size)],
            copy_sems.at[slot * pages_req + page],
        )

    for slot in range(req_dev):
        def start(page, carry, slot=slot):
            page_copy(slot, page).start()
            return carry

        lax.fori_loop(0, pages_req, start, 0)

    span = pages_req * page_size
    positions = lax.broadcasted_iota(jnp.int32, (head_count, span), 1)
    for slot in range(req_dev):
        def finish(page, carry, slot=slot):
            page_copy(slot, page).wait()
            return carry

        lax.fori_loop(0, pages_req, finish, 0)
        live = positions < lengths[slot]
        query_rows = jnp.transpose(queries[slot])
        scores = jnp.dot(query_rows, keys[slot], preferred_element_type=jnp.float32) * score_scale
        scores = jnp.where(live, scores, masked_score)
        row_max = jnp.max(scores, axis=1, keepdims=True)
        exponent = jnp.exp(scores - row_max)
        denominator = jnp.sum(exponent, axis=1, keepdims=True)
        weighted = lax.dot_general(
            exponent.astype(jnp.bfloat16),
            keys[slot, :latent, :],
            (((1,), (1,)), ((), ())),
            preferred_element_type=jnp.float32,
        )
        blocks, block_heads = contexts.shape[0], head_count // contexts.shape[0]
        context = (weighted / denominator).reshape(blocks, block_heads, latent)
        contexts[:, slot * block_heads:(slot + 1) * block_heads, :] = context.astype(contexts.dtype)


def attend_all(queries, page_table, lengths, cache_pool, latent, score_scale, blocks):
    req_dev, head_count, width = queries.shape
    pages_req = page_table.shape[1]
    query_columns = jnp.swapaxes(queries, 1, 2)
    page_size = cache_pool.shape[1]
    cache_columns = jnp.swapaxes(cache_pool, 1, 2)
    kernel = functools.partial(attend_kernel, latent=latent, score_scale=score_scale)
    return pl.pallas_call(
        kernel,
        out_shape=jax.ShapeDtypeStruct((blocks, req_dev * (head_count // blocks), latent), jnp.bfloat16),
        in_specs=[
            pl.BlockSpec(memory_space=pltpu.SMEM),
            pl.BlockSpec(memory_space=pltpu.SMEM),
            pl.BlockSpec(memory_space=pltpu.VMEM),
            pl.BlockSpec(memory_space=pl.ANY),
        ],
        out_specs=pl.BlockSpec(memory_space=pltpu.VMEM),
        scratch_shapes=[
            pltpu.VMEM((req_dev, width, pages_req * page_size), jnp.bfloat16),
            pltpu.SemaphoreType.DMA((req_dev * pages_req,)),
        ],
        compiler_params=pltpu.CompilerParams(vmem_limit_bytes=48 * 1024 * 1024),
    )(page_table, lengths, query_columns, cache_columns)


def streamed_matmul(rows, weights):
    row_count, depth = rows.shape
    width = weights.shape[1]
    block = next(size for size in (1024, 512, 256, 128, depth) if depth % size == 0)

    def kernel(rows_ref, weights_ref, out_ref):
        @pl.when(pl.program_id(0) == 0)
        def _():
            out_ref[...] = jnp.zeros_like(out_ref)

        out_ref[...] += jnp.dot(rows_ref[...], weights_ref[...], preferred_element_type=jnp.float32)

    return pl.pallas_call(
        kernel,
        out_shape=jax.ShapeDtypeStruct((row_count, width), jnp.float32),
        grid=(depth // block,),
        in_specs=[
            pl.BlockSpec((row_count, block), lambda step: (0, step)),
            pl.BlockSpec((block, width), lambda step: (step, 0)),
        ],
        out_specs=pl.BlockSpec((row_count, width), lambda step: (0, 0)),
        compiler_params=pltpu.CompilerParams(dimension_semantics=("arbitrary",)),
    )(rows, weights)


def swap_with(x, axis, distance, size):
    return lax.ppermute(x, axis, [(i, i ^ distance) for i in range(size)])


def halving_scatter(x, axis, size, dim=0):
    index = lax.axis_index(axis)
    x = x.astype(jnp.float32)
    distance = size // 2
    while distance >= 1:
        half = x.shape[dim] // 2
        low = lax.slice_in_dim(x, 0, half, axis=dim)
        high = lax.slice_in_dim(x, half, 2 * half, axis=dim)
        upper = (index & distance) != 0
        keep = jnp.where(upper, high, low)
        send = jnp.where(upper, low, high)
        x = keep + swap_with(send.astype(jnp.bfloat16), axis, distance, size).astype(jnp.float32)
        distance //= 2
    return x


def nearest_first_scatter(parts, axis, size):
    index = lax.axis_index(axis)
    parts = tuple(part.astype(jnp.float32) for part in parts)
    distance = 1
    while distance < size:
        half = parts[0].shape[1] // 2
        upper = (index & distance) != 0
        keeps = tuple(jnp.where(upper, part[:, half:], part[:, :half]) for part in parts)
        sends = tuple(
            jnp.where(upper, part[:, :half], part[:, half:]).astype(jnp.bfloat16) for part in parts
        )
        got = swap_with(sends, axis, distance, size)
        parts = tuple(keep + more.astype(jnp.float32) for keep, more in zip(keeps, got))
        distance *= 2
    return parts


def farthest_first_gather(x, axis, size, dim):
    index = lax.axis_index(axis)
    distance = size // 2
    while distance >= 1:
        got = swap_with(x, axis, distance, size)
        upper = (index & distance) != 0
        x = jnp.where(
            upper, jnp.concatenate([got, x], axis=dim), jnp.concatenate([x, got], axis=dim)
        )
        distance //= 2
    return x


def doubling_gather(x, axis, size, dim):
    index = lax.axis_index(axis)
    distance = 1
    while distance < size:
        got = swap_with(x, axis, distance, size)
        upper = (index & distance) != 0
        x = jnp.where(
            upper, jnp.concatenate([got, x], axis=dim), jnp.concatenate([x, got], axis=dim)
        )
        distance *= 2
    return x


def doubling_sum(x, axis, size):
    distance = 1
    while distance < size:
        x = x + swap_with(x, axis, distance, size)
        distance *= 2
    return x


def nearest_first_rows_scatter(x, axis, size):
    index = lax.axis_index(axis)
    x = x.astype(jnp.float32)
    x = x.reshape((size, x.shape[0] // size) + x.shape[1:])
    distance = 1
    while distance < size:
        pairs = x.reshape((x.shape[0] // 2, 2) + x.shape[1:])
        upper = (index & distance) != 0
        keep = jnp.where(upper, pairs[:, 1], pairs[:, 0])
        send = jnp.where(upper, pairs[:, 0], pairs[:, 1])
        x = keep + swap_with(send.astype(jnp.bfloat16), axis, distance, size).astype(jnp.float32)
        distance *= 2
    return x[0]


def farthest_first_rows_gather(x, axis, size):
    index = lax.axis_index(axis)
    x = x[None]
    distance = size // 2
    while distance >= 1:
        got = swap_with(x, axis, distance, size)
        upper = (index & distance) != 0
        x = jnp.where(upper, jnp.stack([got, x], axis=1), jnp.stack([x, got], axis=1))
        x = x.reshape((-1,) + x.shape[2:])
        distance //= 2
    return x.reshape((-1,) + x.shape[2:])


def matched_sum(x, axis, size):
    x = x.astype(jnp.float32)
    distance = 1
    while distance < size:
        mine = x.astype(jnp.bfloat16)
        x = mine.astype(jnp.float32) + swap_with(mine, axis, distance, size).astype(jnp.float32)
        distance *= 2
    return x


def shards(
    axis_sizes,
    hidden_in,
    queries,
    cache_pool,
    page_table,
    lengths,
    value_up,
    out_proj,
    norm_gain,
    gate_proj,
    up_proj,
    down_proj,
):
    req_dev = queries.shape[0]
    latent = value_up.shape[1]
    value_dim = value_up.shape[2]
    heads_here = value_up.shape[0]
    pages_req = page_table.shape[1]
    score_scale = float(VDIM + ROPE) ** (-0.5)
    units_here = gate_proj.shape[1]
    blocks = axis_sizes["dp"] * axis_sizes["sub"]
    contexts = attend_all(queries, page_table, lengths, cache_pool, latent, score_scale, blocks)
    received = lax.all_to_all(contexts, ("dp", "sub"), split_axis=0, concat_axis=0, tiled=True)
    received = received.reshape(-1, heads_here, latent)
    row_count = received.shape[0]
    values = jnp.einsum("rhc,hcv->rhv", received, value_up, preferred_element_type=jnp.float32)
    values = values.astype(jnp.bfloat16).reshape(row_count, heads_here * value_dim)
    group_values = lax.all_gather(values, "sub", axis=1, tiled=True)
    dp_size = axis_sizes["dp"]
    sub_size = axis_sizes["sub"]
    attention_all = matched_sum(streamed_matmul(group_values, out_proj), "dp", dp_size)
    hidden_all = farthest_first_rows_gather(hidden_in, "dp", dp_size)
    all_residual = hidden_all.astype(jnp.float32) + attention_all
    squares = doubling_sum(jnp.sum(all_residual * all_residual, axis=1), "sub", sub_size)
    gained = (all_residual * norm_gain.astype(jnp.float32)).astype(jnp.bfloat16)
    gate_part = jnp.dot(gained, gate_proj, preferred_element_type=jnp.float32)
    up_part = jnp.dot(gained, up_proj, preferred_element_type=jnp.float32)
    gate_sum, up_sum = nearest_first_scatter((gate_part, up_part), "sub", sub_size)
    scale_rows = lax.rsqrt(squares / float(D) + 1e-06)[:, None]
    hidden_chunk = (jax.nn.silu(gate_sum * scale_rows) * (up_sum * scale_rows)).astype(jnp.bfloat16)
    hidden_units = farthest_first_gather(hidden_chunk, "sub", sub_size, 1)
    feed_forward = nearest_first_rows_scatter(
        streamed_matmul(hidden_units, down_proj), "dp", axis_sizes["dp"]
    )
    own_rows = hidden_in.shape[0]
    first_row = lax.axis_index("dp") * own_rows
    attention = lax.dynamic_slice_in_dim(attention_all, first_row, own_rows, 0)
    residual = lax.dynamic_slice_in_dim(all_residual, first_row, own_rows, 0)
    return (attention.astype(jnp.bfloat16), (residual + feed_forward).astype(jnp.bfloat16))


def solution(mesh):
    placed = (
        P(("grp", "dp"), "sub"),
        P(("grp", "dp", "sub"), None, None),
        P(("grp", "dp", "sub"), None, None),
        P(("grp", "dp", "sub"), None),
        P(("grp", "dp", "sub")),
        P(("dp", "sub"), None, None),
        P("dp", "sub"),
        P("sub"),
        P("sub", "dp"),
        P("sub", "dp"),
        P("dp", "sub"),
    )
    return jax.shard_map(
        functools.partial(shards, dict(mesh.shape)),
        mesh=mesh,
        in_specs=placed,
        out_specs=(P(("grp", "dp"), "sub"), P(("grp", "dp"), "sub")),
        check_vma=False,
    )
```

```python
import functools

import jax
import jax.numpy as jnp
from jax import lax
from jax.experimental import pallas as pl
from jax.experimental.pallas import tpu as pltpu
from jax.sharding import PartitionSpec as P

D = 5120
ROPE = 64
VDIM = 128


masked_score = -1e30


def attend_kernel(page_table, lengths, queries, cache_pool, contexts, keys, finished, copy_sems,
                  *, latent, score_scale):
    req_dev, pages_req = page_table.shape
    page_size = cache_pool.shape[2]
    head_count = queries.shape[2]

    def page_copy(slot, page):
        return pltpu.make_async_copy(
            cache_pool.at[page_table[slot, page]],
            keys.at[slot, :, pl.ds(pl.multiple_of(page * page_size, page_size), page_size)],
            copy_sems.at[slot * pages_req + page],
        )

    for slot in range(req_dev):
        def start(page, carry, slot=slot):
            page_copy(slot, page).start()
            return carry

        lax.fori_loop(0, pages_req, start, 0)

    span = pages_req * page_size
    positions = lax.broadcasted_iota(jnp.int32, (head_count, span), 1)
    for slot in range(req_dev):
        def finish(page, carry, slot=slot):
            page_copy(slot, page).wait()
            return carry

        lax.fori_loop(0, pages_req, finish, 0)
        live = positions < lengths[slot]
        query_rows = jnp.transpose(queries[slot])
        scores = jnp.dot(query_rows, keys[slot], preferred_element_type=jnp.float32) * score_scale
        scores = jnp.where(live, scores, masked_score)
        row_max = jnp.max(scores, axis=1, keepdims=True)
        exponent = jnp.exp(scores - row_max)
        denominator = jnp.sum(exponent, axis=1, keepdims=True)
        weighted = lax.dot_general(
            exponent.astype(jnp.bfloat16),
            keys[slot, :latent, :],
            (((1,), (1,)), ((), ())),
            preferred_element_type=jnp.float32,
        )
        finished[slot] = weighted / denominator
    blocks, block_heads = contexts.shape[0], head_count // contexts.shape[0]
    for block in range(blocks):
        rows = finished[:, block * block_heads:(block + 1) * block_heads, :]
        contexts[block] = rows.reshape(req_dev * block_heads, latent).astype(contexts.dtype)


def attend_all(queries, page_table, lengths, cache_pool, latent, score_scale, blocks):
    req_dev, head_count, width = queries.shape
    pages_req = page_table.shape[1]
    query_columns = jnp.swapaxes(queries, 1, 2)
    page_size = cache_pool.shape[1]
    cache_columns = jnp.swapaxes(cache_pool, 1, 2)
    kernel = functools.partial(attend_kernel, latent=latent, score_scale=score_scale)
    return pl.pallas_call(
        kernel,
        out_shape=jax.ShapeDtypeStruct((blocks, req_dev * (head_count // blocks), latent), jnp.bfloat16),
        in_specs=[
            pl.BlockSpec(memory_space=pltpu.SMEM),
            pl.BlockSpec(memory_space=pltpu.SMEM),
            pl.BlockSpec(memory_space=pltpu.VMEM),
            pl.BlockSpec(memory_space=pl.ANY),
        ],
        out_specs=pl.BlockSpec(memory_space=pltpu.VMEM),
        scratch_shapes=[
            pltpu.VMEM((req_dev, width, pages_req * page_size), jnp.bfloat16),
            pltpu.VMEM((req_dev, head_count, latent), jnp.float32),
            pltpu.SemaphoreType.DMA((req_dev * pages_req,)),
        ],
        compiler_params=pltpu.CompilerParams(vmem_limit_bytes=48 * 1024 * 1024),
    )(page_table, lengths, query_columns, cache_columns)


def swap_with(x, axis, distance, size):
    return lax.ppermute(x, axis, [(i, i ^ distance) for i in range(size)])


def halving_scatter(x, axis, size, dim=0):
    index = lax.axis_index(axis)
    x = x.astype(jnp.float32)
    distance = size // 2
    while distance >= 1:
        half = x.shape[dim] // 2
        low = lax.slice_in_dim(x, 0, half, axis=dim)
        high = lax.slice_in_dim(x, half, 2 * half, axis=dim)
        upper = (index & distance) != 0
        keep = jnp.where(upper, high, low)
        send = jnp.where(upper, low, high)
        x = keep + swap_with(send.astype(jnp.bfloat16), axis, distance, size).astype(jnp.float32)
        distance //= 2
    return x


def nearest_first_scatter(parts, axis, size):
    index = lax.axis_index(axis)
    parts = tuple(part.astype(jnp.float32) for part in parts)
    distance = 1
    while distance < size:
        half = parts[0].shape[1] // 2
        upper = (index & distance) != 0
        keeps = tuple(jnp.where(upper, part[:, half:], part[:, :half]) for part in parts)
        sends = tuple(
            jnp.where(upper, part[:, :half], part[:, half:]).astype(jnp.bfloat16) for part in parts
        )
        got = swap_with(sends, axis, distance, size)
        parts = tuple(keep + more.astype(jnp.float32) for keep, more in zip(keeps, got))
        distance *= 2
    return parts


def farthest_first_gather(x, axis, size, dim):
    index = lax.axis_index(axis)
    distance = size // 2
    while distance >= 1:
        got = swap_with(x, axis, distance, size)
        upper = (index & distance) != 0
        x = jnp.where(
            upper, jnp.concatenate([got, x], axis=dim), jnp.concatenate([x, got], axis=dim)
        )
        distance //= 2
    return x


def doubling_gather(x, axis, size, dim):
    index = lax.axis_index(axis)
    distance = 1
    while distance < size:
        got = swap_with(x, axis, distance, size)
        upper = (index & distance) != 0
        x = jnp.where(
            upper, jnp.concatenate([got, x], axis=dim), jnp.concatenate([x, got], axis=dim)
        )
        distance *= 2
    return x


def doubling_sum(x, axis, size):
    distance = 1
    while distance < size:
        x = x + swap_with(x, axis, distance, size)
        distance *= 2
    return x


def nearest_first_rows_scatter(x, axis, size):
    index = lax.axis_index(axis)
    x = x.astype(jnp.float32)
    x = x.reshape((size, x.shape[0] // size) + x.shape[1:])
    distance = 1
    while distance < size:
        pairs = x.reshape((x.shape[0] // 2, 2) + x.shape[1:])
        upper = (index & distance) != 0
        keep = jnp.where(upper, pairs[:, 1], pairs[:, 0])
        send = jnp.where(upper, pairs[:, 0], pairs[:, 1])
        x = keep + swap_with(send.astype(jnp.bfloat16), axis, distance, size).astype(jnp.float32)
        distance *= 2
    return x[0]


def farthest_first_rows_gather(x, axis, size):
    index = lax.axis_index(axis)
    x = x[None]
    distance = size // 2
    while distance >= 1:
        got = swap_with(x, axis, distance, size)
        upper = (index & distance) != 0
        x = jnp.where(upper, jnp.stack([got, x], axis=1), jnp.stack([x, got], axis=1))
        x = x.reshape((-1,) + x.shape[2:])
        distance //= 2
    return x.reshape((-1,) + x.shape[2:])


def matched_sum(x, axis, size):
    x = x.astype(jnp.float32)
    distance = 1
    while distance < size:
        mine = x.astype(jnp.bfloat16)
        x = mine.astype(jnp.float32) + swap_with(mine, axis, distance, size).astype(jnp.float32)
        distance *= 2
    return x


def shards(
    axis_sizes,
    hidden_in,
    queries,
    cache_pool,
    page_table,
    lengths,
    value_up,
    out_proj,
    norm_gain,
    gate_proj,
    up_proj,
    down_proj,
):
    req_dev = queries.shape[0]
    latent = value_up.shape[1]
    value_dim = value_up.shape[2]
    heads_here = value_up.shape[0]
    pages_req = page_table.shape[1]
    score_scale = float(VDIM + ROPE) ** (-0.5)
    units_here = gate_proj.shape[1]
    blocks = axis_sizes["dp"] * axis_sizes["sub"]
    contexts = attend_all(queries, page_table, lengths, cache_pool, latent, score_scale, blocks)
    received = lax.all_to_all(contexts, ("dp", "sub"), split_axis=0, concat_axis=0, tiled=True)
    received = received.reshape(-1, heads_here, latent)
    row_count = received.shape[0]
    values = jnp.einsum("rhc,hcv->rhv", received, value_up, preferred_element_type=jnp.float32)
    values = values.astype(jnp.bfloat16).reshape(row_count, heads_here * value_dim)
    group_values = lax.all_gather(values, "sub", axis=1, tiled=True)
    dp_size = axis_sizes["dp"]
    sub_size = axis_sizes["sub"]
    attention_all = matched_sum(
        jnp.dot(group_values, out_proj, preferred_element_type=jnp.float32), "dp", dp_size
    )
    hidden_all = farthest_first_rows_gather(hidden_in, "dp", dp_size)
    all_residual = hidden_all.astype(jnp.float32) + attention_all
    squares = doubling_sum(jnp.sum(all_residual * all_residual, axis=1), "sub", sub_size)
    gained = (all_residual * norm_gain.astype(jnp.float32)).astype(jnp.bfloat16)
    gate_part = jnp.dot(gained, gate_proj, preferred_element_type=jnp.float32)
    up_part = jnp.dot(gained, up_proj, preferred_element_type=jnp.float32)
    gate_sum, up_sum = nearest_first_scatter((gate_part, up_part), "sub", sub_size)
    scale_rows = lax.rsqrt(squares / float(D) + 1e-06)[:, None]
    hidden_chunk = (jax.nn.silu(gate_sum * scale_rows) * (up_sum * scale_rows)).astype(jnp.bfloat16)
    hidden_units = farthest_first_gather(hidden_chunk, "sub", sub_size, 1)
    feed_forward = nearest_first_rows_scatter(
        jnp.dot(hidden_units, down_proj, preferred_element_type=jnp.float32), "dp", axis_sizes["dp"]
    )
    own_rows = hidden_in.shape[0]
    first_row = lax.axis_index("dp") * own_rows
    attention = lax.dynamic_slice_in_dim(attention_all, first_row, own_rows, 0)
    residual = lax.dynamic_slice_in_dim(all_residual, first_row, own_rows, 0)
    return (attention.astype(jnp.bfloat16), (residual + feed_forward).astype(jnp.bfloat16))


def solution(mesh):
    placed = (
        P(("grp", "dp"), "sub"),
        P(("grp", "dp", "sub"), None, None),
        P(("grp", "dp", "sub"), None, None),
        P(("grp", "dp", "sub"), None),
        P(("grp", "dp", "sub")),
        P(("dp", "sub"), None, None),
        P("dp", "sub"),
        P("sub"),
        P("sub", "dp"),
        P("sub", "dp"),
        P("dp", "sub"),
    )
    return jax.shard_map(
        functools.partial(shards, dict(mesh.shape)),
        mesh=mesh,
        in_specs=placed,
        out_specs=(P(("grp", "dp"), "sub"), P(("grp", "dp"), "sub")),
        check_vma=False,
    )
```

```python
import functools

import jax
import jax.numpy as jnp
from jax import lax
from jax.experimental import pallas as pl
from jax.experimental.pallas import tpu as pltpu
from jax.sharding import PartitionSpec as P

D = 5120
ROPE = 64
VDIM = 128


masked_score = -1e30


def attend_kernel(page_table, lengths, queries, cache_pool, contexts, keys, copy_sems,
                  *, latent, score_scale):
    req_dev, pages_req = page_table.shape
    page_size = cache_pool.shape[2]
    head_count = queries.shape[2]

    def page_copy(slot, page):
        return pltpu.make_async_copy(
            cache_pool.at[page_table[slot, page]],
            keys.at[slot, :, pl.ds(pl.multiple_of(page * page_size, page_size), page_size)],
            copy_sems.at[slot * pages_req + page],
        )

    for slot in range(req_dev):
        def start(page, carry, slot=slot):
            page_copy(slot, page).start()
            return carry

        lax.fori_loop(0, pages_req, start, 0)

    span = pages_req * page_size
    chunk = min(512, span)
    positions = lax.broadcasted_iota(jnp.int32, (head_count, chunk), 1)
    for slot in range(req_dev):
        def finish(page, carry, slot=slot):
            page_copy(slot, page).wait()
            return carry

        lax.fori_loop(0, pages_req, finish, 0)
        length = lengths[slot]
        query_rows = jnp.transpose(queries[slot])
        blocks_of_scores = []
        row_max = jnp.full((head_count, 1), masked_score, jnp.float32)
        for first in range(0, span, chunk):
            block = jnp.dot(
                query_rows, keys[slot, :, first:first + chunk], preferred_element_type=jnp.float32
            ) * score_scale
            block = jnp.where(positions + first < length, block, masked_score)
            blocks_of_scores.append(block)
            row_max = jnp.maximum(row_max, jnp.max(block, axis=1, keepdims=True))
        denominator = jnp.zeros((head_count, 1), jnp.float32)
        weighted = jnp.zeros((head_count, latent), jnp.float32)
        for first, block in zip(range(0, span, chunk), blocks_of_scores):
            exponent = jnp.exp(block - row_max)
            denominator = denominator + jnp.sum(exponent, axis=1, keepdims=True)
            weighted = weighted + lax.dot_general(
                exponent.astype(jnp.bfloat16),
                keys[slot, :latent, first:first + chunk],
                (((1,), (1,)), ((), ())),
                preferred_element_type=jnp.float32,
            )
        blocks, block_heads = contexts.shape[0], head_count // contexts.shape[0]
        context = (weighted / denominator).reshape(blocks, block_heads, latent)
        contexts[:, slot * block_heads:(slot + 1) * block_heads, :] = context.astype(contexts.dtype)


def attend_all(queries, page_table, lengths, cache_pool, latent, score_scale, blocks):
    req_dev, head_count, width = queries.shape
    pages_req = page_table.shape[1]
    query_columns = jnp.swapaxes(queries, 1, 2)
    page_size = cache_pool.shape[1]
    cache_columns = jnp.swapaxes(cache_pool, 1, 2)
    kernel = functools.partial(attend_kernel, latent=latent, score_scale=score_scale)
    return pl.pallas_call(
        kernel,
        out_shape=jax.ShapeDtypeStruct((blocks, req_dev * (head_count // blocks), latent), jnp.bfloat16),
        in_specs=[
            pl.BlockSpec(memory_space=pltpu.SMEM),
            pl.BlockSpec(memory_space=pltpu.SMEM),
            pl.BlockSpec(memory_space=pltpu.VMEM),
            pl.BlockSpec(memory_space=pl.ANY),
        ],
        out_specs=pl.BlockSpec(memory_space=pltpu.VMEM),
        scratch_shapes=[
            pltpu.VMEM((req_dev, width, pages_req * page_size), jnp.bfloat16),
            pltpu.SemaphoreType.DMA((req_dev * pages_req,)),
        ],
        compiler_params=pltpu.CompilerParams(vmem_limit_bytes=48 * 1024 * 1024),
    )(page_table, lengths, query_columns, cache_columns)


def swap_with(x, axis, distance, size):
    return lax.ppermute(x, axis, [(i, i ^ distance) for i in range(size)])


def halving_scatter(x, axis, size, dim=0):
    index = lax.axis_index(axis)
    x = x.astype(jnp.float32)
    distance = size // 2
    while distance >= 1:
        half = x.shape[dim] // 2
        low = lax.slice_in_dim(x, 0, half, axis=dim)
        high = lax.slice_in_dim(x, half, 2 * half, axis=dim)
        upper = (index & distance) != 0
        keep = jnp.where(upper, high, low)
        send = jnp.where(upper, low, high)
        x = keep + swap_with(send.astype(jnp.bfloat16), axis, distance, size).astype(jnp.float32)
        distance //= 2
    return x


def nearest_first_scatter(parts, axis, size):
    index = lax.axis_index(axis)
    parts = tuple(part.astype(jnp.float32) for part in parts)
    distance = 1
    while distance < size:
        half = parts[0].shape[1] // 2
        upper = (index & distance) != 0
        keeps = tuple(jnp.where(upper, part[:, half:], part[:, :half]) for part in parts)
        sends = tuple(
            jnp.where(upper, part[:, :half], part[:, half:]).astype(jnp.bfloat16) for part in parts
        )
        got = swap_with(sends, axis, distance, size)
        parts = tuple(keep + more.astype(jnp.float32) for keep, more in zip(keeps, got))
        distance *= 2
    return parts


def farthest_first_gather(x, axis, size, dim):
    index = lax.axis_index(axis)
    distance = size // 2
    while distance >= 1:
        got = swap_with(x, axis, distance, size)
        upper = (index & distance) != 0
        x = jnp.where(
            upper, jnp.concatenate([got, x], axis=dim), jnp.concatenate([x, got], axis=dim)
        )
        distance //= 2
    return x


def doubling_gather(x, axis, size, dim):
    index = lax.axis_index(axis)
    distance = 1
    while distance < size:
        got = swap_with(x, axis, distance, size)
        upper = (index & distance) != 0
        x = jnp.where(
            upper, jnp.concatenate([got, x], axis=dim), jnp.concatenate([x, got], axis=dim)
        )
        distance *= 2
    return x


def doubling_sum(x, axis, size):
    distance = 1
    while distance < size:
        x = x + swap_with(x, axis, distance, size)
        distance *= 2
    return x


def nearest_first_rows_scatter(x, axis, size):
    index = lax.axis_index(axis)
    x = x.astype(jnp.float32)
    x = x.reshape((size, x.shape[0] // size) + x.shape[1:])
    distance = 1
    while distance < size:
        pairs = x.reshape((x.shape[0] // 2, 2) + x.shape[1:])
        upper = (index & distance) != 0
        keep = jnp.where(upper, pairs[:, 1], pairs[:, 0])
        send = jnp.where(upper, pairs[:, 0], pairs[:, 1])
        x = keep + swap_with(send.astype(jnp.bfloat16), axis, distance, size).astype(jnp.float32)
        distance *= 2
    return x[0]


def farthest_first_rows_gather(x, axis, size):
    index = lax.axis_index(axis)
    x = x[None]
    distance = size // 2
    while distance >= 1:
        got = swap_with(x, axis, distance, size)
        upper = (index & distance) != 0
        x = jnp.where(upper, jnp.stack([got, x], axis=1), jnp.stack([x, got], axis=1))
        x = x.reshape((-1,) + x.shape[2:])
        distance //= 2
    return x.reshape((-1,) + x.shape[2:])


def matched_sum(x, axis, size):
    x = x.astype(jnp.float32)
    distance = 1
    while distance < size:
        mine = x.astype(jnp.bfloat16)
        x = mine.astype(jnp.float32) + swap_with(mine, axis, distance, size).astype(jnp.float32)
        distance *= 2
    return x


def shards(
    axis_sizes,
    hidden_in,
    queries,
    cache_pool,
    page_table,
    lengths,
    value_up,
    out_proj,
    norm_gain,
    gate_proj,
    up_proj,
    down_proj,
):
    req_dev = queries.shape[0]
    latent = value_up.shape[1]
    value_dim = value_up.shape[2]
    heads_here = value_up.shape[0]
    pages_req = page_table.shape[1]
    score_scale = float(VDIM + ROPE) ** (-0.5)
    units_here = gate_proj.shape[1]
    blocks = axis_sizes["dp"] * axis_sizes["sub"]
    contexts = attend_all(queries, page_table, lengths, cache_pool, latent, score_scale, blocks)
    received = lax.all_to_all(contexts, ("dp", "sub"), split_axis=0, concat_axis=0, tiled=True)
    received = received.reshape(-1, heads_here, latent)
    row_count = received.shape[0]
    values = jnp.einsum("rhc,hcv->rhv", received, value_up, preferred_element_type=jnp.float32)
    values = values.astype(jnp.bfloat16).reshape(row_count, heads_here * value_dim)
    group_values = lax.all_gather(values, "sub", axis=1, tiled=True)
    dp_size = axis_sizes["dp"]
    sub_size = axis_sizes["sub"]
    attention_all = matched_sum(
        jnp.dot(group_values, out_proj, preferred_element_type=jnp.float32), "dp", dp_size
    )
    hidden_all = farthest_first_rows_gather(hidden_in, "dp", dp_size)
    all_residual = hidden_all.astype(jnp.float32) + attention_all
    squares = doubling_sum(jnp.sum(all_residual * all_residual, axis=1), "sub", sub_size)
    gained = (all_residual * norm_gain.astype(jnp.float32)).astype(jnp.bfloat16)
    gate_part = jnp.dot(gained, gate_proj, preferred_element_type=jnp.float32)
    up_part = jnp.dot(gained, up_proj, preferred_element_type=jnp.float32)
    gate_sum, up_sum = nearest_first_scatter((gate_part, up_part), "sub", sub_size)
    scale_rows = lax.rsqrt(squares / float(D) + 1e-06)[:, None]
    hidden_chunk = (jax.nn.silu(gate_sum * scale_rows) * (up_sum * scale_rows)).astype(jnp.bfloat16)
    hidden_units = farthest_first_gather(hidden_chunk, "sub", sub_size, 1)
    feed_forward = nearest_first_rows_scatter(
        jnp.dot(hidden_units, down_proj, preferred_element_type=jnp.float32), "dp", axis_sizes["dp"]
    )
    own_rows = hidden_in.shape[0]
    first_row = lax.axis_index("dp") * own_rows
    attention = lax.dynamic_slice_in_dim(attention_all, first_row, own_rows, 0)
    residual = lax.dynamic_slice_in_dim(all_residual, first_row, own_rows, 0)
    return (attention.astype(jnp.bfloat16), (residual + feed_forward).astype(jnp.bfloat16))


def solution(mesh):
    placed = (
        P(("grp", "dp"), "sub"),
        P(("grp", "dp", "sub"), None, None),
        P(("grp", "dp", "sub"), None, None),
        P(("grp", "dp", "sub"), None),
        P(("grp", "dp", "sub")),
        P(("dp", "sub"), None, None),
        P("dp", "sub"),
        P("sub"),
        P("sub", "dp"),
        P("sub", "dp"),
        P("dp", "sub"),
    )
    return jax.shard_map(
        functools.partial(shards, dict(mesh.shape)),
        mesh=mesh,
        in_specs=placed,
        out_specs=(P(("grp", "dp"), "sub"), P(("grp", "dp"), "sub")),
        check_vma=False,
    )
```

```python
import functools

import jax
import jax.numpy as jnp
from jax import lax
from jax.experimental import pallas as pl
from jax.experimental.pallas import tpu as pltpu
from jax.sharding import PartitionSpec as P

D = 5120
ROPE = 64
VDIM = 128


masked_score = -1e30


def attend_kernel(page_table, lengths, queries, cache_pool, contexts, keys, copy_sems,
                  *, latent, score_scale):
    req_dev, pages_req = page_table.shape
    page_size = cache_pool.shape[2]
    head_count = queries.shape[2]

    def page_copy(slot, page):
        return pltpu.make_async_copy(
            cache_pool.at[page_table[slot, page]],
            keys.at[slot, :, pl.ds(pl.multiple_of(page * page_size, page_size), page_size)],
            copy_sems.at[slot * pages_req + page],
        )

    for slot in range(req_dev):
        def start(page, carry, slot=slot):
            page_copy(slot, page).start()
            return carry

        lax.fori_loop(0, pages_req, start, 0)

    span = pages_req * page_size
    chunk = min(256, span)
    positions = lax.broadcasted_iota(jnp.int32, (head_count, chunk), 1)
    for slot in range(req_dev):
        def finish(page, carry, slot=slot):
            page_copy(slot, page).wait()
            return carry

        lax.fori_loop(0, pages_req, finish, 0)
        length = lengths[slot]
        query_rows = jnp.transpose(queries[slot])
        blocks_of_scores = []
        row_max = jnp.full((head_count, 1), masked_score, jnp.float32)
        for first in range(0, span, chunk):
            block = jnp.dot(
                query_rows, keys[slot, :, first:first + chunk], preferred_element_type=jnp.float32
            ) * score_scale
            block = jnp.where(positions + first < length, block, masked_score)
            blocks_of_scores.append(block)
            row_max = jnp.maximum(row_max, jnp.max(block, axis=1, keepdims=True))
        denominator = jnp.zeros((head_count, 1), jnp.float32)
        weighted = jnp.zeros((head_count, latent), jnp.float32)
        for first, block in zip(range(0, span, chunk), blocks_of_scores):
            exponent = jnp.exp(block - row_max)
            denominator = denominator + jnp.sum(exponent, axis=1, keepdims=True)
            weighted = weighted + lax.dot_general(
                exponent.astype(jnp.bfloat16),
                keys[slot, :latent, first:first + chunk],
                (((1,), (1,)), ((), ())),
                preferred_element_type=jnp.float32,
            )
        blocks, block_heads = contexts.shape[0], head_count // contexts.shape[0]
        context = (weighted / denominator).reshape(blocks, block_heads, latent)
        contexts[:, slot * block_heads:(slot + 1) * block_heads, :] = context.astype(contexts.dtype)


def attend_all(queries, page_table, lengths, cache_pool, latent, score_scale, blocks):
    req_dev, head_count, width = queries.shape
    pages_req = page_table.shape[1]
    query_columns = jnp.swapaxes(queries, 1, 2)
    page_size = cache_pool.shape[1]
    cache_columns = jnp.swapaxes(cache_pool, 1, 2)
    kernel = functools.partial(attend_kernel, latent=latent, score_scale=score_scale)
    return pl.pallas_call(
        kernel,
        out_shape=jax.ShapeDtypeStruct((blocks, req_dev * (head_count // blocks), latent), jnp.bfloat16),
        in_specs=[
            pl.BlockSpec(memory_space=pltpu.SMEM),
            pl.BlockSpec(memory_space=pltpu.SMEM),
            pl.BlockSpec(memory_space=pltpu.VMEM),
            pl.BlockSpec(memory_space=pl.ANY),
        ],
        out_specs=pl.BlockSpec(memory_space=pltpu.VMEM),
        scratch_shapes=[
            pltpu.VMEM((req_dev, width, pages_req * page_size), jnp.bfloat16),
            pltpu.SemaphoreType.DMA((req_dev * pages_req,)),
        ],
        compiler_params=pltpu.CompilerParams(vmem_limit_bytes=48 * 1024 * 1024),
    )(page_table, lengths, query_columns, cache_columns)


def swap_with(x, axis, distance, size):
    return lax.ppermute(x, axis, [(i, i ^ distance) for i in range(size)])


def halving_scatter(x, axis, size, dim=0):
    index = lax.axis_index(axis)
    x = x.astype(jnp.float32)
    distance = size // 2
    while distance >= 1:
        half = x.shape[dim] // 2
        low = lax.slice_in_dim(x, 0, half, axis=dim)
        high = lax.slice_in_dim(x, half, 2 * half, axis=dim)
        upper = (index & distance) != 0
        keep = jnp.where(upper, high, low)
        send = jnp.where(upper, low, high)
        x = keep + swap_with(send.astype(jnp.bfloat16), axis, distance, size).astype(jnp.float32)
        distance //= 2
    return x


def nearest_first_scatter(parts, axis, size):
    index = lax.axis_index(axis)
    parts = tuple(part.astype(jnp.float32) for part in parts)
    distance = 1
    while distance < size:
        half = parts[0].shape[1] // 2
        upper = (index & distance) != 0
        keeps = tuple(jnp.where(upper, part[:, half:], part[:, :half]) for part in parts)
        sends = tuple(
            jnp.where(upper, part[:, :half], part[:, half:]).astype(jnp.bfloat16) for part in parts
        )
        got = swap_with(sends, axis, distance, size)
        parts = tuple(keep + more.astype(jnp.float32) for keep, more in zip(keeps, got))
        distance *= 2
    return parts


def farthest_first_gather(x, axis, size, dim):
    index = lax.axis_index(axis)
    distance = size // 2
    while distance >= 1:
        got = swap_with(x, axis, distance, size)
        upper = (index & distance) != 0
        x = jnp.where(
            upper, jnp.concatenate([got, x], axis=dim), jnp.concatenate([x, got], axis=dim)
        )
        distance //= 2
    return x


def doubling_gather(x, axis, size, dim):
    index = lax.axis_index(axis)
    distance = 1
    while distance < size:
        got = swap_with(x, axis, distance, size)
        upper = (index & distance) != 0
        x = jnp.where(
            upper, jnp.concatenate([got, x], axis=dim), jnp.concatenate([x, got], axis=dim)
        )
        distance *= 2
    return x


def doubling_sum(x, axis, size):
    distance = 1
    while distance < size:
        x = x + swap_with(x, axis, distance, size)
        distance *= 2
    return x


def nearest_first_rows_scatter(x, axis, size):
    index = lax.axis_index(axis)
    x = x.astype(jnp.float32)
    x = x.reshape((size, x.shape[0] // size) + x.shape[1:])
    distance = 1
    while distance < size:
        pairs = x.reshape((x.shape[0] // 2, 2) + x.shape[1:])
        upper = (index & distance) != 0
        keep = jnp.where(upper, pairs[:, 1], pairs[:, 0])
        send = jnp.where(upper, pairs[:, 0], pairs[:, 1])
        x = keep + swap_with(send.astype(jnp.bfloat16), axis, distance, size).astype(jnp.float32)
        distance *= 2
    return x[0]


def farthest_first_rows_gather(x, axis, size):
    index = lax.axis_index(axis)
    x = x[None]
    distance = size // 2
    while distance >= 1:
        got = swap_with(x, axis, distance, size)
        upper = (index & distance) != 0
        x = jnp.where(upper, jnp.stack([got, x], axis=1), jnp.stack([x, got], axis=1))
        x = x.reshape((-1,) + x.shape[2:])
        distance //= 2
    return x.reshape((-1,) + x.shape[2:])


def matched_sum(x, axis, size):
    x = x.astype(jnp.float32)
    distance = 1
    while distance < size:
        mine = x.astype(jnp.bfloat16)
        x = mine.astype(jnp.float32) + swap_with(mine, axis, distance, size).astype(jnp.float32)
        distance *= 2
    return x


def shards(
    axis_sizes,
    hidden_in,
    queries,
    cache_pool,
    page_table,
    lengths,
    value_up,
    out_proj,
    norm_gain,
    gate_proj,
    up_proj,
    down_proj,
):
    req_dev = queries.shape[0]
    latent = value_up.shape[1]
    value_dim = value_up.shape[2]
    heads_here = value_up.shape[0]
    pages_req = page_table.shape[1]
    score_scale = float(VDIM + ROPE) ** (-0.5)
    units_here = gate_proj.shape[1]
    blocks = axis_sizes["dp"] * axis_sizes["sub"]
    contexts = attend_all(queries, page_table, lengths, cache_pool, latent, score_scale, blocks)
    received = lax.all_to_all(contexts, ("dp", "sub"), split_axis=0, concat_axis=0, tiled=True)
    received = received.reshape(-1, heads_here, latent)
    row_count = received.shape[0]
    values = jnp.einsum("rhc,hcv->rhv", received, value_up, preferred_element_type=jnp.float32)
    values = values.astype(jnp.bfloat16).reshape(row_count, heads_here * value_dim)
    group_values = lax.all_gather(values, "sub", axis=1, tiled=True)
    dp_size = axis_sizes["dp"]
    sub_size = axis_sizes["sub"]
    attention_all = matched_sum(
        jnp.dot(group_values, out_proj, preferred_element_type=jnp.float32), "dp", dp_size
    )
    hidden_all = farthest_first_rows_gather(hidden_in, "dp", dp_size)
    all_residual = hidden_all.astype(jnp.float32) + attention_all
    squares = doubling_sum(jnp.sum(all_residual * all_residual, axis=1), "sub", sub_size)
    gained = (all_residual * norm_gain.astype(jnp.float32)).astype(jnp.bfloat16)
    gate_part = jnp.dot(gained, gate_proj, preferred_element_type=jnp.float32)
    up_part = jnp.dot(gained, up_proj, preferred_element_type=jnp.float32)
    gate_sum, up_sum = nearest_first_scatter((gate_part, up_part), "sub", sub_size)
    scale_rows = lax.rsqrt(squares / float(D) + 1e-06)[:, None]
    hidden_chunk = (jax.nn.silu(gate_sum * scale_rows) * (up_sum * scale_rows)).astype(jnp.bfloat16)
    hidden_units = farthest_first_gather(hidden_chunk, "sub", sub_size, 1)
    feed_forward = nearest_first_rows_scatter(
        jnp.dot(hidden_units, down_proj, preferred_element_type=jnp.float32), "dp", axis_sizes["dp"]
    )
    own_rows = hidden_in.shape[0]
    first_row = lax.axis_index("dp") * own_rows
    attention = lax.dynamic_slice_in_dim(attention_all, first_row, own_rows, 0)
    residual = lax.dynamic_slice_in_dim(all_residual, first_row, own_rows, 0)
    return (attention.astype(jnp.bfloat16), (residual + feed_forward).astype(jnp.bfloat16))


def solution(mesh):
    placed = (
        P(("grp", "dp"), "sub"),
        P(("grp", "dp", "sub"), None, None),
        P(("grp", "dp", "sub"), None, None),
        P(("grp", "dp", "sub"), None),
        P(("grp", "dp", "sub")),
        P(("dp", "sub"), None, None),
        P("dp", "sub"),
        P("sub"),
        P("sub", "dp"),
        P("sub", "dp"),
        P("dp", "sub"),
    )
    return jax.shard_map(
        functools.partial(shards, dict(mesh.shape)),
        mesh=mesh,
        in_specs=placed,
        out_specs=(P(("grp", "dp"), "sub"), P(("grp", "dp"), "sub")),
        check_vma=False,
    )
```

```python
import functools

import jax
import jax.numpy as jnp
from jax import lax
from jax.experimental import pallas as pl
from jax.experimental.pallas import tpu as pltpu
from jax.sharding import PartitionSpec as P

D = 5120
ROPE = 64
VDIM = 128


masked_score = -1e30


def attend_kernel(page_table, lengths, queries, cache_pool, contexts, keys, score_ref, row_max_ref,
                  denominator_ref, weighted_ref, copy_sems, *, latent, score_scale, chunk):
    req_dev, pages_req = page_table.shape
    page_size = cache_pool.shape[2]
    head_count = queries.shape[2]

    def page_copy(slot, page):
        return pltpu.make_async_copy(
            cache_pool.at[page_table[slot, page]],
            keys.at[slot, :, pl.ds(pl.multiple_of(page * page_size, page_size), page_size)],
            copy_sems.at[slot * pages_req + page],
        )

    for slot in range(req_dev):
        def start(page, carry, slot=slot):
            page_copy(slot, page).start()
            return carry

        lax.fori_loop(0, pages_req, start, 0)

    span = pages_req * page_size
    positions = lax.broadcasted_iota(jnp.int32, (head_count, chunk), 1)
    for slot in range(req_dev):
        def finish(page, carry, slot=slot):
            page_copy(slot, page).wait()
            return carry

        lax.fori_loop(0, pages_req, finish, 0)
        length = lengths[slot]
        query_rows = jnp.transpose(queries[slot])
        row_max_ref[...] = jnp.full(row_max_ref.shape, masked_score, jnp.float32)
        for index, first in enumerate(range(0, span, chunk)):
            @pl.when(first < length)
            def _(index=index, first=first):
                block = jnp.dot(
                    query_rows, keys[slot, :, first:first + chunk], preferred_element_type=jnp.float32
                ) * score_scale
                block = jnp.where(positions + first < length, block, masked_score)
                score_ref[index] = block
                row_max_ref[...] = jnp.maximum(row_max_ref[...], jnp.max(block, axis=1, keepdims=True))

        row_max = row_max_ref[...]
        denominator_ref[...] = jnp.zeros_like(denominator_ref)
        weighted_ref[...] = jnp.zeros_like(weighted_ref)
        for index, first in enumerate(range(0, span, chunk)):
            @pl.when(first < length)
            def _(index=index, first=first):
                exponent = jnp.exp(score_ref[index] - row_max)
                denominator_ref[...] += jnp.sum(exponent, axis=1, keepdims=True)
                weighted_ref[...] += lax.dot_general(
                    exponent.astype(jnp.bfloat16),
                    keys[slot, :latent, first:first + chunk],
                    (((1,), (1,)), ((), ())),
                    preferred_element_type=jnp.float32,
                )

        weighted = weighted_ref[...]
        denominator = denominator_ref[...]
        blocks, block_heads = contexts.shape[0], head_count // contexts.shape[0]
        context = (weighted / denominator).reshape(blocks, block_heads, latent)
        contexts[:, slot * block_heads:(slot + 1) * block_heads, :] = context.astype(contexts.dtype)


def attend_all(queries, page_table, lengths, cache_pool, latent, score_scale, blocks):
    req_dev, head_count, width = queries.shape
    pages_req = page_table.shape[1]
    query_columns = jnp.swapaxes(queries, 1, 2)
    page_size = cache_pool.shape[1]
    cache_columns = jnp.swapaxes(cache_pool, 1, 2)
    span = pages_req * page_size
    chunk = min(512, span)
    kernel = functools.partial(attend_kernel, latent=latent, score_scale=score_scale, chunk=chunk)
    return pl.pallas_call(
        kernel,
        out_shape=jax.ShapeDtypeStruct((blocks, req_dev * (head_count // blocks), latent), jnp.bfloat16),
        in_specs=[
            pl.BlockSpec(memory_space=pltpu.SMEM),
            pl.BlockSpec(memory_space=pltpu.SMEM),
            pl.BlockSpec(memory_space=pltpu.VMEM),
            pl.BlockSpec(memory_space=pl.ANY),
        ],
        out_specs=pl.BlockSpec(memory_space=pltpu.VMEM),
        scratch_shapes=[
            pltpu.VMEM((req_dev, width, span), jnp.bfloat16),
            pltpu.VMEM((span // chunk, head_count, chunk), jnp.float32),
            pltpu.VMEM((head_count, 1), jnp.float32),
            pltpu.VMEM((head_count, 1), jnp.float32),
            pltpu.VMEM((head_count, latent), jnp.float32),
            pltpu.SemaphoreType.DMA((req_dev * pages_req,)),
        ],
        compiler_params=pltpu.CompilerParams(vmem_limit_bytes=48 * 1024 * 1024),
    )(page_table, lengths, query_columns, cache_columns)


def swap_with(x, axis, distance, size):
    return lax.ppermute(x, axis, [(i, i ^ distance) for i in range(size)])


def halving_scatter(x, axis, size, dim=0):
    index = lax.axis_index(axis)
    x = x.astype(jnp.float32)
    distance = size // 2
    while distance >= 1:
        half = x.shape[dim] // 2
        low = lax.slice_in_dim(x, 0, half, axis=dim)
        high = lax.slice_in_dim(x, half, 2 * half, axis=dim)
        upper = (index & distance) != 0
        keep = jnp.where(upper, high, low)
        send = jnp.where(upper, low, high)
        x = keep + swap_with(send.astype(jnp.bfloat16), axis, distance, size).astype(jnp.float32)
        distance //= 2
    return x


def nearest_first_scatter(parts, axis, size):
    index = lax.axis_index(axis)
    parts = tuple(part.astype(jnp.float32) for part in parts)
    distance = 1
    while distance < size:
        half = parts[0].shape[1] // 2
        upper = (index & distance) != 0
        keeps = tuple(jnp.where(upper, part[:, half:], part[:, :half]) for part in parts)
        sends = tuple(
            jnp.where(upper, part[:, :half], part[:, half:]).astype(jnp.bfloat16) for part in parts
        )
        got = swap_with(sends, axis, distance, size)
        parts = tuple(keep + more.astype(jnp.float32) for keep, more in zip(keeps, got))
        distance *= 2
    return parts


def farthest_first_gather(x, axis, size, dim):
    index = lax.axis_index(axis)
    distance = size // 2
    while distance >= 1:
        got = swap_with(x, axis, distance, size)
        upper = (index & distance) != 0
        x = jnp.where(
            upper, jnp.concatenate([got, x], axis=dim), jnp.concatenate([x, got], axis=dim)
        )
        distance //= 2
    return x


def doubling_gather(x, axis, size, dim):
    index = lax.axis_index(axis)
    distance = 1
    while distance < size:
        got = swap_with(x, axis, distance, size)
        upper = (index & distance) != 0
        x = jnp.where(
            upper, jnp.concatenate([got, x], axis=dim), jnp.concatenate([x, got], axis=dim)
        )
        distance *= 2
    return x


def doubling_sum(x, axis, size):
    distance = 1
    while distance < size:
        x = x + swap_with(x, axis, distance, size)
        distance *= 2
    return x


def nearest_first_rows_scatter(x, axis, size):
    index = lax.axis_index(axis)
    x = x.astype(jnp.float32)
    x = x.reshape((size, x.shape[0] // size) + x.shape[1:])
    distance = 1
    while distance < size:
        pairs = x.reshape((x.shape[0] // 2, 2) + x.shape[1:])
        upper = (index & distance) != 0
        keep = jnp.where(upper, pairs[:, 1], pairs[:, 0])
        send = jnp.where(upper, pairs[:, 0], pairs[:, 1])
        x = keep + swap_with(send.astype(jnp.bfloat16), axis, distance, size).astype(jnp.float32)
        distance *= 2
    return x[0]


def farthest_first_rows_gather(x, axis, size):
    index = lax.axis_index(axis)
    x = x[None]
    distance = size // 2
    while distance >= 1:
        got = swap_with(x, axis, distance, size)
        upper = (index & distance) != 0
        x = jnp.where(upper, jnp.stack([got, x], axis=1), jnp.stack([x, got], axis=1))
        x = x.reshape((-1,) + x.shape[2:])
        distance //= 2
    return x.reshape((-1,) + x.shape[2:])


def matched_sum(x, axis, size):
    x = x.astype(jnp.float32)
    distance = 1
    while distance < size:
        mine = x.astype(jnp.bfloat16)
        x = mine.astype(jnp.float32) + swap_with(mine, axis, distance, size).astype(jnp.float32)
        distance *= 2
    return x


def shards(
    axis_sizes,
    hidden_in,
    queries,
    cache_pool,
    page_table,
    lengths,
    value_up,
    out_proj,
    norm_gain,
    gate_proj,
    up_proj,
    down_proj,
):
    req_dev = queries.shape[0]
    latent = value_up.shape[1]
    value_dim = value_up.shape[2]
    heads_here = value_up.shape[0]
    pages_req = page_table.shape[1]
    score_scale = float(VDIM + ROPE) ** (-0.5)
    units_here = gate_proj.shape[1]
    blocks = axis_sizes["dp"] * axis_sizes["sub"]
    contexts = attend_all(queries, page_table, lengths, cache_pool, latent, score_scale, blocks)
    received = lax.all_to_all(contexts, ("dp", "sub"), split_axis=0, concat_axis=0, tiled=True)
    received = received.reshape(-1, heads_here, latent)
    row_count = received.shape[0]
    values = jnp.einsum("rhc,hcv->rhv", received, value_up, preferred_element_type=jnp.float32)
    values = values.astype(jnp.bfloat16).reshape(row_count, heads_here * value_dim)
    group_values = lax.all_gather(values, "sub", axis=1, tiled=True)
    dp_size = axis_sizes["dp"]
    sub_size = axis_sizes["sub"]
    attention_all = matched_sum(
        jnp.dot(group_values, out_proj, preferred_element_type=jnp.float32), "dp", dp_size
    )
    hidden_all = farthest_first_rows_gather(hidden_in, "dp", dp_size)
    all_residual = hidden_all.astype(jnp.float32) + attention_all
    squares = doubling_sum(jnp.sum(all_residual * all_residual, axis=1), "sub", sub_size)
    gained = (all_residual * norm_gain.astype(jnp.float32)).astype(jnp.bfloat16)
    gate_part = jnp.dot(gained, gate_proj, preferred_element_type=jnp.float32)
    up_part = jnp.dot(gained, up_proj, preferred_element_type=jnp.float32)
    gate_sum, up_sum = nearest_first_scatter((gate_part, up_part), "sub", sub_size)
    scale_rows = lax.rsqrt(squares / float(D) + 1e-06)[:, None]
    hidden_chunk = (jax.nn.silu(gate_sum * scale_rows) * (up_sum * scale_rows)).astype(jnp.bfloat16)
    hidden_units = farthest_first_gather(hidden_chunk, "sub", sub_size, 1)
    feed_forward = nearest_first_rows_scatter(
        jnp.dot(hidden_units, down_proj, preferred_element_type=jnp.float32), "dp", axis_sizes["dp"]
    )
    own_rows = hidden_in.shape[0]
    first_row = lax.axis_index("dp") * own_rows
    attention = lax.dynamic_slice_in_dim(attention_all, first_row, own_rows, 0)
    residual = lax.dynamic_slice_in_dim(all_residual, first_row, own_rows, 0)
    return (attention.astype(jnp.bfloat16), (residual + feed_forward).astype(jnp.bfloat16))


def solution(mesh):
    placed = (
        P(("grp", "dp"), "sub"),
        P(("grp", "dp", "sub"), None, None),
        P(("grp", "dp", "sub"), None, None),
        P(("grp", "dp", "sub"), None),
        P(("grp", "dp", "sub")),
        P(("dp", "sub"), None, None),
        P("dp", "sub"),
        P("sub"),
        P("sub", "dp"),
        P("sub", "dp"),
        P("dp", "sub"),
    )
    return jax.shard_map(
        functools.partial(shards, dict(mesh.shape)),
        mesh=mesh,
        in_specs=placed,
        out_specs=(P(("grp", "dp"), "sub"), P(("grp", "dp"), "sub")),
        check_vma=False,
    )
```

```python
import functools

import jax
import jax.numpy as jnp
from jax import lax
from jax.experimental import pallas as pl
from jax.experimental.pallas import tpu as pltpu
from jax.sharding import PartitionSpec as P

D = 5120
ROPE = 64
VDIM = 128


masked_score = -1e30


def attend_kernel(page_table, lengths, queries, cache_pool, contexts, keys, copy_sems,
                  *, latent, score_scale):
    req_dev, pages_req = page_table.shape
    page_size = cache_pool.shape[2]
    head_count = queries.shape[2]

    def page_copy(slot, page):
        return pltpu.make_async_copy(
            cache_pool.at[page_table[slot, page]],
            keys.at[slot, :, pl.ds(pl.multiple_of(page * page_size, page_size), page_size)],
            copy_sems.at[slot * pages_req + page],
        )

    for slot in range(req_dev):
        def start(page, carry, slot=slot):
            page_copy(slot, page).start()
            return carry

        lax.fori_loop(0, pages_req, start, 0)

    span = pages_req * page_size
    chunk = min(1024, span)
    positions = lax.broadcasted_iota(jnp.int32, (head_count, chunk), 1)
    for slot in range(req_dev):
        def finish(page, carry, slot=slot):
            page_copy(slot, page).wait()
            return carry

        lax.fori_loop(0, pages_req, finish, 0)
        length = lengths[slot]
        query_rows = jnp.transpose(queries[slot])
        blocks_of_scores = []
        row_max = jnp.full((head_count, 1), masked_score, jnp.float32)
        for first in range(0, span, chunk):
            block = jnp.dot(
                query_rows, keys[slot, :, first:first + chunk], preferred_element_type=jnp.float32
            ) * score_scale
            block = jnp.where(positions + first < length, block, masked_score)
            blocks_of_scores.append(block)
            row_max = jnp.maximum(row_max, jnp.max(block, axis=1, keepdims=True))
        denominator = jnp.zeros((head_count, 1), jnp.float32)
        weighted = jnp.zeros((head_count, latent), jnp.float32)
        for first, block in zip(range(0, span, chunk), blocks_of_scores):
            exponent = jnp.exp(block - row_max)
            denominator = denominator + jnp.sum(exponent, axis=1, keepdims=True)
            weighted = weighted + lax.dot_general(
                exponent.astype(jnp.bfloat16),
                keys[slot, :latent, first:first + chunk],
                (((1,), (1,)), ((), ())),
                preferred_element_type=jnp.float32,
            )
        blocks, block_heads = contexts.shape[0], head_count // contexts.shape[0]
        context = (weighted / denominator).reshape(blocks, block_heads, latent)
        contexts[:, slot * block_heads:(slot + 1) * block_heads, :] = context.astype(contexts.dtype)


def attend_all(queries, page_table, lengths, cache_pool, latent, score_scale, blocks):
    req_dev, head_count, width = queries.shape
    pages_req = page_table.shape[1]
    query_columns = jnp.swapaxes(queries, 1, 2)
    page_size = cache_pool.shape[1]
    cache_columns = jnp.swapaxes(cache_pool, 1, 2)
    kernel = functools.partial(attend_kernel, latent=latent, score_scale=score_scale)
    return pl.pallas_call(
        kernel,
        out_shape=jax.ShapeDtypeStruct((blocks, req_dev * (head_count // blocks), latent), jnp.bfloat16),
        in_specs=[
            pl.BlockSpec(memory_space=pltpu.SMEM),
            pl.BlockSpec(memory_space=pltpu.SMEM),
            pl.BlockSpec(memory_space=pltpu.VMEM),
            pl.BlockSpec(memory_space=pl.ANY),
        ],
        out_specs=pl.BlockSpec(memory_space=pltpu.VMEM),
        scratch_shapes=[
            pltpu.VMEM((req_dev, width, pages_req * page_size), jnp.bfloat16),
            pltpu.SemaphoreType.DMA((req_dev * pages_req,)),
        ],
        compiler_params=pltpu.CompilerParams(vmem_limit_bytes=48 * 1024 * 1024),
    )(page_table, lengths, query_columns, cache_columns)


def swap_with(x, axis, distance, size):
    return lax.ppermute(x, axis, [(i, i ^ distance) for i in range(size)])


def halving_scatter(x, axis, size, dim=0):
    index = lax.axis_index(axis)
    x = x.astype(jnp.float32)
    distance = size // 2
    while distance >= 1:
        half = x.shape[dim] // 2
        low = lax.slice_in_dim(x, 0, half, axis=dim)
        high = lax.slice_in_dim(x, half, 2 * half, axis=dim)
        upper = (index & distance) != 0
        keep = jnp.where(upper, high, low)
        send = jnp.where(upper, low, high)
        x = keep + swap_with(send.astype(jnp.bfloat16), axis, distance, size).astype(jnp.float32)
        distance //= 2
    return x


def nearest_first_scatter(parts, axis, size):
    index = lax.axis_index(axis)
    parts = tuple(part.astype(jnp.float32) for part in parts)
    distance = 1
    while distance < size:
        half = parts[0].shape[1] // 2
        upper = (index & distance) != 0
        keeps = tuple(jnp.where(upper, part[:, half:], part[:, :half]) for part in parts)
        sends = tuple(
            jnp.where(upper, part[:, :half], part[:, half:]).astype(jnp.bfloat16) for part in parts
        )
        got = swap_with(sends, axis, distance, size)
        parts = tuple(keep + more.astype(jnp.float32) for keep, more in zip(keeps, got))
        distance *= 2
    return parts


def farthest_first_gather(x, axis, size, dim):
    index = lax.axis_index(axis)
    distance = size // 2
    while distance >= 1:
        got = swap_with(x, axis, distance, size)
        upper = (index & distance) != 0
        x = jnp.where(
            upper, jnp.concatenate([got, x], axis=dim), jnp.concatenate([x, got], axis=dim)
        )
        distance //= 2
    return x


def doubling_gather(x, axis, size, dim):
    index = lax.axis_index(axis)
    distance = 1
    while distance < size:
        got = swap_with(x, axis, distance, size)
        upper = (index & distance) != 0
        x = jnp.where(
            upper, jnp.concatenate([got, x], axis=dim), jnp.concatenate([x, got], axis=dim)
        )
        distance *= 2
    return x


def doubling_sum(x, axis, size):
    distance = 1
    while distance < size:
        x = x + swap_with(x, axis, distance, size)
        distance *= 2
    return x


def nearest_first_rows_scatter(x, axis, size):
    index = lax.axis_index(axis)
    x = x.astype(jnp.float32)
    x = x.reshape((size, x.shape[0] // size) + x.shape[1:])
    distance = 1
    while distance < size:
        pairs = x.reshape((x.shape[0] // 2, 2) + x.shape[1:])
        upper = (index & distance) != 0
        keep = jnp.where(upper, pairs[:, 1], pairs[:, 0])
        send = jnp.where(upper, pairs[:, 0], pairs[:, 1])
        x = keep + swap_with(send.astype(jnp.bfloat16), axis, distance, size).astype(jnp.float32)
        distance *= 2
    return x[0]


def farthest_first_rows_gather(x, axis, size):
    index = lax.axis_index(axis)
    x = x[None]
    distance = size // 2
    while distance >= 1:
        got = swap_with(x, axis, distance, size)
        upper = (index & distance) != 0
        x = jnp.where(upper, jnp.stack([got, x], axis=1), jnp.stack([x, got], axis=1))
        x = x.reshape((-1,) + x.shape[2:])
        distance //= 2
    return x.reshape((-1,) + x.shape[2:])


def matched_sum(x, axis, size):
    x = x.astype(jnp.float32)
    distance = 1
    while distance < size:
        mine = x.astype(jnp.bfloat16)
        x = mine.astype(jnp.float32) + swap_with(mine, axis, distance, size).astype(jnp.float32)
        distance *= 2
    return x


def shards(
    axis_sizes,
    hidden_in,
    queries,
    cache_pool,
    page_table,
    lengths,
    value_up,
    out_proj,
    norm_gain,
    gate_proj,
    up_proj,
    down_proj,
):
    req_dev = queries.shape[0]
    latent = value_up.shape[1]
    value_dim = value_up.shape[2]
    heads_here = value_up.shape[0]
    pages_req = page_table.shape[1]
    score_scale = float(VDIM + ROPE) ** (-0.5)
    units_here = gate_proj.shape[1]
    blocks = axis_sizes["dp"] * axis_sizes["sub"]
    contexts = attend_all(queries, page_table, lengths, cache_pool, latent, score_scale, blocks)
    received = lax.all_to_all(contexts, ("dp", "sub"), split_axis=0, concat_axis=0, tiled=True)
    received = received.reshape(-1, heads_here, latent)
    row_count = received.shape[0]
    values = jnp.einsum("rhc,hcv->rhv", received, value_up, preferred_element_type=jnp.float32)
    values = values.astype(jnp.bfloat16).reshape(row_count, heads_here * value_dim)
    group_values = lax.all_gather(values, "sub", axis=1, tiled=True)
    dp_size = axis_sizes["dp"]
    sub_size = axis_sizes["sub"]
    attention_all = matched_sum(
        jnp.dot(group_values, out_proj, preferred_element_type=jnp.float32), "dp", dp_size
    )
    hidden_all = farthest_first_rows_gather(hidden_in, "dp", dp_size)
    all_residual = hidden_all.astype(jnp.float32) + attention_all
    squares = doubling_sum(jnp.sum(all_residual * all_residual, axis=1), "sub", sub_size)
    gained = (all_residual * norm_gain.astype(jnp.float32)).astype(jnp.bfloat16)
    gate_part = jnp.dot(gained, gate_proj, preferred_element_type=jnp.float32)
    up_part = jnp.dot(gained, up_proj, preferred_element_type=jnp.float32)
    gate_sum, up_sum = nearest_first_scatter((gate_part, up_part), "sub", sub_size)
    scale_rows = lax.rsqrt(squares / float(D) + 1e-06)[:, None]
    hidden_chunk = (jax.nn.silu(gate_sum * scale_rows) * (up_sum * scale_rows)).astype(jnp.bfloat16)
    hidden_units = farthest_first_gather(hidden_chunk, "sub", sub_size, 1)
    feed_forward = nearest_first_rows_scatter(
        jnp.dot(hidden_units, down_proj, preferred_element_type=jnp.float32), "dp", axis_sizes["dp"]
    )
    own_rows = hidden_in.shape[0]
    first_row = lax.axis_index("dp") * own_rows
    attention = lax.dynamic_slice_in_dim(attention_all, first_row, own_rows, 0)
    residual = lax.dynamic_slice_in_dim(all_residual, first_row, own_rows, 0)
    return (attention.astype(jnp.bfloat16), (residual + feed_forward).astype(jnp.bfloat16))


def solution(mesh):
    placed = (
        P(("grp", "dp"), "sub"),
        P(("grp", "dp", "sub"), None, None),
        P(("grp", "dp", "sub"), None, None),
        P(("grp", "dp", "sub"), None),
        P(("grp", "dp", "sub")),
        P(("dp", "sub"), None, None),
        P("dp", "sub"),
        P("sub"),
        P("sub", "dp"),
        P("sub", "dp"),
        P("dp", "sub"),
    )
    return jax.shard_map(
        functools.partial(shards, dict(mesh.shape)),
        mesh=mesh,
        in_specs=placed,
        out_specs=(P(("grp", "dp"), "sub"), P(("grp", "dp"), "sub")),
        check_vma=False,
    )
```

```python
import functools

import jax
import jax.numpy as jnp
from jax import lax
from jax.experimental import pallas as pl
from jax.experimental.pallas import tpu as pltpu
from jax.sharding import PartitionSpec as P

D = 5120
ROPE = 64
VDIM = 128


masked_score = -1e30


def attend_kernel(page_table, lengths, queries, cache_pool, contexts, keys, copy_sems,
                  *, latent, score_scale):
    req_dev, pages_req = page_table.shape
    page_size = cache_pool.shape[2]
    head_count = queries.shape[2]

    def page_copy(slot, page):
        return pltpu.make_async_copy(
            cache_pool.at[page_table[slot, page]],
            keys.at[slot, :, pl.ds(pl.multiple_of(page * page_size, page_size), page_size)],
            copy_sems.at[slot * pages_req + page],
        )

    for slot in range(req_dev):
        def start(page, carry, slot=slot):
            page_copy(slot, page).start()
            return carry

        lax.fori_loop(0, pages_req, start, 0)

    span = pages_req * page_size
    chunk = min(512, span)
    positions = lax.broadcasted_iota(jnp.int32, (head_count, chunk), 1)
    for slot in range(req_dev):
        def finish(page, carry, slot=slot):
            page_copy(slot, page).wait()
            return carry

        lax.fori_loop(0, pages_req, finish, 0)
        length = lengths[slot]
        query_rows = jnp.transpose(queries[slot])
        blocks_of_scores = []
        row_max = jnp.full((head_count, 1), masked_score, jnp.float32)
        for first in range(0, span, chunk):
            block = jnp.dot(
                query_rows, keys[slot, :, first:first + chunk], preferred_element_type=jnp.float32
            ) * score_scale
            block = jnp.where(positions + first < length, block, masked_score)
            blocks_of_scores.append(block)
            row_max = jnp.maximum(row_max, jnp.max(block, axis=1, keepdims=True))
        denominator = jnp.zeros((head_count, 1), jnp.float32)
        weighted = jnp.zeros((head_count, latent), jnp.float32)
        for first, block in zip(range(0, span, chunk), blocks_of_scores):
            exponent = jnp.exp(block - row_max)
            denominator = denominator + jnp.sum(exponent, axis=1, keepdims=True)
            weighted = weighted + lax.dot_general(
                exponent.astype(jnp.bfloat16),
                keys[slot, :latent, first:first + chunk],
                (((1,), (1,)), ((), ())),
                preferred_element_type=jnp.float32,
            )
        blocks, block_heads = contexts.shape[0], head_count // contexts.shape[0]
        context = (weighted / denominator).reshape(blocks, block_heads, latent)
        contexts[:, slot * block_heads:(slot + 1) * block_heads, :] = context.astype(contexts.dtype)


def attend_all(queries, page_table, lengths, cache_pool, latent, score_scale, blocks):
    req_dev, head_count, width = queries.shape
    pages_req = page_table.shape[1]
    query_columns = jnp.swapaxes(queries, 1, 2)
    page_size = cache_pool.shape[1]
    cache_columns = jnp.swapaxes(cache_pool, 1, 2)
    kernel = functools.partial(attend_kernel, latent=latent, score_scale=score_scale)
    return pl.pallas_call(
        kernel,
        out_shape=jax.ShapeDtypeStruct((blocks, req_dev * (head_count // blocks), latent), jnp.bfloat16),
        in_specs=[
            pl.BlockSpec(memory_space=pltpu.SMEM),
            pl.BlockSpec(memory_space=pltpu.SMEM),
            pl.BlockSpec(memory_space=pltpu.VMEM),
            pl.BlockSpec(memory_space=pl.ANY),
        ],
        out_specs=pl.BlockSpec(memory_space=pltpu.VMEM),
        scratch_shapes=[
            pltpu.VMEM((req_dev, width, pages_req * page_size), jnp.bfloat16),
            pltpu.SemaphoreType.DMA((req_dev * pages_req,)),
        ],
        compiler_params=pltpu.CompilerParams(vmem_limit_bytes=48 * 1024 * 1024),
    )(page_table, lengths, query_columns, cache_columns)


def swap_with(x, axis, distance, size):
    return lax.ppermute(x, axis, [(i, i ^ distance) for i in range(size)])


def halving_scatter(x, axis, size, dim=0):
    index = lax.axis_index(axis)
    x = x.astype(jnp.float32)
    distance = size // 2
    while distance >= 1:
        half = x.shape[dim] // 2
        low = lax.slice_in_dim(x, 0, half, axis=dim)
        high = lax.slice_in_dim(x, half, 2 * half, axis=dim)
        upper = (index & distance) != 0
        keep = jnp.where(upper, high, low)
        send = jnp.where(upper, low, high)
        x = keep + swap_with(send.astype(jnp.bfloat16), axis, distance, size).astype(jnp.float32)
        distance //= 2
    return x


def nearest_first_scatter(parts, axis, size):
    index = lax.axis_index(axis)
    parts = tuple(part.astype(jnp.float32) for part in parts)
    distance = 1
    while distance < size:
        half = parts[0].shape[1] // 2
        upper = (index & distance) != 0
        keeps = tuple(jnp.where(upper, part[:, half:], part[:, :half]) for part in parts)
        sends = tuple(
            jnp.where(upper, part[:, :half], part[:, half:]).astype(jnp.bfloat16) for part in parts
        )
        joined = swap_with(jnp.concatenate(sends, axis=1), axis, distance, size)
        got = jnp.split(joined, len(parts), axis=1)
        parts = tuple(keep + more.astype(jnp.float32) for keep, more in zip(keeps, got))
        distance *= 2
    return parts


def farthest_first_gather(x, axis, size, dim):
    index = lax.axis_index(axis)
    distance = size // 2
    while distance >= 1:
        got = swap_with(x, axis, distance, size)
        upper = (index & distance) != 0
        x = jnp.where(
            upper, jnp.concatenate([got, x], axis=dim), jnp.concatenate([x, got], axis=dim)
        )
        distance //= 2
    return x


def doubling_gather(x, axis, size, dim):
    index = lax.axis_index(axis)
    distance = 1
    while distance < size:
        got = swap_with(x, axis, distance, size)
        upper = (index & distance) != 0
        x = jnp.where(
            upper, jnp.concatenate([got, x], axis=dim), jnp.concatenate([x, got], axis=dim)
        )
        distance *= 2
    return x


def doubling_sum(x, axis, size):
    distance = 1
    while distance < size:
        x = x + swap_with(x, axis, distance, size)
        distance *= 2
    return x


def nearest_first_rows_scatter(x, axis, size):
    index = lax.axis_index(axis)
    x = x.astype(jnp.float32)
    x = x.reshape((size, x.shape[0] // size) + x.shape[1:])
    distance = 1
    while distance < size:
        pairs = x.reshape((x.shape[0] // 2, 2) + x.shape[1:])
        upper = (index & distance) != 0
        keep = jnp.where(upper, pairs[:, 1], pairs[:, 0])
        send = jnp.where(upper, pairs[:, 0], pairs[:, 1])
        x = keep + swap_with(send.astype(jnp.bfloat16), axis, distance, size).astype(jnp.float32)
        distance *= 2
    return x[0]


def farthest_first_rows_gather(x, axis, size):
    index = lax.axis_index(axis)
    x = x[None]
    distance = size // 2
    while distance >= 1:
        got = swap_with(x, axis, distance, size)
        upper = (index & distance) != 0
        x = jnp.where(upper, jnp.stack([got, x], axis=1), jnp.stack([x, got], axis=1))
        x = x.reshape((-1,) + x.shape[2:])
        distance //= 2
    return x.reshape((-1,) + x.shape[2:])


def matched_sum(x, axis, size):
    x = x.astype(jnp.float32)
    distance = 1
    while distance < size:
        mine = x.astype(jnp.bfloat16)
        x = mine.astype(jnp.float32) + swap_with(mine, axis, distance, size).astype(jnp.float32)
        distance *= 2
    return x


def shards(
    axis_sizes,
    hidden_in,
    queries,
    cache_pool,
    page_table,
    lengths,
    value_up,
    out_proj,
    norm_gain,
    gate_proj,
    up_proj,
    down_proj,
):
    req_dev = queries.shape[0]
    latent = value_up.shape[1]
    value_dim = value_up.shape[2]
    heads_here = value_up.shape[0]
    pages_req = page_table.shape[1]
    score_scale = float(VDIM + ROPE) ** (-0.5)
    units_here = gate_proj.shape[1]
    blocks = axis_sizes["dp"] * axis_sizes["sub"]
    contexts = attend_all(queries, page_table, lengths, cache_pool, latent, score_scale, blocks)
    received = lax.all_to_all(contexts, ("dp", "sub"), split_axis=0, concat_axis=0, tiled=True)
    received = received.reshape(-1, heads_here, latent)
    row_count = received.shape[0]
    values = jnp.einsum("rhc,hcv->rhv", received, value_up, preferred_element_type=jnp.float32)
    values = values.astype(jnp.bfloat16).reshape(row_count, heads_here * value_dim)
    group_values = lax.all_gather(values, "sub", axis=1, tiled=True)
    dp_size = axis_sizes["dp"]
    sub_size = axis_sizes["sub"]
    attention_all = matched_sum(
        jnp.dot(group_values, out_proj, preferred_element_type=jnp.float32), "dp", dp_size
    )
    hidden_all = farthest_first_rows_gather(hidden_in, "dp", dp_size)
    all_residual = hidden_all.astype(jnp.float32) + attention_all
    squares = doubling_sum(jnp.sum(all_residual * all_residual, axis=1), "sub", sub_size)
    gained = (all_residual * norm_gain.astype(jnp.float32)).astype(jnp.bfloat16)
    gate_part = jnp.dot(gained, gate_proj, preferred_element_type=jnp.float32)
    up_part = jnp.dot(gained, up_proj, preferred_element_type=jnp.float32)
    gate_sum, up_sum = nearest_first_scatter((gate_part, up_part), "sub", sub_size)
    scale_rows = lax.rsqrt(squares / float(D) + 1e-06)[:, None]
    hidden_chunk = (jax.nn.silu(gate_sum * scale_rows) * (up_sum * scale_rows)).astype(jnp.bfloat16)
    hidden_units = farthest_first_gather(hidden_chunk, "sub", sub_size, 1)
    feed_forward = nearest_first_rows_scatter(
        jnp.dot(hidden_units, down_proj, preferred_element_type=jnp.float32), "dp", axis_sizes["dp"]
    )
    own_rows = hidden_in.shape[0]
    first_row = lax.axis_index("dp") * own_rows
    attention = lax.dynamic_slice_in_dim(attention_all, first_row, own_rows, 0)
    residual = lax.dynamic_slice_in_dim(all_residual, first_row, own_rows, 0)
    return (attention.astype(jnp.bfloat16), (residual + feed_forward).astype(jnp.bfloat16))


def solution(mesh):
    placed = (
        P(("grp", "dp"), "sub"),
        P(("grp", "dp", "sub"), None, None),
        P(("grp", "dp", "sub"), None, None),
        P(("grp", "dp", "sub"), None),
        P(("grp", "dp", "sub")),
        P(("dp", "sub"), None, None),
        P("dp", "sub"),
        P("sub"),
        P("sub", "dp"),
        P("sub", "dp"),
        P("dp", "sub"),
    )
    return jax.shard_map(
        functools.partial(shards, dict(mesh.shape)),
        mesh=mesh,
        in_specs=placed,
        out_specs=(P(("grp", "dp"), "sub"), P(("grp", "dp"), "sub")),
        check_vma=False,
    )
```

```python
import functools

import jax
import jax.numpy as jnp
from jax import lax
from jax.experimental import pallas as pl
from jax.experimental.pallas import tpu as pltpu
from jax.sharding import PartitionSpec as P

D = 5120
ROPE = 64
VDIM = 128


masked_score = -1e30


def attend_kernel(page_table, lengths, queries, cache_pool, contexts, keys, copy_sems,
                  *, latent, score_scale):
    req_dev, pages_req = page_table.shape
    page_size = cache_pool.shape[2]
    head_count = queries.shape[2]

    def page_copy(slot, page):
        return pltpu.make_async_copy(
            cache_pool.at[page_table[slot, page]],
            keys.at[slot, :, pl.ds(pl.multiple_of(page * page_size, page_size), page_size)],
            copy_sems.at[slot * pages_req + page],
        )

    for slot in range(req_dev):
        def start(page, carry, slot=slot):
            page_copy(slot, page).start()
            return carry

        lax.fori_loop(0, pages_req, start, 0)

    span = pages_req * page_size
    chunk = min(512, span)
    positions = lax.broadcasted_iota(jnp.int32, (head_count, chunk), 1)

    def score_pass(slot):
        length = lengths[slot]
        query_rows = jnp.transpose(queries[slot])
        blocks_of_scores = []
        row_max = jnp.full((head_count, 1), masked_score, jnp.float32)
        for first in range(0, span, chunk):
            block = jnp.dot(
                query_rows, keys[slot, :, first:first + chunk], preferred_element_type=jnp.float32
            ) * score_scale
            block = jnp.where(positions + first < length, block, masked_score)
            blocks_of_scores.append(block)
            row_max = jnp.maximum(row_max, jnp.max(block, axis=1, keepdims=True))
        return slot, blocks_of_scores, row_max

    def weight_pass(slot, blocks_of_scores, row_max):
        denominator = jnp.zeros((head_count, 1), jnp.float32)
        weighted = jnp.zeros((head_count, latent), jnp.float32)
        for first, block in zip(range(0, span, chunk), blocks_of_scores):
            exponent = jnp.exp(block - row_max)
            denominator = denominator + jnp.sum(exponent, axis=1, keepdims=True)
            weighted = weighted + lax.dot_general(
                exponent.astype(jnp.bfloat16),
                keys[slot, :latent, first:first + chunk],
                (((1,), (1,)), ((), ())),
                preferred_element_type=jnp.float32,
            )
        blocks, block_heads = contexts.shape[0], head_count // contexts.shape[0]
        context = (weighted / denominator).reshape(blocks, block_heads, latent)
        contexts[:, slot * block_heads:(slot + 1) * block_heads, :] = context.astype(contexts.dtype)

    pending = None
    for slot in range(req_dev):
        def finish(page, carry, slot=slot):
            page_copy(slot, page).wait()
            return carry

        lax.fori_loop(0, pages_req, finish, 0)
        scored = score_pass(slot)
        if pending is not None:
            weight_pass(*pending)
        pending = scored
    weight_pass(*pending)


def attend_all(queries, page_table, lengths, cache_pool, latent, score_scale, blocks):
    req_dev, head_count, width = queries.shape
    pages_req = page_table.shape[1]
    query_columns = jnp.swapaxes(queries, 1, 2)
    page_size = cache_pool.shape[1]
    cache_columns = jnp.swapaxes(cache_pool, 1, 2)
    kernel = functools.partial(attend_kernel, latent=latent, score_scale=score_scale)
    return pl.pallas_call(
        kernel,
        out_shape=jax.ShapeDtypeStruct((blocks, req_dev * (head_count // blocks), latent), jnp.bfloat16),
        in_specs=[
            pl.BlockSpec(memory_space=pltpu.SMEM),
            pl.BlockSpec(memory_space=pltpu.SMEM),
            pl.BlockSpec(memory_space=pltpu.VMEM),
            pl.BlockSpec(memory_space=pl.ANY),
        ],
        out_specs=pl.BlockSpec(memory_space=pltpu.VMEM),
        scratch_shapes=[
            pltpu.VMEM((req_dev, width, pages_req * page_size), jnp.bfloat16),
            pltpu.SemaphoreType.DMA((req_dev * pages_req,)),
        ],
        compiler_params=pltpu.CompilerParams(vmem_limit_bytes=48 * 1024 * 1024),
    )(page_table, lengths, query_columns, cache_columns)


def swap_with(x, axis, distance, size):
    return lax.ppermute(x, axis, [(i, i ^ distance) for i in range(size)])


def halving_scatter(x, axis, size, dim=0):
    index = lax.axis_index(axis)
    x = x.astype(jnp.float32)
    distance = size // 2
    while distance >= 1:
        half = x.shape[dim] // 2
        low = lax.slice_in_dim(x, 0, half, axis=dim)
        high = lax.slice_in_dim(x, half, 2 * half, axis=dim)
        upper = (index & distance) != 0
        keep = jnp.where(upper, high, low)
        send = jnp.where(upper, low, high)
        x = keep + swap_with(send.astype(jnp.bfloat16), axis, distance, size).astype(jnp.float32)
        distance //= 2
    return x


def nearest_first_scatter(parts, axis, size):
    index = lax.axis_index(axis)
    parts = tuple(part.astype(jnp.float32) for part in parts)
    distance = 1
    while distance < size:
        half = parts[0].shape[1] // 2
        upper = (index & distance) != 0
        keeps = tuple(jnp.where(upper, part[:, half:], part[:, :half]) for part in parts)
        sends = tuple(
            jnp.where(upper, part[:, :half], part[:, half:]).astype(jnp.bfloat16) for part in parts
        )
        got = swap_with(sends, axis, distance, size)
        parts = tuple(keep + more.astype(jnp.float32) for keep, more in zip(keeps, got))
        distance *= 2
    return parts


def farthest_first_gather(x, axis, size, dim):
    index = lax.axis_index(axis)
    distance = size // 2
    while distance >= 1:
        got = swap_with(x, axis, distance, size)
        upper = (index & distance) != 0
        x = jnp.where(
            upper, jnp.concatenate([got, x], axis=dim), jnp.concatenate([x, got], axis=dim)
        )
        distance //= 2
    return x


def doubling_gather(x, axis, size, dim):
    index = lax.axis_index(axis)
    distance = 1
    while distance < size:
        got = swap_with(x, axis, distance, size)
        upper = (index & distance) != 0
        x = jnp.where(
            upper, jnp.concatenate([got, x], axis=dim), jnp.concatenate([x, got], axis=dim)
        )
        distance *= 2
    return x


def doubling_sum(x, axis, size):
    distance = 1
    while distance < size:
        x = x + swap_with(x, axis, distance, size)
        distance *= 2
    return x


def nearest_first_rows_scatter(x, axis, size):
    index = lax.axis_index(axis)
    x = x.astype(jnp.float32)
    x = x.reshape((size, x.shape[0] // size) + x.shape[1:])
    distance = 1
    while distance < size:
        pairs = x.reshape((x.shape[0] // 2, 2) + x.shape[1:])
        upper = (index & distance) != 0
        keep = jnp.where(upper, pairs[:, 1], pairs[:, 0])
        send = jnp.where(upper, pairs[:, 0], pairs[:, 1])
        x = keep + swap_with(send.astype(jnp.bfloat16), axis, distance, size).astype(jnp.float32)
        distance *= 2
    return x[0]


def farthest_first_rows_gather(x, axis, size):
    index = lax.axis_index(axis)
    x = x[None]
    distance = size // 2
    while distance >= 1:
        got = swap_with(x, axis, distance, size)
        upper = (index & distance) != 0
        x = jnp.where(upper, jnp.stack([got, x], axis=1), jnp.stack([x, got], axis=1))
        x = x.reshape((-1,) + x.shape[2:])
        distance //= 2
    return x.reshape((-1,) + x.shape[2:])


def matched_sum(x, axis, size):
    x = x.astype(jnp.float32)
    distance = 1
    while distance < size:
        mine = x.astype(jnp.bfloat16)
        x = mine.astype(jnp.float32) + swap_with(mine, axis, distance, size).astype(jnp.float32)
        distance *= 2
    return x


def shards(
    axis_sizes,
    hidden_in,
    queries,
    cache_pool,
    page_table,
    lengths,
    value_up,
    out_proj,
    norm_gain,
    gate_proj,
    up_proj,
    down_proj,
):
    req_dev = queries.shape[0]
    latent = value_up.shape[1]
    value_dim = value_up.shape[2]
    heads_here = value_up.shape[0]
    pages_req = page_table.shape[1]
    score_scale = float(VDIM + ROPE) ** (-0.5)
    units_here = gate_proj.shape[1]
    blocks = axis_sizes["dp"] * axis_sizes["sub"]
    contexts = attend_all(queries, page_table, lengths, cache_pool, latent, score_scale, blocks)
    received = lax.all_to_all(contexts, ("dp", "sub"), split_axis=0, concat_axis=0, tiled=True)
    received = received.reshape(-1, heads_here, latent)
    row_count = received.shape[0]
    values = jnp.einsum("rhc,hcv->rhv", received, value_up, preferred_element_type=jnp.float32)
    values = values.astype(jnp.bfloat16).reshape(row_count, heads_here * value_dim)
    group_values = lax.all_gather(values, "sub", axis=1, tiled=True)
    dp_size = axis_sizes["dp"]
    sub_size = axis_sizes["sub"]
    attention_all = matched_sum(
        jnp.dot(group_values, out_proj, preferred_element_type=jnp.float32), "dp", dp_size
    )
    hidden_all = farthest_first_rows_gather(hidden_in, "dp", dp_size)
    all_residual = hidden_all.astype(jnp.float32) + attention_all
    squares = doubling_sum(jnp.sum(all_residual * all_residual, axis=1), "sub", sub_size)
    gained = (all_residual * norm_gain.astype(jnp.float32)).astype(jnp.bfloat16)
    gate_part = jnp.dot(gained, gate_proj, preferred_element_type=jnp.float32)
    up_part = jnp.dot(gained, up_proj, preferred_element_type=jnp.float32)
    gate_sum, up_sum = nearest_first_scatter((gate_part, up_part), "sub", sub_size)
    scale_rows = lax.rsqrt(squares / float(D) + 1e-06)[:, None]
    hidden_chunk = (jax.nn.silu(gate_sum * scale_rows) * (up_sum * scale_rows)).astype(jnp.bfloat16)
    hidden_units = farthest_first_gather(hidden_chunk, "sub", sub_size, 1)
    feed_forward = nearest_first_rows_scatter(
        jnp.dot(hidden_units, down_proj, preferred_element_type=jnp.float32), "dp", axis_sizes["dp"]
    )
    own_rows = hidden_in.shape[0]
    first_row = lax.axis_index("dp") * own_rows
    attention = lax.dynamic_slice_in_dim(attention_all, first_row, own_rows, 0)
    residual = lax.dynamic_slice_in_dim(all_residual, first_row, own_rows, 0)
    return (attention.astype(jnp.bfloat16), (residual + feed_forward).astype(jnp.bfloat16))


def solution(mesh):
    placed = (
        P(("grp", "dp"), "sub"),
        P(("grp", "dp", "sub"), None, None),
        P(("grp", "dp", "sub"), None, None),
        P(("grp", "dp", "sub"), None),
        P(("grp", "dp", "sub")),
        P(("dp", "sub"), None, None),
        P("dp", "sub"),
        P("sub"),
        P("sub", "dp"),
        P("sub", "dp"),
        P("dp", "sub"),
    )
    return jax.shard_map(
        functools.partial(shards, dict(mesh.shape)),
        mesh=mesh,
        in_specs=placed,
        out_specs=(P(("grp", "dp"), "sub"), P(("grp", "dp"), "sub")),
        check_vma=False,
    )
```
